128 devices in a mesh: row: 16 (over z, x), col: 8 (over y, core).
Axes of the slice: x: 4, y: 4, z: 4, core: 2. Of those that a mesh axis runs over, the one named last changes fastest.
Arguments:
- front: bfloat16 [128, 96, 256, 256], P('row', 'col'), may hold values from -1.5 to 1.5
- pattern: int32 [128, 96], replicated, may hold values from 0 to 1
- pivots: int32 [2], replicated, may hold values from 0 to 95, as said below
- pivot_inv: bfloat16 [2, 256, 256], replicated, may hold values from -0.09375 to 0.09375
Outputs:
- factored: bfloat16 [128, 96, 256, 256], P('row', 'col')
The draws below stay inside these ranges and needn't reach their ends.
Inputs may be any that keep to these rules, and one draw needn't show every extreme that they name: The two pivots are distinct front block indices below 96; one of them is 95, the last block column of the window.
All inputs are finite; a program needn't handle non-finite values.
Results may differ from the reference program's by a relative error of at most 0.0051.
Values may be sent and summed in bfloat16 or wider, within the bound.
No kernel may reach another device: no remote copies, remote signals or barrier semaphores. Data moves between devices by JAX's collectives and lax.ppermute only.
A program may use at most 128 MiB of HBM per device.

```python
import jax
import jax.numpy as jnp
from jax import lax

BS = 256
MB_DEV = 8
NB_DEV = 12
NB = 128
NBC = 96
N_ROW = 16
N_COL = 8


def draw_pattern(key, part):
    front_row = jnp.arange(NB, dtype=jnp.int32)
    owner = front_row % N_ROW
    threshold = 30 + 60 * owner // max(N_ROW - 1, 1)
    coins = jax.random.randint(jax.random.fold_in(key, 11), (NB, NBC), 0, 100)
    return (coins < threshold[:, None]).astype(jnp.int32)


def draw_pivots(key, part):
    other = jax.random.randint(jax.random.fold_in(key, 23), (), 0, NBC - 1)
    flip = jax.random.randint(jax.random.fold_in(key, 29), (), 0, 2)
    last = jnp.int32(NBC - 1)
    first = jnp.where(flip > 0, other, last)
    second = jnp.where(flip > 0, last, other)
    return jnp.stack([first, second]).astype(jnp.int32)


def level_of(stream_key, shape, cuts, low, top_value):
    level, own = 1.0, jax.random.fold_in(stream_key, 6)
    for position, blocks in cuts:
        heights = jnp.exp(jax.random.uniform(jax.random.fold_in(own, position), (blocks,), jnp.float32, low / len(cuts), top_value / len(cuts)))
        level = level * jnp.repeat(heights, shape[position] // blocks).reshape([-1 if axis == position else 1 for axis in range(len(shape))])
    return level


def gaussian(own_key, extent, deviation, bound, split=(), kind=jnp.bfloat16):
    values = jax.random.normal(own_key, extent, jnp.float32) * deviation
    if len(split) > 0:
        values = level_of(own_key, extent, split, -0.22, 0.18) * values
    return jnp.clip(values, min=-bound, max=bound).astype(kind)


def setup_inputs(seed: int = 0) -> dict:
    seeds = jax.random.split(jax.random.key(seed), 5)
    front = gaussian(seeds[0], (NB, NBC, BS, BS), 0.25, 1.5, ((0, 16), (1, 8)))
    pattern = draw_pattern(jax.random.fold_in(seeds[4], 71), 0)
    pivots = draw_pivots(jax.random.fold_in(seeds[4], 71), 0)
    pivot_inv = gaussian(seeds[3], (2, BS, BS), (16 * BS) ** -0.5, 0.09375)
    return dict(front=front, pattern=pattern, pivots=pivots, pivot_inv=pivot_inv)


def reference(front, pattern, pivots, pivot_inv):
    nb = front.shape[0]
    nbc = front.shape[1]
    apos = jnp.arange(nb, dtype=jnp.int32)
    bpos = jnp.arange(nbc, dtype=jnp.int32)
    front_rows = (apos % MB_DEV) * N_ROW + apos // MB_DEV
    front_cols = (bpos % NB_DEV) * N_COL + bpos // NB_DEV
    local_pattern = pattern[front_rows][:, front_cols]
    matrix = jnp.where(local_pattern[:, :, None, None] > 0, front, jnp.zeros_like(front))
    rows_ok = jnp.ones((nb,), dtype=bool)
    cols_ok = jnp.ones((nbc,), dtype=bool)
    for step in range(2):
        pivot = pivots[step].astype(jnp.int32)
        row_at = ((pivot % N_ROW) * MB_DEV + pivot // N_ROW).astype(jnp.int32)
        col_at = ((pivot % N_COL) * NB_DEV + pivot // N_COL).astype(jnp.int32)
        rows_ok = rows_ok & (front_rows != pivot)
        cols_ok = cols_ok & (front_cols != pivot)
        column = lax.dynamic_index_in_dim(matrix, col_at, 1, keepdims=False)
        lower = jnp.einsum("iab,bc->iac", column.astype(jnp.float32), pivot_inv[step].astype(jnp.float32))
        lower = jnp.where(rows_ok[:, None, None], lower, 0.0).astype(jnp.bfloat16)
        upper = lax.dynamic_index_in_dim(matrix, row_at, 0, keepdims=False).astype(jnp.float32)
        ok_cols = cols_ok
        is_pivot_col = front_cols == pivot

        def one_row(items):
            block_row, low, ok_row, pat_row = items
            product = jnp.einsum("ab,jbc->jac", low.astype(jnp.float32), upper)
            changed = (block_row.astype(jnp.float32) - product).astype(jnp.bfloat16)
            update = ok_row & ok_cols & (pat_row > 0)
            result = jnp.where(update[:, None, None], changed, block_row)
            place = ok_row & is_pivot_col
            return jnp.where(place[:, None, None], low[None], result)

        matrix = lax.map(one_row, (matrix, lower, rows_ok, local_pattern))
    return matrix
```

```python
import jax
import jax.numpy as jnp
from jax import lax
from jax.sharding import PartitionSpec as P

RING = 4
CORES = 2


def pick(index, options):
    out = options[-1]
    for k in range(len(options) - 2, -1, -1):
        out = jnp.where(index == k, options[k], out)
    return out


def ring_bcast(value, axis, plus, minus, me, root):
    half = value.shape[0] // 2
    first, second = value[:half], value[half:]
    got_plus = lax.ppermute(first, axis, plus)
    got_minus = lax.ppermute(second, axis, minus)
    dist = (me - root) % RING
    at_root = dist == 0
    send_plus = jnp.where(at_root, second, got_plus)
    send_minus = jnp.where(at_root, first, got_minus)
    got_plus2 = lax.ppermute(send_plus, axis, plus)
    got_minus2 = lax.ppermute(send_minus, axis, minus)
    out_first = pick(dist, [first, got_plus, got_plus2, got_minus2])
    out_second = pick(dist, [second, got_plus2, got_minus2, got_minus])
    return jnp.concatenate([out_first, out_second], axis=0)


def row_pairs(step_z, step_x):
    return [
        (RING * z + x, RING * ((z + step_z) % RING) + (x + step_x) % RING)
        for z in range(RING)
        for x in range(RING)
    ]


def row_bcast(value, root):
    me = lax.axis_index("row")
    mz, mx = me // RING, me % RING
    rz, rx = root // RING, root % RING
    xp, xm = row_pairs(0, 1), row_pairs(0, RING - 1)
    zp, zm = row_pairs(1, 0), row_pairs(RING - 1, 0)
    half = value.shape[0] // 2
    along_x = value[:half]
    along_z = value[half:]
    along_x = ring_bcast(along_x, "row", xp, xm, mx, rx)
    along_z = ring_bcast(along_z, "row", zp, zm, mz, rz)
    along_x = ring_bcast(along_x, "row", zp, zm, mz, rz)
    along_z = ring_bcast(along_z, "row", xp, xm, mx, rx)
    return jnp.concatenate([along_x, along_z], axis=0)


def col_bcast(value, root):
    me = lax.axis_index("col")
    my, mk = me // CORES, me % CORES
    ry = root // CORES
    swap = [(CORES * y + k, CORES * y + 1 - k) for y in range(RING) for k in range(CORES)]
    hop = [(CORES * y, CORES * ((y + 1) % RING)) for y in range(RING)] + [
        (CORES * y + 1, CORES * ((y - 1) % RING) + 1) for y in range(RING)
    ]
    got_swap = lax.ppermute(value, "col", swap)
    on_root_chip = jnp.where(me == root, value, got_swap)
    got_hop = lax.ppermute(on_root_chip, "col", hop)
    dist = (my - ry) % RING
    near = jnp.where(dist == 0, on_root_chip, got_hop)
    got_swap2 = lax.ppermute(near, "col", swap)
    half = value.shape[0] // 2
    fwd = jnp.where(mk == 0, near[:half], near[half:])
    got_fwd = lax.ppermute(fwd, "col", hop)
    got_swap3 = lax.ppermute(got_fwd, "col", swap)
    far = jnp.where(
        mk == 0,
        jnp.concatenate([got_fwd, got_swap3], axis=0),
        jnp.concatenate([got_swap3, got_fwd], axis=0),
    )
    own_hop = (dist == 1) & (mk == 0) | (dist == 3) & (mk == 1)
    other_hop = (dist == 1) & (mk == 1) | (dist == 3) & (mk == 0)
    out = jnp.where(own_hop, got_hop, far)
    out = jnp.where(other_hop, got_swap2, out)
    return jnp.where(dist == 0, on_root_chip, out)


def lower_local(column, inverse, rows_ok):
    lower = jnp.einsum("iab,bc->iac", column, inverse, preferred_element_type=jnp.float32)
    return jnp.where(rows_ok[:, None, None], lower, 0.0).astype(jnp.bfloat16)


def eliminate(matrix, lower, upper, pivot, rows_ok, cols_ok, local, front_cols):
    product = jnp.einsum("iab,jbc->ijac", lower, upper, preferred_element_type=jnp.float32)
    update = rows_ok[:, None] & cols_ok[None, :] & (local > 0)
    changed = (matrix.astype(jnp.float32) - product).astype(jnp.bfloat16)
    result = jnp.where(update[:, :, None, None], changed, matrix)
    place = rows_ok[:, None] & (front_cols == pivot)[None, :]
    return jnp.where(place[:, :, None, None], lower[:, None], result)


def body(front, pattern, pivots, pivot_inv):
    rows_dev = front.shape[0]
    cols_dev = front.shape[1]
    nrow = lax.axis_size("row")
    ncol = lax.axis_size("col")
    row_index = lax.axis_index("row")
    col_index = lax.axis_index("col")
    grid = pattern.reshape(rows_dev, nrow, cols_dev, ncol)
    local = lax.dynamic_index_in_dim(grid, row_index, 1, keepdims=False)
    local = lax.dynamic_index_in_dim(local, col_index, 2, keepdims=False)
    front_rows = jnp.arange(rows_dev, dtype=jnp.int32) * nrow + row_index
    front_cols = jnp.arange(cols_dev, dtype=jnp.int32) * ncol + col_index
    matrix = jnp.where(local[:, :, None, None] > 0, front, jnp.zeros_like(front))
    first = pivots[0]
    second = pivots[1]
    rows_first = front_rows != first
    cols_first = front_cols != first
    rows_second = rows_first & (front_rows != second)
    cols_second = cols_first & (front_cols != second)

    column_first = lax.dynamic_index_in_dim(matrix, first // ncol, 1, keepdims=False)
    lower_first = col_bcast(lower_local(column_first, pivot_inv[0], rows_first), first % ncol)
    first_row = lax.dynamic_index_in_dim(matrix, first // nrow, 0, keepdims=False)
    upper_first = row_bcast(first_row, first % nrow)

    a2 = second // nrow
    row_before = lax.dynamic_slice_in_dim(matrix, a2, 1, 0)
    row_after = eliminate(
        row_before,
        lax.dynamic_slice_in_dim(lower_first, a2, 1, 0),
        upper_first,
        first,
        lax.dynamic_slice_in_dim(rows_first, a2, 1, 0),
        cols_first,
        lax.dynamic_slice_in_dim(local, a2, 1, 0),
        front_cols,
    )
    upper_second = row_bcast(row_after[0], second % nrow)
    b2 = second // ncol
    col_before = lax.dynamic_slice_in_dim(matrix, b2, 1, 1)
    col_after = eliminate(
        col_before,
        lower_first,
        lax.dynamic_slice_in_dim(upper_first, b2, 1, 0),
        first,
        rows_first,
        lax.dynamic_slice_in_dim(cols_first, b2, 1, 0),
        lax.dynamic_slice_in_dim(local, b2, 1, 1),
        lax.dynamic_slice_in_dim(front_cols, b2, 1, 0),
    )
    lower_second = col_bcast(lower_local(col_after[:, 0], pivot_inv[1], rows_second), second % ncol)

    matrix = eliminate(
        matrix, lower_first, upper_first, first, rows_first, cols_first, local, front_cols
    )
    matrix = eliminate(
        matrix, lower_second, upper_second, second, rows_second, cols_second, local, front_cols
    )
    return matrix


def solution(mesh):
    placed = (P("row", "col", None, None), P(), P(), P())
    return jax.shard_map(
        body, mesh=mesh, in_specs=placed, out_specs=P("row", "col", None, None), check_vma=False
    )
```

```python
import jax
import jax.numpy as jnp
from jax import lax
from jax.experimental import pallas as pl
from jax.experimental.pallas import tpu as pltpu
from jax.sharding import PartitionSpec as P

RING = 4
CORES = 2


def pick(index, options):
    out = options[-1]
    for k in range(len(options) - 2, -1, -1):
        out = jnp.where(index == k, options[k], out)
    return out


def ring_bcast(value, axis, plus, minus, me, root):
    half = value.shape[0] // 2
    first, second = value[:half], value[half:]
    got_plus = lax.ppermute(first, axis, plus)
    got_minus = lax.ppermute(second, axis, minus)
    dist = (me - root) % RING
    at_root = dist == 0
    send_plus = jnp.where(at_root, second, got_plus)
    send_minus = jnp.where(at_root, first, got_minus)
    got_plus2 = lax.ppermute(send_plus, axis, plus)
    got_minus2 = lax.ppermute(send_minus, axis, minus)
    out_first = pick(dist, [first, got_plus, got_plus2, got_minus2])
    out_second = pick(dist, [second, got_plus2, got_minus2, got_minus])
    return jnp.concatenate([out_first, out_second], axis=0)


def row_pairs(step_z, step_x):
    return [
        (RING * z + x, RING * ((z + step_z) % RING) + (x + step_x) % RING)
        for z in range(RING)
        for x in range(RING)
    ]


def row_bcast(value, root):
    me = lax.axis_index("row")
    mz, mx = me // RING, me % RING
    rz, rx = root // RING, root % RING
    xp, xm = row_pairs(0, 1), row_pairs(0, RING - 1)
    zp, zm = row_pairs(1, 0), row_pairs(RING - 1, 0)
    half = value.shape[0] // 2
    along_x = value[:half]
    along_z = value[half:]
    along_x = ring_bcast(along_x, "row", xp, xm, mx, rx)
    along_z = ring_bcast(along_z, "row", zp, zm, mz, rz)
    along_x = ring_bcast(along_x, "row", zp, zm, mz, rz)
    along_z = ring_bcast(along_z, "row", xp, xm, mx, rx)
    return jnp.concatenate([along_x, along_z], axis=0)


def col_bcast(value, root):
    me = lax.axis_index("col")
    my, mk = me // CORES, me % CORES
    ry = root // CORES
    swap = [(CORES * y + k, CORES * y + 1 - k) for y in range(RING) for k in range(CORES)]
    hop = [(CORES * y, CORES * ((y + 1) % RING)) for y in range(RING)] + [
        (CORES * y + 1, CORES * ((y - 1) % RING) + 1) for y in range(RING)
    ]
    got_swap = lax.ppermute(value, "col", swap)
    on_root_chip = jnp.where(me == root, value, got_swap)
    got_hop = lax.ppermute(on_root_chip, "col", hop)
    dist = (my - ry) % RING
    near = jnp.where(dist == 0, on_root_chip, got_hop)
    got_swap2 = lax.ppermute(near, "col", swap)
    half = value.shape[0] // 2
    fwd = jnp.where(mk == 0, near[:half], near[half:])
    got_fwd = lax.ppermute(fwd, "col", hop)
    got_swap3 = lax.ppermute(got_fwd, "col", swap)
    far = jnp.where(
        mk == 0,
        jnp.concatenate([got_fwd, got_swap3], axis=0),
        jnp.concatenate([got_swap3, got_fwd], axis=0),
    )
    own_hop = (dist == 1) & (mk == 0) | (dist == 3) & (mk == 1)
    other_hop = (dist == 1) & (mk == 1) | (dist == 3) & (mk == 0)
    out = jnp.where(own_hop, got_hop, far)
    out = jnp.where(other_hop, got_swap2, out)
    return jnp.where(dist == 0, on_root_chip, out)


def lower_local(column, inverse, rows_ok):
    lower = jnp.einsum("iab,bc->iac", column, inverse, preferred_element_type=jnp.float32)
    return jnp.where(rows_ok[:, None, None], lower, 0.0).astype(jnp.bfloat16)


def eliminate(matrix, lower, upper, pivot, rows_ok, cols_ok, local, front_cols):
    product = jnp.einsum("iab,jbc->ijac", lower, upper, preferred_element_type=jnp.float32)
    update = rows_ok[:, None] & cols_ok[None, :] & (local > 0)
    changed = (matrix.astype(jnp.float32) - product).astype(jnp.bfloat16)
    result = jnp.where(update[:, :, None, None], changed, matrix)
    place = rows_ok[:, None] & (front_cols == pivot)[None, :]
    return jnp.where(place[:, :, None, None], lower[:, None], result)


def update_kernel(codes, front_ref, l1_ref, l2_ref, u1_ref, u2_ref, out_ref):
    i = pl.program_id(0)
    lower1 = l1_ref[0]
    lower2 = l2_ref[0]
    for j in range(front_ref.shape[1]):
        code = codes[i, j]
        block = front_ref[0, j]
        block = jnp.where((code & 1) != 0, block, jnp.zeros_like(block))
        product = jnp.dot(lower1, u1_ref[j], preferred_element_type=jnp.float32)
        changed = (block.astype(jnp.float32) - product).astype(jnp.bfloat16)
        block = jnp.where((code & 2) != 0, changed, block)
        block = jnp.where((code & 4) != 0, lower1, block)
        product = jnp.dot(lower2, u2_ref[j], preferred_element_type=jnp.float32)
        changed = (block.astype(jnp.float32) - product).astype(jnp.bfloat16)
        block = jnp.where((code & 8) != 0, changed, block)
        block = jnp.where((code & 16) != 0, lower2, block)
        out_ref[0, j] = block


def both_updates(front, codes, lower1, lower2, upper1, upper2):
    rows, cols, bs, _ = front.shape
    row_block = pl.BlockSpec((1, cols, bs, bs), lambda i, c: (i, 0, 0, 0))
    lower_block = pl.BlockSpec((1, bs, bs), lambda i, c: (i, 0, 0))
    upper_block = pl.BlockSpec((cols, bs, bs), lambda i, c: (0, 0, 0))
    return pl.pallas_call(
        update_kernel,
        grid_spec=pltpu.PrefetchScalarGridSpec(
            num_scalar_prefetch=1,
            grid=(rows,),
            in_specs=[row_block, lower_block, lower_block, upper_block, upper_block],
            out_specs=row_block,
        ),
        out_shape=jax.ShapeDtypeStruct(front.shape, front.dtype),
        compiler_params=pltpu.CompilerParams(dimension_semantics=("arbitrary",)),
    )(codes, front, lower1, lower2, upper1, upper2)


def masked(blocks, keep):
    shape = keep.shape + (1,) * (blocks.ndim - keep.ndim)
    return jnp.where(keep.reshape(shape) > 0, blocks, jnp.zeros_like(blocks))


def body(front, pattern, pivots, pivot_inv):
    rows_dev = front.shape[0]
    cols_dev = front.shape[1]
    nrow = lax.axis_size("row")
    ncol = lax.axis_size("col")
    row_index = lax.axis_index("row")
    col_index = lax.axis_index("col")
    grid = pattern.reshape(rows_dev, nrow, cols_dev, ncol)
    local = lax.dynamic_index_in_dim(grid, row_index, 1, keepdims=False)
    local = lax.dynamic_index_in_dim(local, col_index, 2, keepdims=False)
    front_rows = jnp.arange(rows_dev, dtype=jnp.int32) * nrow + row_index
    front_cols = jnp.arange(cols_dev, dtype=jnp.int32) * ncol + col_index
    first = pivots[0]
    second = pivots[1]
    rows_first = front_rows != first
    cols_first = front_cols != first
    rows_second = rows_first & (front_rows != second)
    cols_second = cols_first & (front_cols != second)

    b1 = first // ncol
    column_first = masked(
        lax.dynamic_index_in_dim(front, b1, 1, keepdims=False),
        lax.dynamic_index_in_dim(local, b1, 1, keepdims=False),
    )
    lower_first = col_bcast(lower_local(column_first, pivot_inv[0], rows_first), first % ncol)
    a1 = first // nrow
    first_row = masked(
        lax.dynamic_index_in_dim(front, a1, 0, keepdims=False),
        lax.dynamic_index_in_dim(local, a1, 0, keepdims=False),
    )
    upper_first = row_bcast(first_row, first % nrow)

    a2 = second // nrow
    local_row = lax.dynamic_slice_in_dim(local, a2, 1, 0)
    row_before = masked(lax.dynamic_slice_in_dim(front, a2, 1, 0), local_row)
    row_after = eliminate(
        row_before,
        lax.dynamic_slice_in_dim(lower_first, a2, 1, 0),
        upper_first,
        first,
        lax.dynamic_slice_in_dim(rows_first, a2, 1, 0),
        cols_first,
        local_row,
        front_cols,
    )
    upper_second = row_bcast(row_after[0], second % nrow)
    b2 = second // ncol
    local_col = lax.dynamic_slice_in_dim(local, b2, 1, 1)
    col_before = masked(lax.dynamic_slice_in_dim(front, b2, 1, 1), local_col)
    col_after = eliminate(
        col_before,
        lower_first,
        lax.dynamic_slice_in_dim(upper_first, b2, 1, 0),
        first,
        rows_first,
        lax.dynamic_slice_in_dim(cols_first, b2, 1, 0),
        local_col,
        lax.dynamic_slice_in_dim(front_cols, b2, 1, 0),
    )
    lower_second = col_bcast(lower_local(col_after[:, 0], pivot_inv[1], rows_second), second % ncol)

    keep = local > 0
    update_first = rows_first[:, None] & cols_first[None, :] & keep
    place_first = rows_first[:, None] & (front_cols == first)[None, :]
    update_second = rows_second[:, None] & cols_second[None, :] & keep
    place_second = rows_second[:, None] & (front_cols == second)[None, :]
    codes = (
        keep.astype(jnp.int32)
        + 2 * update_first.astype(jnp.int32)
        + 4 * place_first.astype(jnp.int32)
        + 8 * update_second.astype(jnp.int32)
        + 16 * place_second.astype(jnp.int32)
    )
    return both_updates(front, codes, lower_first, lower_second, upper_first, upper_second)


def solution(mesh):
    placed = (P("row", "col", None, None), P(), P(), P())
    return jax.shard_map(
        body, mesh=mesh, in_specs=placed, out_specs=P("row", "col", None, None), check_vma=False
    )
```

```python
import jax
import jax.numpy as jnp
from jax import lax
from jax.experimental import pallas as pl
from jax.experimental.pallas import tpu as pltpu
from jax.sharding import PartitionSpec as P

RING = 4
CORES = 2


def per_part(cond, a, b):
    return jnp.where(cond.reshape((-1,) + (1,) * (a.ndim - 1)), a, b)


def pick(index, options):
    out = options[-1]
    for k in range(len(options) - 2, -1, -1):
        out = per_part(index == k, options[k], out)
    return out


def ring_bcast(value, axis, plus, minus, me, root):
    half = value.shape[1] // 2
    first, second = value[:, :half], value[:, half:]
    got_plus = lax.ppermute(first, axis, plus)
    got_minus = lax.ppermute(second, axis, minus)
    dist = (me - root) % RING
    at_root = dist == 0
    send_plus = per_part(at_root, second, got_plus)
    send_minus = per_part(at_root, first, got_minus)
    got_plus2 = lax.ppermute(send_plus, axis, plus)
    got_minus2 = lax.ppermute(send_minus, axis, minus)
    out_first = pick(dist, [first, got_plus, got_plus2, got_minus2])
    out_second = pick(dist, [second, got_plus2, got_minus2, got_minus])
    return jnp.concatenate([out_first, out_second], axis=1)


def row_pairs(step_z, step_x):
    return [
        (RING * z + x, RING * ((z + step_z) % RING) + (x + step_x) % RING)
        for z in range(RING)
        for x in range(RING)
    ]


def row_bcast(value, root):
    me = lax.axis_index("row")
    mz, mx = me // RING, me % RING
    rz, rx = root // RING, root % RING
    xp, xm = row_pairs(0, 1), row_pairs(0, RING - 1)
    zp, zm = row_pairs(1, 0), row_pairs(RING - 1, 0)
    half = value.shape[1] // 2
    along_x = value[:, :half]
    along_z = value[:, half:]
    along_x = ring_bcast(along_x, "row", xp, xm, mx, rx)
    along_z = ring_bcast(along_z, "row", zp, zm, mz, rz)
    along_x = ring_bcast(along_x, "row", zp, zm, mz, rz)
    along_z = ring_bcast(along_z, "row", xp, xm, mx, rx)
    return jnp.concatenate([along_x, along_z], axis=1)


def col_bcast(value, root):
    me = lax.axis_index("col")
    my, mk = me // CORES, me % CORES
    ry = root // CORES
    swap = [(CORES * y + k, CORES * y + 1 - k) for y in range(RING) for k in range(CORES)]
    hop = [(CORES * y, CORES * ((y + 1) % RING)) for y in range(RING)] + [
        (CORES * y + 1, CORES * ((y - 1) % RING) + 1) for y in range(RING)
    ]
    got_swap = lax.ppermute(value, "col", swap)
    on_root_chip = per_part(me == root, value, got_swap)
    got_hop = lax.ppermute(on_root_chip, "col", hop)
    dist = (my - ry) % RING
    near = per_part(dist == 0, on_root_chip, got_hop)
    got_swap2 = lax.ppermute(near, "col", swap)
    half = value.shape[1] // 2
    fwd = jnp.where(mk == 0, near[:, :half], near[:, half:])
    got_fwd = lax.ppermute(fwd, "col", hop)
    got_swap3 = lax.ppermute(got_fwd, "col", swap)
    far = jnp.where(
        mk == 0,
        jnp.concatenate([got_fwd, got_swap3], axis=1),
        jnp.concatenate([got_swap3, got_fwd], axis=1),
    )
    own_hop = (dist == 1) & (mk == 0) | (dist == 3) & (mk == 1)
    other_hop = (dist == 1) & (mk == 1) | (dist == 3) & (mk == 0)
    out = per_part(own_hop, got_hop, far)
    out = per_part(other_hop, got_swap2, out)
    return per_part(dist == 0, on_root_chip, out)


def lower_local(column, inverse, rows_ok):
    lower = jnp.einsum("iab,bc->iac", column, inverse, preferred_element_type=jnp.float32)
    return jnp.where(rows_ok[:, None, None], lower, 0.0).astype(jnp.bfloat16)


def eliminate(matrix, lower, upper, pivot, rows_ok, cols_ok, local, front_cols):
    product = jnp.einsum("iab,jbc->ijac", lower, upper, preferred_element_type=jnp.float32)
    update = rows_ok[:, None] & cols_ok[None, :] & (local > 0)
    changed = (matrix.astype(jnp.float32) - product).astype(jnp.bfloat16)
    result = jnp.where(update[:, :, None, None], changed, matrix)
    place = rows_ok[:, None] & (front_cols == pivot)[None, :]
    return jnp.where(place[:, :, None, None], lower[:, None], result)


def update_kernel(codes, front_ref, l1_ref, l2_ref, u1_ref, u2_ref, out_ref):
    i = pl.program_id(0)
    lower1 = l1_ref[0]
    lower2 = l2_ref[0]
    for j in range(front_ref.shape[1]):
        code = codes[i, j]
        block = front_ref[0, j]
        block = jnp.where((code & 1) != 0, block, jnp.zeros_like(block))
        product = jnp.dot(lower1, u1_ref[j], preferred_element_type=jnp.float32)
        changed = (block.astype(jnp.float32) - product).astype(jnp.bfloat16)
        block = jnp.where((code & 2) != 0, changed, block)
        block = jnp.where((code & 4) != 0, lower1, block)
        product = jnp.dot(lower2, u2_ref[j], preferred_element_type=jnp.float32)
        changed = (block.astype(jnp.float32) - product).astype(jnp.bfloat16)
        block = jnp.where((code & 8) != 0, changed, block)
        block = jnp.where((code & 16) != 0, lower2, block)
        out_ref[0, j] = block


def both_updates(front, codes, lower1, lower2, upper1, upper2):
    rows, cols, bs, _ = front.shape
    row_block = pl.BlockSpec((1, cols, bs, bs), lambda i, c: (i, 0, 0, 0))
    lower_block = pl.BlockSpec((1, bs, bs), lambda i, c: (i, 0, 0))
    upper_block = pl.BlockSpec((cols, bs, bs), lambda i, c: (0, 0, 0))
    return pl.pallas_call(
        update_kernel,
        grid_spec=pltpu.PrefetchScalarGridSpec(
            num_scalar_prefetch=1,
            grid=(rows,),
            in_specs=[row_block, lower_block, lower_block, upper_block, upper_block],
            out_specs=row_block,
        ),
        out_shape=jax.ShapeDtypeStruct(front.shape, front.dtype),
        compiler_params=pltpu.CompilerParams(dimension_semantics=("arbitrary",)),
    )(codes, front, lower1, lower2, upper1, upper2)


def masked(blocks, keep):
    shape = keep.shape + (1,) * (blocks.ndim - keep.ndim)
    return jnp.where(keep.reshape(shape) > 0, blocks, jnp.zeros_like(blocks))


def body(front, pattern, pivots, pivot_inv):
    rows_dev = front.shape[0]
    cols_dev = front.shape[1]
    nrow = lax.axis_size("row")
    ncol = lax.axis_size("col")
    row_index = lax.axis_index("row")
    col_index = lax.axis_index("col")
    grid = pattern.reshape(rows_dev, nrow, cols_dev, ncol)
    local = lax.dynamic_index_in_dim(grid, row_index, 1, keepdims=False)
    local = lax.dynamic_index_in_dim(local, col_index, 2, keepdims=False)
    front_rows = jnp.arange(rows_dev, dtype=jnp.int32) * nrow + row_index
    front_cols = jnp.arange(cols_dev, dtype=jnp.int32) * ncol + col_index
    first = pivots[0]
    second = pivots[1]
    rows_first = front_rows != first
    cols_first = front_cols != first
    rows_second = rows_first & (front_rows != second)
    cols_second = cols_first & (front_cols != second)

    a1, b1 = first // nrow, first // ncol
    a2, b2 = second // nrow, second // ncol
    r1, c1 = first % nrow, first % ncol
    r2, c2 = second % nrow, second % ncol

    def local_row(a):
        return masked(
            lax.dynamic_index_in_dim(front, a, 0, keepdims=False),
            lax.dynamic_index_in_dim(local, a, 0, keepdims=False),
        )

    def local_col(b):
        return masked(
            lax.dynamic_index_in_dim(front, b, 1, keepdims=False),
            lax.dynamic_index_in_dim(local, b, 1, keepdims=False),
        )

    lower_first = lower_local(local_col(b1), pivot_inv[0], rows_first)
    cols_sent = col_bcast(jnp.stack([lower_first, local_col(b2)]), jnp.stack([c1, c2]))
    rows_sent = row_bcast(jnp.stack([local_row(a1), local_row(a2)]), jnp.stack([r1, r2]))
    lower_first, second_col = cols_sent[0], cols_sent[1]
    upper_first, second_row = rows_sent[0], rows_sent[1]

    def one_block(a, b, r, c):
        block = masked(front[a, b], local[a, b])
        owner = (row_index == r) & (col_index == c)
        return jnp.where(owner, block, jnp.zeros_like(block))

    cross = lax.psum(
        jnp.stack([one_block(a1, b2, r1, c2), one_block(a2, b1, r2, c1)]), ("row", "col")
    )
    first_at_second, second_at_first = cross[0], cross[1]

    second_ok = (second != first)[None]
    lower_first_at_second = lower_local(second_at_first[None], pivot_inv[0], second_ok)
    row_after = eliminate(
        second_row[None],
        lower_first_at_second,
        upper_first,
        first,
        second_ok,
        cols_first,
        pattern[second][front_cols][None],
        front_cols,
    )
    upper_second = row_after[0]
    col_after = eliminate(
        second_col[:, None],
        lower_first,
        first_at_second[None],
        first,
        rows_first,
        second_ok,
        pattern[front_rows, second][:, None],
        second[None],
    )
    lower_second = lower_local(col_after[:, 0], pivot_inv[1], rows_second)

    keep = local > 0
    update_first = rows_first[:, None] & cols_first[None, :] & keep
    place_first = rows_first[:, None] & (front_cols == first)[None, :]
    update_second = rows_second[:, None] & cols_second[None, :] & keep
    place_second = rows_second[:, None] & (front_cols == second)[None, :]
    codes = (
        keep.astype(jnp.int32)
        + 2 * update_first.astype(jnp.int32)
        + 4 * place_first.astype(jnp.int32)
        + 8 * update_second.astype(jnp.int32)
        + 16 * place_second.astype(jnp.int32)
    )
    return both_updates(front, codes, lower_first, lower_second, upper_first, upper_second)


def solution(mesh):
    placed = (P("row", "col", None, None), P(), P(), P())
    return jax.shard_map(
        body, mesh=mesh, in_specs=placed, out_specs=P("row", "col", None, None), check_vma=False
    )
```

```python
import jax
import jax.numpy as jnp
from jax import lax
from jax.experimental import pallas as pl
from jax.experimental.pallas import tpu as pltpu
from jax.sharding import PartitionSpec as P

RING = 4
CORES = 2


def pick(index, options):
    out = options[-1]
    for k in range(len(options) - 2, -1, -1):
        out = jnp.where(index == k, options[k], out)
    return out


def ring_bcast(value, axis, plus, minus, me, root):
    half = value.shape[0] // 2
    first, second = value[:half], value[half:]
    got_plus = lax.ppermute(first, axis, plus)
    got_minus = lax.ppermute(second, axis, minus)
    dist = (me - root) % RING
    at_root = dist == 0
    send_plus = jnp.where(at_root, second, got_plus)
    send_minus = jnp.where(at_root, first, got_minus)
    got_plus2 = lax.ppermute(send_plus, axis, plus)
    got_minus2 = lax.ppermute(send_minus, axis, minus)
    out_first = pick(dist, [first, got_plus, got_plus2, got_minus2])
    out_second = pick(dist, [second, got_plus2, got_minus2, got_minus])
    return jnp.concatenate([out_first, out_second], axis=0)


def row_pairs(step_z, step_x):
    return [
        (RING * z + x, RING * ((z + step_z) % RING) + (x + step_x) % RING)
        for z in range(RING)
        for x in range(RING)
    ]


def row_bcast(value, root):
    me = lax.axis_index("row")
    mz, mx = me // RING, me % RING
    rz, rx = root // RING, root % RING
    xp, xm = row_pairs(0, 1), row_pairs(0, RING - 1)
    zp, zm = row_pairs(1, 0), row_pairs(RING - 1, 0)
    half = value.shape[0] // 2
    along_x = value[:half]
    along_z = value[half:]
    along_x = ring_bcast(along_x, "row", xp, xm, mx, rx)
    along_z = ring_bcast(along_z, "row", zp, zm, mz, rz)
    along_x = ring_bcast(along_x, "row", zp, zm, mz, rz)
    along_z = ring_bcast(along_z, "row", xp, xm, mx, rx)
    return jnp.concatenate([along_x, along_z], axis=0)


def col_bcast(value, root):
    me = lax.axis_index("col")
    my, mk = me // CORES, me % CORES
    ry = root // CORES
    swap = [(CORES * y + k, CORES * y + 1 - k) for y in range(RING) for k in range(CORES)]
    hop = [(CORES * y, CORES * ((y + 1) % RING)) for y in range(RING)] + [
        (CORES * y + 1, CORES * ((y - 1) % RING) + 1) for y in range(RING)
    ]
    got_swap = lax.ppermute(value, "col", swap)
    on_root_chip = jnp.where(me == root, value, got_swap)
    got_hop = lax.ppermute(on_root_chip, "col", hop)
    dist = (my - ry) % RING
    near = jnp.where(dist == 0, on_root_chip, got_hop)
    got_swap2 = lax.ppermute(near, "col", swap)
    half = value.shape[0] // 2
    fwd = jnp.where(mk == 0, near[:half], near[half:])
    got_fwd = lax.ppermute(fwd, "col", hop)
    got_swap3 = lax.ppermute(got_fwd, "col", swap)
    far = jnp.where(
        mk == 0,
        jnp.concatenate([got_fwd, got_swap3], axis=0),
        jnp.concatenate([got_swap3, got_fwd], axis=0),
    )
    own_hop = (dist == 1) & (mk == 0) | (dist == 3) & (mk == 1)
    other_hop = (dist == 1) & (mk == 1) | (dist == 3) & (mk == 0)
    out = jnp.where(own_hop, got_hop, far)
    out = jnp.where(other_hop, got_swap2, out)
    return jnp.where(dist == 0, on_root_chip, out)


def from_root(value, axis, source):
    kept = jnp.where(lax.axis_index(axis) == source, value, 0).astype(value.dtype)
    return lax.psum(kept, axis)


def lower_local(column, inverse, rows_ok):
    lower = jnp.einsum("iab,bc->iac", column, inverse, preferred_element_type=jnp.float32)
    return jnp.where(rows_ok[:, None, None], lower, 0.0).astype(jnp.bfloat16)


def eliminate(matrix, lower, upper, pivot, rows_ok, cols_ok, local, front_cols):
    product = jnp.einsum("iab,jbc->ijac", lower, upper, preferred_element_type=jnp.float32)
    update = rows_ok[:, None] & cols_ok[None, :] & (local > 0)
    changed = (matrix.astype(jnp.float32) - product).astype(jnp.bfloat16)
    result = jnp.where(update[:, :, None, None], changed, matrix)
    place = rows_ok[:, None] & (front_cols == pivot)[None, :]
    return jnp.where(place[:, :, None, None], lower[:, None], result)


def update_kernel(codes, front_ref, l1_ref, l2_ref, u1_ref, u2_ref, out_ref):
    i = pl.program_id(0)
    lower1 = l1_ref[0]
    lower2 = l2_ref[0]
    for j in range(front_ref.shape[1]):
        code = codes[i, j]
        block = front_ref[0, j]
        block = jnp.where((code & 1) != 0, block, jnp.zeros_like(block))
        product = jnp.dot(lower1, u1_ref[j], preferred_element_type=jnp.float32)
        changed = (block.astype(jnp.float32) - product).astype(jnp.bfloat16)
        block = jnp.where((code & 2) != 0, changed, block)
        block = jnp.where((code & 4) != 0, lower1, block)
        product = jnp.dot(lower2, u2_ref[j], preferred_element_type=jnp.float32)
        changed = (block.astype(jnp.float32) - product).astype(jnp.bfloat16)
        block = jnp.where((code & 8) != 0, changed, block)
        block = jnp.where((code & 16) != 0, lower2, block)
        out_ref[0, j] = block


def both_updates(front, codes, lower1, lower2, upper1, upper2):
    rows, cols, bs, _ = front.shape
    row_block = pl.BlockSpec((1, cols, bs, bs), lambda i, c: (i, 0, 0, 0))
    lower_block = pl.BlockSpec((1, bs, bs), lambda i, c: (i, 0, 0))
    upper_block = pl.BlockSpec((cols, bs, bs), lambda i, c: (0, 0, 0))
    return pl.pallas_call(
        update_kernel,
        grid_spec=pltpu.PrefetchScalarGridSpec(
            num_scalar_prefetch=1,
            grid=(rows,),
            in_specs=[row_block, lower_block, lower_block, upper_block, upper_block],
            out_specs=row_block,
        ),
        out_shape=jax.ShapeDtypeStruct(front.shape, front.dtype),
        compiler_params=pltpu.CompilerParams(dimension_semantics=("arbitrary",)),
    )(codes, front, lower1, lower2, upper1, upper2)


def masked(blocks, keep):
    shape = keep.shape + (1,) * (blocks.ndim - keep.ndim)
    return jnp.where(keep.reshape(shape) > 0, blocks, jnp.zeros_like(blocks))


def body(front, pattern, pivots, pivot_inv):
    rows_dev = front.shape[0]
    cols_dev = front.shape[1]
    nrow = lax.axis_size("row")
    ncol = lax.axis_size("col")
    row_index = lax.axis_index("row")
    col_index = lax.axis_index("col")
    grid = pattern.reshape(rows_dev, nrow, cols_dev, ncol)
    local = lax.dynamic_index_in_dim(grid, row_index, 1, keepdims=False)
    local = lax.dynamic_index_in_dim(local, col_index, 2, keepdims=False)
    front_rows = jnp.arange(rows_dev, dtype=jnp.int32) * nrow + row_index
    front_cols = jnp.arange(cols_dev, dtype=jnp.int32) * ncol + col_index
    first = pivots[0]
    second = pivots[1]
    rows_first = front_rows != first
    cols_first = front_cols != first
    rows_second = rows_first & (front_rows != second)
    cols_second = cols_first & (front_cols != second)

    b1 = first // ncol
    column_first = masked(
        lax.dynamic_index_in_dim(front, b1, 1, keepdims=False),
        lax.dynamic_index_in_dim(local, b1, 1, keepdims=False),
    )
    lower_first = from_root(lower_local(column_first, pivot_inv[0], rows_first), "col", first % ncol)
    a1 = first // nrow
    first_row = masked(
        lax.dynamic_index_in_dim(front, a1, 0, keepdims=False),
        lax.dynamic_index_in_dim(local, a1, 0, keepdims=False),
    )
    upper_first = row_bcast(first_row, first % nrow)

    a2 = second // nrow
    local_row = lax.dynamic_slice_in_dim(local, a2, 1, 0)
    row_before = masked(lax.dynamic_slice_in_dim(front, a2, 1, 0), local_row)
    row_after = eliminate(
        row_before,
        lax.dynamic_slice_in_dim(lower_first, a2, 1, 0),
        upper_first,
        first,
        lax.dynamic_slice_in_dim(rows_first, a2, 1, 0),
        cols_first,
        local_row,
        front_cols,
    )
    upper_second = row_bcast(row_after[0], second % nrow)
    b2 = second // ncol
    local_col = lax.dynamic_slice_in_dim(local, b2, 1, 1)
    col_before = masked(lax.dynamic_slice_in_dim(front, b2, 1, 1), local_col)
    col_after = eliminate(
        col_before,
        lower_first,
        lax.dynamic_slice_in_dim(upper_first, b2, 1, 0),
        first,
        rows_first,
        lax.dynamic_slice_in_dim(cols_first, b2, 1, 0),
        local_col,
        lax.dynamic_slice_in_dim(front_cols, b2, 1, 0),
    )
    lower_second = from_root(
        lower_local(col_after[:, 0], pivot_inv[1], rows_second), "col", second % ncol
    )

    keep = local > 0
    update_first = rows_first[:, None] & cols_first[None, :] & keep
    place_first = rows_first[:, None] & (front_cols == first)[None, :]
    update_second = rows_second[:, None] & cols_second[None, :] & keep
    place_second = rows_second[:, None] & (front_cols == second)[None, :]
    codes = (
        keep.astype(jnp.int32)
        + 2 * update_first.astype(jnp.int32)
        + 4 * place_first.astype(jnp.int32)
        + 8 * update_second.astype(jnp.int32)
        + 16 * place_second.astype(jnp.int32)
    )
    return both_updates(front, codes, lower_first, lower_second, upper_first, upper_second)


def solution(mesh):
    placed = (P("row", "col", None, None), P(), P(), P())
    return jax.shard_map(
        body, mesh=mesh, in_specs=placed, out_specs=P("row", "col", None, None), check_vma=False
    )
```

```python
import jax
import jax.numpy as jnp
from jax import lax
from jax.experimental import pallas as pl
from jax.experimental.pallas import tpu as pltpu
from jax.sharding import PartitionSpec as P

RING = 4
CORES = 2


def pick(index, options):
    out = options[-1]
    for k in range(len(options) - 2, -1, -1):
        out = jnp.where(index == k, options[k], out)
    return out


def ring_bcast(value, axis, plus, minus, me, root):
    half = value.shape[0] // 2
    first, second = value[:half], value[half:]
    got_plus = lax.ppermute(first, axis, plus)
    got_minus = lax.ppermute(second, axis, minus)
    dist = (me - root) % RING
    at_root = dist == 0
    send_plus = jnp.where(at_root, second, got_plus)
    send_minus = jnp.where(at_root, first, got_minus)
    got_plus2 = lax.ppermute(send_plus, axis, plus)
    got_minus2 = lax.ppermute(send_minus, axis, minus)
    out_first = pick(dist, [first, got_plus, got_plus2, got_minus2])
    out_second = pick(dist, [second, got_plus2, got_minus2, got_minus])
    return jnp.concatenate([out_first, out_second], axis=0)


def row_pairs(step_z, step_x):
    return [
        (RING * z + x, RING * ((z + step_z) % RING) + (x + step_x) % RING)
        for z in range(RING)
        for x in range(RING)
    ]


def row_bcast(value, root):
    me = lax.axis_index("row")
    mz, mx = me // RING, me % RING
    rz, rx = root // RING, root % RING
    xp, xm = row_pairs(0, 1), row_pairs(0, RING - 1)
    zp, zm = row_pairs(1, 0), row_pairs(RING - 1, 0)
    half = value.shape[0] // 2
    along_x = value[:half]
    along_z = value[half:]
    along_x = ring_bcast(along_x, "row", xp, xm, mx, rx)
    along_z = ring_bcast(along_z, "row", zp, zm, mz, rz)
    along_x = ring_bcast(along_x, "row", zp, zm, mz, rz)
    along_z = ring_bcast(along_z, "row", xp, xm, mx, rx)
    return jnp.concatenate([along_x, along_z], axis=0)


def col_bcast(value, root):
    me = lax.axis_index("col")
    my, mk = me // CORES, me % CORES
    ry = root // CORES
    swap = [(CORES * y + k, CORES * y + 1 - k) for y in range(RING) for k in range(CORES)]
    hop = [(CORES * y, CORES * ((y + 1) % RING)) for y in range(RING)] + [
        (CORES * y + 1, CORES * ((y - 1) % RING) + 1) for y in range(RING)
    ]
    got_swap = lax.ppermute(value, "col", swap)
    on_root_chip = jnp.where(me == root, value, got_swap)
    got_hop = lax.ppermute(on_root_chip, "col", hop)
    dist = (my - ry) % RING
    near = jnp.where(dist == 0, on_root_chip, got_hop)
    got_swap2 = lax.ppermute(near, "col", swap)
    half = value.shape[0] // 2
    fwd = jnp.where(mk == 0, near[:half], near[half:])
    got_fwd = lax.ppermute(fwd, "col", hop)
    got_swap3 = lax.ppermute(got_fwd, "col", swap)
    far = jnp.where(
        mk == 0,
        jnp.concatenate([got_fwd, got_swap3], axis=0),
        jnp.concatenate([got_swap3, got_fwd], axis=0),
    )
    own_hop = (dist == 1) & (mk == 0) | (dist == 3) & (mk == 1)
    other_hop = (dist == 1) & (mk == 1) | (dist == 3) & (mk == 0)
    out = jnp.where(own_hop, got_hop, far)
    out = jnp.where(other_hop, got_swap2, out)
    return jnp.where(dist == 0, on_root_chip, out)


ROW_ORDERS = ((3, 2, 1, 0), (1, 0, 3, 2))
COL_ORDER = (0, 1, 2)


def xor_pairs(nrow, ncol, on_row, step):
    pairs = []
    for r in range(nrow):
        for c in range(ncol):
            if on_row:
                pairs.append((r * ncol + c, (r ^ (1 << ROW_ORDERS[c % CORES][step])) * ncol + c))
            else:
                pairs.append((r * ncol + c, r * ncol + (c ^ (1 << COL_ORDER[step]))))
    return pairs


def xor_bcast(value, root, on_row):
    nrow = lax.axis_size("row")
    ncol = lax.axis_size("col")
    me = lax.axis_index("row") if on_row else lax.axis_index("col")
    parity = lax.axis_index("col") % CORES
    steps = (nrow if on_row else ncol).bit_length() - 1
    relative = me ^ root

    def bit(step):
        if on_row:
            b = jnp.where(parity == 0, ROW_ORDERS[0][step], ROW_ORDERS[1][step])
        else:
            b = COL_ORDER[step]
        return (relative >> b) & 1

    shape = value.shape
    pieces = 1 << steps
    buf = value.reshape(pieces, -1, shape[-1])
    axes = ("row", "col")
    for step in range(steps):
        half = buf.shape[0] // 2
        got = lax.ppermute(buf[half:], axes, xor_pairs(nrow, ncol, on_row, step))
        buf = jnp.where(bit(step) == 1, got, buf[:half])
    for step in reversed(range(steps)):
        got = lax.ppermute(buf, axes, xor_pairs(nrow, ncol, on_row, step))
        low = bit(step) == 0
        buf = jnp.where(low, jnp.concatenate([buf, got]), jnp.concatenate([got, buf]))
    return buf.reshape(shape)


def lower_local(column, inverse, rows_ok):
    lower = jnp.einsum("iab,bc->iac", column, inverse, preferred_element_type=jnp.float32)
    return jnp.where(rows_ok[:, None, None], lower, 0.0).astype(jnp.bfloat16)


def eliminate(matrix, lower, upper, pivot, rows_ok, cols_ok, local, front_cols):
    product = jnp.einsum("iab,jbc->ijac", lower, upper, preferred_element_type=jnp.float32)
    update = rows_ok[:, None] & cols_ok[None, :] & (local > 0)
    changed = (matrix.astype(jnp.float32) - product).astype(jnp.bfloat16)
    result = jnp.where(update[:, :, None, None], changed, matrix)
    place = rows_ok[:, None] & (front_cols == pivot)[None, :]
    return jnp.where(place[:, :, None, None], lower[:, None], result)


def update_kernel(codes, front_ref, l1_ref, l2_ref, u1_ref, u2_ref, out_ref):
    i = pl.program_id(0)
    lower1 = l1_ref[0]
    lower2 = l2_ref[0]
    for j in range(front_ref.shape[1]):
        code = codes[i, j]
        block = front_ref[0, j]
        block = jnp.where((code & 1) != 0, block, jnp.zeros_like(block))
        product = jnp.dot(lower1, u1_ref[j], preferred_element_type=jnp.float32)
        changed = (block.astype(jnp.float32) - product).astype(jnp.bfloat16)
        block = jnp.where((code & 2) != 0, changed, block)
        block = jnp.where((code & 4) != 0, lower1, block)
        product = jnp.dot(lower2, u2_ref[j], preferred_element_type=jnp.float32)
        changed = (block.astype(jnp.float32) - product).astype(jnp.bfloat16)
        block = jnp.where((code & 8) != 0, changed, block)
        block = jnp.where((code & 16) != 0, lower2, block)
        out_ref[0, j] = block


def both_updates(front, codes, lower1, lower2, upper1, upper2):
    rows, cols, bs, _ = front.shape
    row_block = pl.BlockSpec((1, cols, bs, bs), lambda i, c: (i, 0, 0, 0))
    lower_block = pl.BlockSpec((1, bs, bs), lambda i, c: (i, 0, 0))
    upper_block = pl.BlockSpec((cols, bs, bs), lambda i, c: (0, 0, 0))
    return pl.pallas_call(
        update_kernel,
        grid_spec=pltpu.PrefetchScalarGridSpec(
            num_scalar_prefetch=1,
            grid=(rows,),
            in_specs=[row_block, lower_block, lower_block, upper_block, upper_block],
            out_specs=row_block,
        ),
        out_shape=jax.ShapeDtypeStruct(front.shape, front.dtype),
        compiler_params=pltpu.CompilerParams(dimension_semantics=("arbitrary",)),
    )(codes, front, lower1, lower2, upper1, upper2)


def masked(blocks, keep):
    shape = keep.shape + (1,) * (blocks.ndim - keep.ndim)
    return jnp.where(keep.reshape(shape) > 0, blocks, jnp.zeros_like(blocks))


def body(front, pattern, pivots, pivot_inv):
    rows_dev = front.shape[0]
    cols_dev = front.shape[1]
    nrow = lax.axis_size("row")
    ncol = lax.axis_size("col")
    row_index = lax.axis_index("row")
    col_index = lax.axis_index("col")
    grid = pattern.reshape(rows_dev, nrow, cols_dev, ncol)
    local = lax.dynamic_index_in_dim(grid, row_index, 1, keepdims=False)
    local = lax.dynamic_index_in_dim(local, col_index, 2, keepdims=False)
    front_rows = jnp.arange(rows_dev, dtype=jnp.int32) * nrow + row_index
    front_cols = jnp.arange(cols_dev, dtype=jnp.int32) * ncol + col_index
    first = pivots[0]
    second = pivots[1]
    rows_first = front_rows != first
    cols_first = front_cols != first
    rows_second = rows_first & (front_rows != second)
    cols_second = cols_first & (front_cols != second)

    b1 = first // ncol
    column_first = masked(
        lax.dynamic_index_in_dim(front, b1, 1, keepdims=False),
        lax.dynamic_index_in_dim(local, b1, 1, keepdims=False),
    )
    lower_first = xor_bcast(lower_local(column_first, pivot_inv[0], rows_first), first % ncol, False)
    a1 = first // nrow
    first_row = masked(
        lax.dynamic_index_in_dim(front, a1, 0, keepdims=False),
        lax.dynamic_index_in_dim(local, a1, 0, keepdims=False),
    )
    upper_first = xor_bcast(first_row, first % nrow, True)

    a2 = second // nrow
    local_row = lax.dynamic_slice_in_dim(local, a2, 1, 0)
    row_before = masked(lax.dynamic_slice_in_dim(front, a2, 1, 0), local_row)
    row_after = eliminate(
        row_before,
        lax.dynamic_slice_in_dim(lower_first, a2, 1, 0),
        upper_first,
        first,
        lax.dynamic_slice_in_dim(rows_first, a2, 1, 0),
        cols_first,
        local_row,
        front_cols,
    )
    upper_second = xor_bcast(row_after[0], second % nrow, True)
    b2 = second // ncol
    local_col = lax.dynamic_slice_in_dim(local, b2, 1, 1)
    col_before = masked(lax.dynamic_slice_in_dim(front, b2, 1, 1), local_col)
    col_after = eliminate(
        col_before,
        lower_first,
        lax.dynamic_slice_in_dim(upper_first, b2, 1, 0),
        first,
        rows_first,
        lax.dynamic_slice_in_dim(cols_first, b2, 1, 0),
        local_col,
        lax.dynamic_slice_in_dim(front_cols, b2, 1, 0),
    )
    lower_second = xor_bcast(
        lower_local(col_after[:, 0], pivot_inv[1], rows_second), second % ncol, False
    )

    keep = local > 0
    update_first = rows_first[:, None] & cols_first[None, :] & keep
    place_first = rows_first[:, None] & (front_cols == first)[None, :]
    update_second = rows_second[:, None] & cols_second[None, :] & keep
    place_second = rows_second[:, None] & (front_cols == second)[None, :]
    codes = (
        keep.astype(jnp.int32)
        + 2 * update_first.astype(jnp.int32)
        + 4 * place_first.astype(jnp.int32)
        + 8 * update_second.astype(jnp.int32)
        + 16 * place_second.astype(jnp.int32)
    )
    return both_updates(front, codes, lower_first, lower_second, upper_first, upper_second)


def solution(mesh):
    placed = (P("row", "col", None, None), P(), P(), P())
    return jax.shard_map(
        body, mesh=mesh, in_specs=placed, out_specs=P("row", "col", None, None), check_vma=False
    )
```

```python
import jax
import jax.numpy as jnp
from jax import lax
from jax.experimental import pallas as pl
from jax.experimental.pallas import tpu as pltpu
from jax.sharding import PartitionSpec as P

RING = 4
CORES = 2


def per_part(cond, a, b):
    return jnp.where(cond.reshape((-1,) + (1,) * (a.ndim - 1)), a, b)


def pick(index, options):
    out = options[-1]
    for k in range(len(options) - 2, -1, -1):
        out = jnp.where(index == k, options[k], out)
    return out


def ring_bcast(value, axis, plus, minus, me, root):
    half = value.shape[0] // 2
    first, second = value[:half], value[half:]
    got_plus = lax.ppermute(first, axis, plus)
    got_minus = lax.ppermute(second, axis, minus)
    dist = (me - root) % RING
    at_root = dist == 0
    send_plus = jnp.where(at_root, second, got_plus)
    send_minus = jnp.where(at_root, first, got_minus)
    got_plus2 = lax.ppermute(send_plus, axis, plus)
    got_minus2 = lax.ppermute(send_minus, axis, minus)
    out_first = pick(dist, [first, got_plus, got_plus2, got_minus2])
    out_second = pick(dist, [second, got_plus2, got_minus2, got_minus])
    return jnp.concatenate([out_first, out_second], axis=0)


def row_pairs(step_z, step_x):
    return [
        (RING * z + x, RING * ((z + step_z) % RING) + (x + step_x) % RING)
        for z in range(RING)
        for x in range(RING)
    ]


def row_bcast(value, root):
    me = lax.axis_index("row")
    mz, mx = me // RING, me % RING
    rz, rx = root // RING, root % RING
    xp, xm = row_pairs(0, 1), row_pairs(0, RING - 1)
    zp, zm = row_pairs(1, 0), row_pairs(RING - 1, 0)
    half = value.shape[0] // 2
    along_x = value[:half]
    along_z = value[half:]
    along_x = ring_bcast(along_x, "row", xp, xm, mx, rx)
    along_z = ring_bcast(along_z, "row", zp, zm, mz, rz)
    along_x = ring_bcast(along_x, "row", zp, zm, mz, rz)
    along_z = ring_bcast(along_z, "row", xp, xm, mx, rx)
    return jnp.concatenate([along_x, along_z], axis=0)


def col_bcast(value, root):
    me = lax.axis_index("col")
    my, mk = me // CORES, me % CORES
    ry = root // CORES
    swap = [(CORES * y + k, CORES * y + 1 - k) for y in range(RING) for k in range(CORES)]
    hop = [(CORES * y, CORES * ((y + 1) % RING)) for y in range(RING)] + [
        (CORES * y + 1, CORES * ((y - 1) % RING) + 1) for y in range(RING)
    ]
    got_swap = lax.ppermute(value, "col", swap)
    on_root_chip = jnp.where(me == root, value, got_swap)
    got_hop = lax.ppermute(on_root_chip, "col", hop)
    dist = (my - ry) % RING
    near = jnp.where(dist == 0, on_root_chip, got_hop)
    got_swap2 = lax.ppermute(near, "col", swap)
    half = value.shape[0] // 2
    fwd = jnp.where(mk == 0, near[:half], near[half:])
    got_fwd = lax.ppermute(fwd, "col", hop)
    got_swap3 = lax.ppermute(got_fwd, "col", swap)
    far = jnp.where(
        mk == 0,
        jnp.concatenate([got_fwd, got_swap3], axis=0),
        jnp.concatenate([got_swap3, got_fwd], axis=0),
    )
    own_hop = (dist == 1) & (mk == 0) | (dist == 3) & (mk == 1)
    other_hop = (dist == 1) & (mk == 1) | (dist == 3) & (mk == 0)
    out = jnp.where(own_hop, got_hop, far)
    out = jnp.where(other_hop, got_swap2, out)
    return jnp.where(dist == 0, on_root_chip, out)


ROW_ORDERS = ((3, 2, 1, 0), (1, 0, 3, 2))
COL_ORDER = (0, 1, 2)


def xor_pairs(nrow, ncol, on_row, step):
    pairs = []
    for r in range(nrow):
        for c in range(ncol):
            if on_row:
                pairs.append((r * ncol + c, (r ^ (1 << ROW_ORDERS[c % CORES][step])) * ncol + c))
            else:
                pairs.append((r * ncol + c, r * ncol + (c ^ (1 << COL_ORDER[step]))))
    return pairs


def xor_bcast(value, root, on_row):
    nrow = lax.axis_size("row")
    ncol = lax.axis_size("col")
    me = lax.axis_index("row") if on_row else lax.axis_index("col")
    parity = lax.axis_index("col") % CORES
    steps = (nrow if on_row else ncol).bit_length() - 1
    relative = me ^ root

    def bit(step):
        if on_row:
            b = jnp.where(parity == 0, ROW_ORDERS[0][step], ROW_ORDERS[1][step])
        else:
            b = COL_ORDER[step]
        return (relative >> b) & 1

    shape = value.shape
    pieces = 1 << steps
    buf = value.reshape(shape[0], pieces, -1, shape[-1])
    axes = ("row", "col")
    for step in range(steps):
        half = buf.shape[1] // 2
        got = lax.ppermute(buf[:, half:], axes, xor_pairs(nrow, ncol, on_row, step))
        buf = per_part(bit(step) == 1, got, buf[:, :half])
    for step in reversed(range(steps)):
        got = lax.ppermute(buf, axes, xor_pairs(nrow, ncol, on_row, step))
        low = bit(step) == 0
        buf = per_part(low, jnp.concatenate([buf, got], 1), jnp.concatenate([got, buf], 1))
    return buf.reshape(shape)


def all_bcast(value, root):
    nrow = lax.axis_size("row")
    ncol = lax.axis_size("col")
    n = nrow * ncol
    relative = (lax.axis_index("row") * ncol + lax.axis_index("col")) ^ root
    for b in range(n.bit_length() - 1):
        got = lax.ppermute(value, ("row", "col"), [(d, d ^ (1 << b)) for d in range(n)])
        value = per_part((relative >> b) == 1, got, value)
    return value


def lower_local(column, inverse, rows_ok):
    lower = jnp.einsum("iab,bc->iac", column, inverse, preferred_element_type=jnp.float32)
    return jnp.where(rows_ok[:, None, None], lower, 0.0).astype(jnp.bfloat16)


def eliminate(matrix, lower, upper, pivot, rows_ok, cols_ok, local, front_cols):
    product = jnp.einsum("iab,jbc->ijac", lower, upper, preferred_element_type=jnp.float32)
    update = rows_ok[:, None] & cols_ok[None, :] & (local > 0)
    changed = (matrix.astype(jnp.float32) - product).astype(jnp.bfloat16)
    result = jnp.where(update[:, :, None, None], changed, matrix)
    place = rows_ok[:, None] & (front_cols == pivot)[None, :]
    return jnp.where(place[:, :, None, None], lower[:, None], result)


def update_kernel(codes, front_ref, l1_ref, l2_ref, u1_ref, u2_ref, out_ref):
    i = pl.program_id(0)
    lower1 = l1_ref[0]
    lower2 = l2_ref[0]
    for j in range(front_ref.shape[1]):
        code = codes[i, j]
        block = front_ref[0, j]
        block = jnp.where((code & 1) != 0, block, jnp.zeros_like(block))
        product = jnp.dot(lower1, u1_ref[j], preferred_element_type=jnp.float32)
        changed = (block.astype(jnp.float32) - product).astype(jnp.bfloat16)
        block = jnp.where((code & 2) != 0, changed, block)
        block = jnp.where((code & 4) != 0, lower1, block)
        product = jnp.dot(lower2, u2_ref[j], preferred_element_type=jnp.float32)
        changed = (block.astype(jnp.float32) - product).astype(jnp.bfloat16)
        block = jnp.where((code & 8) != 0, changed, block)
        block = jnp.where((code & 16) != 0, lower2, block)
        out_ref[0, j] = block


def both_updates(front, codes, lower1, lower2, upper1, upper2):
    rows, cols, bs, _ = front.shape
    row_block = pl.BlockSpec((1, cols, bs, bs), lambda i, c: (i, 0, 0, 0))
    lower_block = pl.BlockSpec((1, bs, bs), lambda i, c: (i, 0, 0))
    upper_block = pl.BlockSpec((cols, bs, bs), lambda i, c: (0, 0, 0))
    return pl.pallas_call(
        update_kernel,
        grid_spec=pltpu.PrefetchScalarGridSpec(
            num_scalar_prefetch=1,
            grid=(rows,),
            in_specs=[row_block, lower_block, lower_block, upper_block, upper_block],
            out_specs=row_block,
        ),
        out_shape=jax.ShapeDtypeStruct(front.shape, front.dtype),
        compiler_params=pltpu.CompilerParams(dimension_semantics=("arbitrary",)),
    )(codes, front, lower1, lower2, upper1, upper2)


def masked(blocks, keep):
    shape = keep.shape + (1,) * (blocks.ndim - keep.ndim)
    return jnp.where(keep.reshape(shape) > 0, blocks, jnp.zeros_like(blocks))


def body(front, pattern, pivots, pivot_inv):
    rows_dev = front.shape[0]
    cols_dev = front.shape[1]
    nrow = lax.axis_size("row")
    ncol = lax.axis_size("col")
    row_index = lax.axis_index("row")
    col_index = lax.axis_index("col")
    grid = pattern.reshape(rows_dev, nrow, cols_dev, ncol)
    local = lax.dynamic_index_in_dim(grid, row_index, 1, keepdims=False)
    local = lax.dynamic_index_in_dim(local, col_index, 2, keepdims=False)
    front_rows = jnp.arange(rows_dev, dtype=jnp.int32) * nrow + row_index
    front_cols = jnp.arange(cols_dev, dtype=jnp.int32) * ncol + col_index
    first = pivots[0]
    second = pivots[1]
    rows_first = front_rows != first
    cols_first = front_cols != first
    rows_second = rows_first & (front_rows != second)
    cols_second = cols_first & (front_cols != second)

    a1, b1 = first // nrow, first // ncol
    a2, b2 = second // nrow, second // ncol
    r1, c1 = first % nrow, first % ncol
    r2, c2 = second % nrow, second % ncol

    def local_row(a):
        return masked(
            lax.dynamic_index_in_dim(front, a, 0, keepdims=False),
            lax.dynamic_index_in_dim(local, a, 0, keepdims=False),
        )

    def local_col(b):
        return masked(
            lax.dynamic_index_in_dim(front, b, 1, keepdims=False),
            lax.dynamic_index_in_dim(local, b, 1, keepdims=False),
        )

    lower_first = lower_local(local_col(b1), pivot_inv[0], rows_first)
    cols_sent = xor_bcast(jnp.stack([lower_first, local_col(b2)]), jnp.stack([c1, c2]), False)
    rows_sent = xor_bcast(jnp.stack([local_row(a1), local_row(a2)]), jnp.stack([r1, r2]), True)
    lower_first, second_col = cols_sent[0], cols_sent[1]
    upper_first, second_row = rows_sent[0], rows_sent[1]

    cross = all_bcast(
        jnp.stack([masked(front[a1, b2], local[a1, b2]), masked(front[a2, b1], local[a2, b1])]),
        jnp.stack([r1 * ncol + c2, r2 * ncol + c1]),
    )
    first_at_second, second_at_first = cross[0], cross[1]

    second_ok = (second != first)[None]
    lower_first_at_second = lower_local(second_at_first[None], pivot_inv[0], second_ok)
    row_after = eliminate(
        second_row[None],
        lower_first_at_second,
        upper_first,
        first,
        second_ok,
        cols_first,
        pattern[second][front_cols][None],
        front_cols,
    )
    upper_second = row_after[0]
    col_after = eliminate(
        second_col[:, None],
        lower_first,
        first_at_second[None],
        first,
        rows_first,
        second_ok,
        pattern[front_rows, second][:, None],
        second[None],
    )
    lower_second = lower_local(col_after[:, 0], pivot_inv[1], rows_second)

    keep = local > 0
    update_first = rows_first[:, None] & cols_first[None, :] & keep
    place_first = rows_first[:, None] & (front_cols == first)[None, :]
    update_second = rows_second[:, None] & cols_second[None, :] & keep
    place_second = rows_second[:, None] & (front_cols == second)[None, :]
    codes = (
        keep.astype(jnp.int32)
        + 2 * update_first.astype(jnp.int32)
        + 4 * place_first.astype(jnp.int32)
        + 8 * update_second.astype(jnp.int32)
        + 16 * place_second.astype(jnp.int32)
    )
    return both_updates(front, codes, lower_first, lower_second, upper_first, upper_second)


def solution(mesh):
    placed = (P("row", "col", None, None), P(), P(), P())
    return jax.shard_map(
        body, mesh=mesh, in_specs=placed, out_specs=P("row", "col", None, None), check_vma=False
    )
```

```python
import jax
import jax.numpy as jnp
from jax import lax
from jax.experimental import pallas as pl
from jax.experimental.pallas import tpu as pltpu
from jax.sharding import PartitionSpec as P

RING = 4
CORES = 2


def per_part(cond, a, b):
    return jnp.where(cond.reshape((-1,) + (1,) * (a.ndim - 1)), a, b)


def pick(index, options):
    out = options[-1]
    for k in range(len(options) - 2, -1, -1):
        out = jnp.where(index == k, options[k], out)
    return out


def ring_bcast(value, axis, plus, minus, me, root):
    half = value.shape[0] // 2
    first, second = value[:half], value[half:]
    got_plus = lax.ppermute(first, axis, plus)
    got_minus = lax.ppermute(second, axis, minus)
    dist = (me - root) % RING
    at_root = dist == 0
    send_plus = jnp.where(at_root, second, got_plus)
    send_minus = jnp.where(at_root, first, got_minus)
    got_plus2 = lax.ppermute(send_plus, axis, plus)
    got_minus2 = lax.ppermute(send_minus, axis, minus)
    out_first = pick(dist, [first, got_plus, got_plus2, got_minus2])
    out_second = pick(dist, [second, got_plus2, got_minus2, got_minus])
    return jnp.concatenate([out_first, out_second], axis=0)


def row_pairs(step_z, step_x):
    return [
        (RING * z + x, RING * ((z + step_z) % RING) + (x + step_x) % RING)
        for z in range(RING)
        for x in range(RING)
    ]


def row_bcast(value, root):
    me = lax.axis_index("row")
    mz, mx = me // RING, me % RING
    rz, rx = root // RING, root % RING
    xp, xm = row_pairs(0, 1), row_pairs(0, RING - 1)
    zp, zm = row_pairs(1, 0), row_pairs(RING - 1, 0)
    half = value.shape[0] // 2
    along_x = value[:half]
    along_z = value[half:]
    along_x = ring_bcast(along_x, "row", xp, xm, mx, rx)
    along_z = ring_bcast(along_z, "row", zp, zm, mz, rz)
    along_x = ring_bcast(along_x, "row", zp, zm, mz, rz)
    along_z = ring_bcast(along_z, "row", xp, xm, mx, rx)
    return jnp.concatenate([along_x, along_z], axis=0)


def col_bcast(value, root):
    me = lax.axis_index("col")
    my, mk = me // CORES, me % CORES
    ry = root // CORES
    swap = [(CORES * y + k, CORES * y + 1 - k) for y in range(RING) for k in range(CORES)]
    hop = [(CORES * y, CORES * ((y + 1) % RING)) for y in range(RING)] + [
        (CORES * y + 1, CORES * ((y - 1) % RING) + 1) for y in range(RING)
    ]
    got_swap = lax.ppermute(value, "col", swap)
    on_root_chip = jnp.where(me == root, value, got_swap)
    got_hop = lax.ppermute(on_root_chip, "col", hop)
    dist = (my - ry) % RING
    near = jnp.where(dist == 0, on_root_chip, got_hop)
    got_swap2 = lax.ppermute(near, "col", swap)
    half = value.shape[0] // 2
    fwd = jnp.where(mk == 0, near[:half], near[half:])
    got_fwd = lax.ppermute(fwd, "col", hop)
    got_swap3 = lax.ppermute(got_fwd, "col", swap)
    far = jnp.where(
        mk == 0,
        jnp.concatenate([got_fwd, got_swap3], axis=0),
        jnp.concatenate([got_swap3, got_fwd], axis=0),
    )
    own_hop = (dist == 1) & (mk == 0) | (dist == 3) & (mk == 1)
    other_hop = (dist == 1) & (mk == 1) | (dist == 3) & (mk == 0)
    out = jnp.where(own_hop, got_hop, far)
    out = jnp.where(other_hop, got_swap2, out)
    return jnp.where(dist == 0, on_root_chip, out)


ROW_ORDERS = ((3, 2, 1, 0), (1, 0, 3, 2))
COL_ORDER = (0, 1, 2)


def xor_pairs(nrow, ncol, on_row, step):
    pairs = []
    for r in range(nrow):
        for c in range(ncol):
            if on_row:
                pairs.append((r * ncol + c, (r ^ (1 << ROW_ORDERS[c % CORES][step])) * ncol + c))
            else:
                pairs.append((r * ncol + c, r * ncol + (c ^ (1 << COL_ORDER[step]))))
    return pairs


def xor_bcast(value, root, on_row):
    nrow = lax.axis_size("row")
    ncol = lax.axis_size("col")
    me = lax.axis_index("row") if on_row else lax.axis_index("col")
    parity = lax.axis_index("col") % CORES
    steps = (nrow if on_row else ncol).bit_length() - 1
    relative = me ^ root

    def bit(step):
        if on_row:
            b = jnp.where(parity == 0, ROW_ORDERS[0][step], ROW_ORDERS[1][step])
        else:
            b = COL_ORDER[step]
        return (relative >> b) & 1

    shape = value.shape
    pieces = 1 << steps
    buf = value.reshape(shape[0], pieces, -1, shape[-1])
    axes = ("row", "col")
    for step in range(steps):
        half = buf.shape[1] // 2
        got = lax.ppermute(buf[:, half:], axes, xor_pairs(nrow, ncol, on_row, step))
        buf = per_part(bit(step) == 1, got, buf[:, :half])
    for step in reversed(range(steps)):
        got = lax.ppermute(buf, axes, xor_pairs(nrow, ncol, on_row, step))
        low = bit(step) == 0
        buf = per_part(low, jnp.concatenate([buf, got], 1), jnp.concatenate([got, buf], 1))
    return buf.reshape(shape)


def all_bcast(value, root):
    nrow = lax.axis_size("row")
    ncol = lax.axis_size("col")
    n = nrow * ncol
    relative = (lax.axis_index("row") * ncol + lax.axis_index("col")) ^ root
    for b in range(n.bit_length() - 1):
        got = lax.ppermute(value, ("row", "col"), [(d, d ^ (1 << b)) for d in range(n)])
        value = per_part((relative >> b) == 1, got, value)
    return value


def lower_local(column, inverse, rows_ok):
    lower = jnp.einsum("iab,bc->iac", column, inverse, preferred_element_type=jnp.float32)
    return jnp.where(rows_ok[:, None, None], lower, 0.0).astype(jnp.bfloat16)


def eliminate(matrix, lower, upper, pivot, rows_ok, cols_ok, local, front_cols):
    product = jnp.einsum("iab,jbc->ijac", lower, upper, preferred_element_type=jnp.float32)
    update = rows_ok[:, None] & cols_ok[None, :] & (local > 0)
    changed = (matrix.astype(jnp.float32) - product).astype(jnp.bfloat16)
    result = jnp.where(update[:, :, None, None], changed, matrix)
    place = rows_ok[:, None] & (front_cols == pivot)[None, :]
    return jnp.where(place[:, :, None, None], lower[:, None], result)


def update_kernel(codes, front_ref, l1_ref, l2_ref, u1_ref, u2_ref, out_ref):
    i = pl.program_id(0)
    for j in range(front_ref.shape[1]):
        code = codes[i, j]
        block = front_ref[0, j]
        out_ref[0, j] = jnp.where((code & 1) != 0, block, jnp.zeros_like(block))

        def step(lower_ref, upper_ref, update_bit, place_bit, j=j, code=code):
            @pl.when((code & update_bit) != 0)
            def _():
                product = jnp.dot(lower_ref[0], upper_ref[j], preferred_element_type=jnp.float32)
                out_ref[0, j] = (out_ref[0, j].astype(jnp.float32) - product).astype(jnp.bfloat16)

            @pl.when((code & place_bit) != 0)
            def _():
                out_ref[0, j] = lower_ref[0]

        step(l1_ref, u1_ref, 2, 4)
        step(l2_ref, u2_ref, 8, 16)


def both_updates(front, codes, lower1, lower2, upper1, upper2):
    rows, cols, bs, _ = front.shape
    row_block = pl.BlockSpec((1, cols, bs, bs), lambda i, c: (i, 0, 0, 0))
    lower_block = pl.BlockSpec((1, bs, bs), lambda i, c: (i, 0, 0))
    upper_block = pl.BlockSpec((cols, bs, bs), lambda i, c: (0, 0, 0))
    return pl.pallas_call(
        update_kernel,
        grid_spec=pltpu.PrefetchScalarGridSpec(
            num_scalar_prefetch=1,
            grid=(rows,),
            in_specs=[row_block, lower_block, lower_block, upper_block, upper_block],
            out_specs=row_block,
        ),
        out_shape=jax.ShapeDtypeStruct(front.shape, front.dtype),
        compiler_params=pltpu.CompilerParams(dimension_semantics=("arbitrary",)),
    )(codes, front, lower1, lower2, upper1, upper2)


def masked(blocks, keep):
    shape = keep.shape + (1,) * (blocks.ndim - keep.ndim)
    return jnp.where(keep.reshape(shape) > 0, blocks, jnp.zeros_like(blocks))


def body(front, pattern, pivots, pivot_inv):
    rows_dev = front.shape[0]
    cols_dev = front.shape[1]
    nrow = lax.axis_size("row")
    ncol = lax.axis_size("col")
    row_index = lax.axis_index("row")
    col_index = lax.axis_index("col")
    grid = pattern.reshape(rows_dev, nrow, cols_dev, ncol)
    local = lax.dynamic_index_in_dim(grid, row_index, 1, keepdims=False)
    local = lax.dynamic_index_in_dim(local, col_index, 2, keepdims=False)
    front_rows = jnp.arange(rows_dev, dtype=jnp.int32) * nrow + row_index
    front_cols = jnp.arange(cols_dev, dtype=jnp.int32) * ncol + col_index
    first = pivots[0]
    second = pivots[1]
    rows_first = front_rows != first
    cols_first = front_cols != first
    rows_second = rows_first & (front_rows != second)
    cols_second = cols_first & (front_cols != second)

    a1, b1 = first // nrow, first // ncol
    a2, b2 = second // nrow, second // ncol
    r1, c1 = first % nrow, first % ncol
    r2, c2 = second % nrow, second % ncol

    def local_row(a):
        return masked(
            lax.dynamic_index_in_dim(front, a, 0, keepdims=False),
            lax.dynamic_index_in_dim(local, a, 0, keepdims=False),
        )

    def local_col(b):
        return masked(
            lax.dynamic_index_in_dim(front, b, 1, keepdims=False),
            lax.dynamic_index_in_dim(local, b, 1, keepdims=False),
        )

    lower_first = lower_local(local_col(b1), pivot_inv[0], rows_first)
    cols_sent = xor_bcast(jnp.stack([lower_first, local_col(b2)]), jnp.stack([c1, c2]), False)
    rows_sent = xor_bcast(jnp.stack([local_row(a1), local_row(a2)]), jnp.stack([r1, r2]), True)
    lower_first, second_col = cols_sent[0], cols_sent[1]
    upper_first, second_row = rows_sent[0], rows_sent[1]

    cross = all_bcast(
        jnp.stack([masked(front[a1, b2], local[a1, b2]), masked(front[a2, b1], local[a2, b1])]),
        jnp.stack([r1 * ncol + c2, r2 * ncol + c1]),
    )
    first_at_second, second_at_first = cross[0], cross[1]

    second_ok = (second != first)[None]
    lower_first_at_second = lower_local(second_at_first[None], pivot_inv[0], second_ok)
    row_after = eliminate(
        second_row[None],
        lower_first_at_second,
        upper_first,
        first,
        second_ok,
        cols_first,
        pattern[second][front_cols][None],
        front_cols,
    )
    upper_second = row_after[0]
    col_after = eliminate(
        second_col[:, None],
        lower_first,
        first_at_second[None],
        first,
        rows_first,
        second_ok,
        pattern[front_rows, second][:, None],
        second[None],
    )
    lower_second = lower_local(col_after[:, 0], pivot_inv[1], rows_second)

    keep = local > 0
    update_first = rows_first[:, None] & cols_first[None, :] & keep
    place_first = rows_first[:, None] & (front_cols == first)[None, :]
    update_second = rows_second[:, None] & cols_second[None, :] & keep
    place_second = rows_second[:, None] & (front_cols == second)[None, :]
    codes = (
        keep.astype(jnp.int32)
        + 2 * update_first.astype(jnp.int32)
        + 4 * place_first.astype(jnp.int32)
        + 8 * update_second.astype(jnp.int32)
        + 16 * place_second.astype(jnp.int32)
    )
    return both_updates(front, codes, lower_first, lower_second, upper_first, upper_second)


def solution(mesh):
    placed = (P("row", "col", None, None), P(), P(), P())
    return jax.shard_map(
        body, mesh=mesh, in_specs=placed, out_specs=P("row", "col", None, None), check_vma=False
    )
```

```python
import jax
import jax.numpy as jnp
from jax import lax
from jax.experimental import pallas as pl
from jax.experimental.pallas import tpu as pltpu
from jax.sharding import PartitionSpec as P

RING = 4
CORES = 2


def per_part(cond, a, b):
    return jnp.where(cond.reshape((-1,) + (1,) * (a.ndim - 1)), a, b)


def pick(index, options):
    out = options[-1]
    for k in range(len(options) - 2, -1, -1):
        out = per_part(index == k, options[k], out)
    return out


def ring_bcast(value, axis, plus, minus, me, root):
    half = value.shape[0] // 2
    first, second = value[:half], value[half:]
    got_plus = lax.ppermute(first, axis, plus)
    got_minus = lax.ppermute(second, axis, minus)
    dist = (me - root) % RING
    at_root = dist == 0
    send_plus = jnp.where(at_root, second, got_plus)
    send_minus = jnp.where(at_root, first, got_minus)
    got_plus2 = lax.ppermute(send_plus, axis, plus)
    got_minus2 = lax.ppermute(send_minus, axis, minus)
    out_first = pick(dist, [first, got_plus, got_plus2, got_minus2])
    out_second = pick(dist, [second, got_plus2, got_minus2, got_minus])
    return jnp.concatenate([out_first, out_second], axis=0)


def row_pairs(step_z, step_x):
    return [
        (RING * z + x, RING * ((z + step_z) % RING) + (x + step_x) % RING)
        for z in range(RING)
        for x in range(RING)
    ]


def row_bcast(value, root):
    me = lax.axis_index("row")
    mz, mx = me // RING, me % RING
    rz, rx = root // RING, root % RING
    xp, xm = row_pairs(0, 1), row_pairs(0, RING - 1)
    zp, zm = row_pairs(1, 0), row_pairs(RING - 1, 0)
    half = value.shape[0] // 2
    along_x = value[:half]
    along_z = value[half:]
    along_x = ring_bcast(along_x, "row", xp, xm, mx, rx)
    along_z = ring_bcast(along_z, "row", zp, zm, mz, rz)
    along_x = ring_bcast(along_x, "row", zp, zm, mz, rz)
    along_z = ring_bcast(along_z, "row", xp, xm, mx, rx)
    return jnp.concatenate([along_x, along_z], axis=0)


def col_bcast(value, root):
    me = lax.axis_index("col")
    my, mk = me // CORES, me % CORES
    ry = root // CORES
    swap = [(CORES * y + k, CORES * y + 1 - k) for y in range(RING) for k in range(CORES)]
    hop = [(CORES * y, CORES * ((y + 1) % RING)) for y in range(RING)] + [
        (CORES * y + 1, CORES * ((y - 1) % RING) + 1) for y in range(RING)
    ]
    got_swap = lax.ppermute(value, "col", swap)
    on_root_chip = jnp.where(me == root, value, got_swap)
    got_hop = lax.ppermute(on_root_chip, "col", hop)
    dist = (my - ry) % RING
    near = jnp.where(dist == 0, on_root_chip, got_hop)
    got_swap2 = lax.ppermute(near, "col", swap)
    half = value.shape[0] // 2
    fwd = jnp.where(mk == 0, near[:half], near[half:])
    got_fwd = lax.ppermute(fwd, "col", hop)
    got_swap3 = lax.ppermute(got_fwd, "col", swap)
    far = jnp.where(
        mk == 0,
        jnp.concatenate([got_fwd, got_swap3], axis=0),
        jnp.concatenate([got_swap3, got_fwd], axis=0),
    )
    own_hop = (dist == 1) & (mk == 0) | (dist == 3) & (mk == 1)
    other_hop = (dist == 1) & (mk == 1) | (dist == 3) & (mk == 0)
    out = jnp.where(own_hop, got_hop, far)
    out = jnp.where(other_hop, got_swap2, out)
    return jnp.where(dist == 0, on_root_chip, out)


ROW_ORDERS = ((3, 2, 1, 0), (1, 0, 3, 2))
COL_ORDER = (0, 1, 2)


def xor_pairs(nrow, ncol, on_row, step):
    pairs = []
    for r in range(nrow):
        for c in range(ncol):
            if on_row:
                pairs.append((r * ncol + c, (r ^ (1 << ROW_ORDERS[c % CORES][step])) * ncol + c))
            else:
                pairs.append((r * ncol + c, r * ncol + (c ^ (1 << COL_ORDER[step]))))
    return pairs


def dims_of(on_row, parity, step):
    if on_row:
        z_first = (parity == 0) == (step == 0)
        return (2 if z_first else 0), RING
    return ((0, CORES), (1, RING))[step]


def digit_pairs(nrow, ncol, on_row, step, mask):
    pairs = []
    for r in range(nrow):
        for c in range(ncol):
            shift, _ = dims_of(on_row, c % CORES, step)
            if on_row:
                pairs.append((r * ncol + c, (r ^ (mask << shift)) * ncol + c))
            else:
                pairs.append((r * ncol + c, r * ncol + (c ^ (mask << shift))))
    return pairs


def xor_bcast(value, root, on_row):
    nrow = lax.axis_size("row")
    ncol = lax.axis_size("col")
    me = lax.axis_index("row") if on_row else lax.axis_index("col")
    parity = lax.axis_index("col") % CORES
    relative = me ^ root
    axes = ("row", "col")

    def digit(step):
        if on_row:
            shift = jnp.where(parity == 0, 2 if step == 0 else 0, 0 if step == 0 else 2)
        else:
            shift = dims_of(False, 0, step)[0]
        return (relative >> shift) & (RING - 1 if on_row or step == 1 else CORES - 1)

    sizes = [dims_of(on_row, 0, step)[1] for step in range(2)]
    shape = value.shape
    buf = value.reshape(shape[0], sizes[0], sizes[1], -1, shape[-1])
    for step in range(2):
        d = digit(step)
        groups = [buf[:, m] for m in range(sizes[step])]
        got = [None] + [
            lax.ppermute(groups[m], axes, digit_pairs(nrow, ncol, on_row, step, m))
            for m in range(1, sizes[step])
        ]
        buf = pick(d, [groups[0]] + got[1:])
    for step in reversed(range(2)):
        d = digit(step)
        got = [buf] + [
            lax.ppermute(buf, axes, digit_pairs(nrow, ncol, on_row, step, m))
            for m in range(1, sizes[step])
        ]
        buf = jnp.stack(
            [pick(d, [got[dd ^ t] for dd in range(sizes[step])]) for t in range(sizes[step])], axis=1
        )
    return buf.reshape(shape)


def all_bcast(value, root):
    nrow = lax.axis_size("row")
    ncol = lax.axis_size("col")
    n = nrow * ncol
    relative = (lax.axis_index("row") * ncol + lax.axis_index("col")) ^ root
    for b in range(n.bit_length() - 1):
        got = lax.ppermute(value, ("row", "col"), [(d, d ^ (1 << b)) for d in range(n)])
        value = per_part((relative >> b) == 1, got, value)
    return value


def lower_local(column, inverse, rows_ok):
    lower = jnp.einsum("iab,bc->iac", column, inverse, preferred_element_type=jnp.float32)
    return jnp.where(rows_ok[:, None, None], lower, 0.0).astype(jnp.bfloat16)


def eliminate(matrix, lower, upper, pivot, rows_ok, cols_ok, local, front_cols):
    product = jnp.einsum("iab,jbc->ijac", lower, upper, preferred_element_type=jnp.float32)
    update = rows_ok[:, None] & cols_ok[None, :] & (local > 0)
    changed = (matrix.astype(jnp.float32) - product).astype(jnp.bfloat16)
    result = jnp.where(update[:, :, None, None], changed, matrix)
    place = rows_ok[:, None] & (front_cols == pivot)[None, :]
    return jnp.where(place[:, :, None, None], lower[:, None], result)


def update_kernel(codes, front_ref, l1_ref, l2_ref, u1_ref, u2_ref, out_ref):
    i = pl.program_id(0)
    lower1 = l1_ref[0]
    lower2 = l2_ref[0]
    for j in range(front_ref.shape[1]):
        code = codes[i, j]
        block = front_ref[0, j]
        block = jnp.where((code & 1) != 0, block, jnp.zeros_like(block))
        product = jnp.dot(lower1, u1_ref[j], preferred_element_type=jnp.float32)
        changed = (block.astype(jnp.float32) - product).astype(jnp.bfloat16)
        block = jnp.where((code & 2) != 0, changed, block)
        block = jnp.where((code & 4) != 0, lower1, block)
        product = jnp.dot(lower2, u2_ref[j], preferred_element_type=jnp.float32)
        changed = (block.astype(jnp.float32) - product).astype(jnp.bfloat16)
        block = jnp.where((code & 8) != 0, changed, block)
        block = jnp.where((code & 16) != 0, lower2, block)
        out_ref[0, j] = block


def both_updates(front, codes, lower1, lower2, upper1, upper2):
    rows, cols, bs, _ = front.shape
    row_block = pl.BlockSpec((1, cols, bs, bs), lambda i, c: (i, 0, 0, 0))
    lower_block = pl.BlockSpec((1, bs, bs), lambda i, c: (i, 0, 0))
    upper_block = pl.BlockSpec((cols, bs, bs), lambda i, c: (0, 0, 0))
    return pl.pallas_call(
        update_kernel,
        grid_spec=pltpu.PrefetchScalarGridSpec(
            num_scalar_prefetch=1,
            grid=(rows,),
            in_specs=[row_block, lower_block, lower_block, upper_block, upper_block],
            out_specs=row_block,
        ),
        out_shape=jax.ShapeDtypeStruct(front.shape, front.dtype),
        compiler_params=pltpu.CompilerParams(dimension_semantics=("arbitrary",)),
    )(codes, front, lower1, lower2, upper1, upper2)


def masked(blocks, keep):
    shape = keep.shape + (1,) * (blocks.ndim - keep.ndim)
    return jnp.where(keep.reshape(shape) > 0, blocks, jnp.zeros_like(blocks))


def body(front, pattern, pivots, pivot_inv):
    rows_dev = front.shape[0]
    cols_dev = front.shape[1]
    nrow = lax.axis_size("row")
    ncol = lax.axis_size("col")
    row_index = lax.axis_index("row")
    col_index = lax.axis_index("col")
    grid = pattern.reshape(rows_dev, nrow, cols_dev, ncol)
    local = lax.dynamic_index_in_dim(grid, row_index, 1, keepdims=False)
    local = lax.dynamic_index_in_dim(local, col_index, 2, keepdims=False)
    front_rows = jnp.arange(rows_dev, dtype=jnp.int32) * nrow + row_index
    front_cols = jnp.arange(cols_dev, dtype=jnp.int32) * ncol + col_index
    first = pivots[0]
    second = pivots[1]
    rows_first = front_rows != first
    cols_first = front_cols != first
    rows_second = rows_first & (front_rows != second)
    cols_second = cols_first & (front_cols != second)

    a1, b1 = first // nrow, first // ncol
    a2, b2 = second // nrow, second // ncol
    r1, c1 = first % nrow, first % ncol
    r2, c2 = second % nrow, second % ncol

    def local_row(a):
        return masked(
            lax.dynamic_index_in_dim(front, a, 0, keepdims=False),
            lax.dynamic_index_in_dim(local, a, 0, keepdims=False),
        )

    def local_col(b):
        return masked(
            lax.dynamic_index_in_dim(front, b, 1, keepdims=False),
            lax.dynamic_index_in_dim(local, b, 1, keepdims=False),
        )

    lower_first = lower_local(local_col(b1), pivot_inv[0], rows_first)
    cols_sent = xor_bcast(jnp.stack([lower_first, local_col(b2)]), jnp.stack([c1, c2]), False)
    rows_sent = xor_bcast(jnp.stack([local_row(a1), local_row(a2)]), jnp.stack([r1, r2]), True)
    lower_first, second_col = cols_sent[0], cols_sent[1]
    upper_first, second_row = rows_sent[0], rows_sent[1]

    cross = all_bcast(
        jnp.stack([masked(front[a1, b2], local[a1, b2]), masked(front[a2, b1], local[a2, b1])]),
        jnp.stack([r1 * ncol + c2, r2 * ncol + c1]),
    )
    first_at_second, second_at_first = cross[0], cross[1]

    second_ok = (second != first)[None]
    lower_first_at_second = lower_local(second_at_first[None], pivot_inv[0], second_ok)
    row_after = eliminate(
        second_row[None],
        lower_first_at_second,
        upper_first,
        first,
        second_ok,
        cols_first,
        pattern[second][front_cols][None],
        front_cols,
    )
    upper_second = row_after[0]
    col_after = eliminate(
        second_col[:, None],
        lower_first,
        first_at_second[None],
        first,
        rows_first,
        second_ok,
        pattern[front_rows, second][:, None],
        second[None],
    )
    lower_second = lower_local(col_after[:, 0], pivot_inv[1], rows_second)

    keep = local > 0
    update_first = rows_first[:, None] & cols_first[None, :] & keep
    place_first = rows_first[:, None] & (front_cols == first)[None, :]
    update_second = rows_second[:, None] & cols_second[None, :] & keep
    place_second = rows_second[:, None] & (front_cols == second)[None, :]
    codes = (
        keep.astype(jnp.int32)
        + 2 * update_first.astype(jnp.int32)
        + 4 * place_first.astype(jnp.int32)
        + 8 * update_second.astype(jnp.int32)
        + 16 * place_second.astype(jnp.int32)
    )
    return both_updates(front, codes, lower_first, lower_second, upper_first, upper_second)


def solution(mesh):
    placed = (P("row", "col", None, None), P(), P(), P())
    return jax.shard_map(
        body, mesh=mesh, in_specs=placed, out_specs=P("row", "col", None, None), check_vma=False
    )
```

```python
import jax
import jax.numpy as jnp
from jax import lax
from jax.experimental import pallas as pl
from jax.experimental.pallas import tpu as pltpu
from jax.sharding import PartitionSpec as P

RING = 4
CORES = 2


def per_part(cond, a, b):
    return jnp.where(cond.reshape((-1,) + (1,) * (a.ndim - 1)), a, b)


def pick(index, options):
    out = options[-1]
    for k in range(len(options) - 2, -1, -1):
        out = per_part(index == k, options[k], out)
    return out


def ring_bcast(value, axis, plus, minus, me, root):
    half = value.shape[0] // 2
    first, second = value[:half], value[half:]
    got_plus = lax.ppermute(first, axis, plus)
    got_minus = lax.ppermute(second, axis, minus)
    dist = (me - root) % RING
    at_root = dist == 0
    send_plus = jnp.where(at_root, second, got_plus)
    send_minus = jnp.where(at_root, first, got_minus)
    got_plus2 = lax.ppermute(send_plus, axis, plus)
    got_minus2 = lax.ppermute(send_minus, axis, minus)
    out_first = pick(dist, [first, got_plus, got_plus2, got_minus2])
    out_second = pick(dist, [second, got_plus2, got_minus2, got_minus])
    return jnp.concatenate([out_first, out_second], axis=0)


def row_pairs(step_z, step_x):
    return [
        (RING * z + x, RING * ((z + step_z) % RING) + (x + step_x) % RING)
        for z in range(RING)
        for x in range(RING)
    ]


def row_bcast(value, root):
    me = lax.axis_index("row")
    mz, mx = me // RING, me % RING
    rz, rx = root // RING, root % RING
    xp, xm = row_pairs(0, 1), row_pairs(0, RING - 1)
    zp, zm = row_pairs(1, 0), row_pairs(RING - 1, 0)
    half = value.shape[0] // 2
    along_x = value[:half]
    along_z = value[half:]
    along_x = ring_bcast(along_x, "row", xp, xm, mx, rx)
    along_z = ring_bcast(along_z, "row", zp, zm, mz, rz)
    along_x = ring_bcast(along_x, "row", zp, zm, mz, rz)
    along_z = ring_bcast(along_z, "row", xp, xm, mx, rx)
    return jnp.concatenate([along_x, along_z], axis=0)


def col_bcast(value, root):
    me = lax.axis_index("col")
    my, mk = me // CORES, me % CORES
    ry = root // CORES
    swap = [(CORES * y + k, CORES * y + 1 - k) for y in range(RING) for k in range(CORES)]
    hop = [(CORES * y, CORES * ((y + 1) % RING)) for y in range(RING)] + [
        (CORES * y + 1, CORES * ((y - 1) % RING) + 1) for y in range(RING)
    ]
    got_swap = lax.ppermute(value, "col", swap)
    on_root_chip = jnp.where(me == root, value, got_swap)
    got_hop = lax.ppermute(on_root_chip, "col", hop)
    dist = (my - ry) % RING
    near = jnp.where(dist == 0, on_root_chip, got_hop)
    got_swap2 = lax.ppermute(near, "col", swap)
    half = value.shape[0] // 2
    fwd = jnp.where(mk == 0, near[:half], near[half:])
    got_fwd = lax.ppermute(fwd, "col", hop)
    got_swap3 = lax.ppermute(got_fwd, "col", swap)
    far = jnp.where(
        mk == 0,
        jnp.concatenate([got_fwd, got_swap3], axis=0),
        jnp.concatenate([got_swap3, got_fwd], axis=0),
    )
    own_hop = (dist == 1) & (mk == 0) | (dist == 3) & (mk == 1)
    other_hop = (dist == 1) & (mk == 1) | (dist == 3) & (mk == 0)
    out = jnp.where(own_hop, got_hop, far)
    out = jnp.where(other_hop, got_swap2, out)
    return jnp.where(dist == 0, on_root_chip, out)


ROW_ORDERS = ((3, 2, 1, 0), (1, 0, 3, 2))
COL_ORDER = (0, 1, 2)


def xor_pairs(nrow, ncol, on_row, step):
    pairs = []
    for r in range(nrow):
        for c in range(ncol):
            if on_row:
                pairs.append((r * ncol + c, (r ^ (1 << ROW_ORDERS[c % CORES][step])) * ncol + c))
            else:
                pairs.append((r * ncol + c, r * ncol + (c ^ (1 << COL_ORDER[step]))))
    return pairs


def dims_of(on_row, parity, step):
    if on_row:
        z_first = (parity == 0) == (step == 0)
        return (2 if z_first else 0), RING
    return ((0, CORES), (1, RING))[step]


def digit_pairs(nrow, ncol, on_row, step, mask):
    pairs = []
    for r in range(nrow):
        for c in range(ncol):
            shift, _ = dims_of(on_row, c % CORES, step)
            if on_row:
                pairs.append((r * ncol + c, (r ^ (mask << shift)) * ncol + c))
            else:
                pairs.append((r * ncol + c, r * ncol + (c ^ (mask << shift))))
    return pairs


def xor_bcast(value, root, on_row):
    nrow = lax.axis_size("row")
    ncol = lax.axis_size("col")
    me = lax.axis_index("row") if on_row else lax.axis_index("col")
    parity = lax.axis_index("col") % CORES
    relative = me ^ root
    axes = ("row", "col")

    def digit(step):
        if on_row:
            shift = jnp.where(parity == 0, 2 if step == 0 else 0, 0 if step == 0 else 2)
        else:
            shift = dims_of(False, 0, step)[0]
        return (relative >> shift) & (RING - 1 if on_row or step == 1 else CORES - 1)

    sizes = [dims_of(on_row, 0, step)[1] for step in range(2)]
    shape = value.shape
    buf = value.reshape(shape[0], sizes[0], sizes[1], -1, shape[-1])
    for step in range(2):
        d = digit(step)
        groups = [buf[:, m] for m in range(sizes[step])]
        got = [None] + [
            lax.ppermute(groups[m], axes, digit_pairs(nrow, ncol, on_row, step, m))
            for m in range(1, sizes[step])
        ]
        buf = pick(d, [groups[0]] + got[1:])
    for step in reversed(range(2)):
        d = digit(step)
        got = [buf] + [
            lax.ppermute(buf, axes, digit_pairs(nrow, ncol, on_row, step, m))
            for m in range(1, sizes[step])
        ]
        buf = jnp.stack(
            [pick(d, [got[dd ^ t] for dd in range(sizes[step])]) for t in range(sizes[step])], axis=1
        )
    return buf.reshape(shape)


def all_bcast(value, root):
    nrow = lax.axis_size("row")
    ncol = lax.axis_size("col")
    n = nrow * ncol
    relative = (lax.axis_index("row") * ncol + lax.axis_index("col")) ^ root
    shift = 0
    for size in (CORES, RING, RING, RING):
        mask = size - 1
        got = [value] + [
            lax.ppermute(value, ("row", "col"), [(d, d ^ (m << shift)) for d in range(n)])
            for m in range(1, size)
        ]
        value = pick((relative >> shift) & mask, got)
        shift += mask.bit_length()
    return value


def lower_local(column, inverse, rows_ok):
    lower = jnp.einsum("iab,bc->iac", column, inverse, preferred_element_type=jnp.float32)
    return jnp.where(rows_ok[:, None, None], lower, 0.0).astype(jnp.bfloat16)


def eliminate(matrix, lower, upper, pivot, rows_ok, cols_ok, local, front_cols):
    product = jnp.einsum("iab,jbc->ijac", lower, upper, preferred_element_type=jnp.float32)
    update = rows_ok[:, None] & cols_ok[None, :] & (local > 0)
    changed = (matrix.astype(jnp.float32) - product).astype(jnp.bfloat16)
    result = jnp.where(update[:, :, None, None], changed, matrix)
    place = rows_ok[:, None] & (front_cols == pivot)[None, :]
    return jnp.where(place[:, :, None, None], lower[:, None], result)


def update_kernel(codes, front_ref, l1_ref, l2_ref, u1_ref, u2_ref, out_ref):
    i = pl.program_id(0)
    lower1 = l1_ref[0]
    lower2 = l2_ref[0]
    for j in range(front_ref.shape[1]):
        code = codes[i, j]
        block = front_ref[0, j]
        block = jnp.where((code & 1) != 0, block, jnp.zeros_like(block))
        product = jnp.dot(lower1, u1_ref[j], preferred_element_type=jnp.float32)
        changed = (block.astype(jnp.float32) - product).astype(jnp.bfloat16)
        block = jnp.where((code & 2) != 0, changed, block)
        block = jnp.where((code & 4) != 0, lower1, block)
        product = jnp.dot(lower2, u2_ref[j], preferred_element_type=jnp.float32)
        changed = (block.astype(jnp.float32) - product).astype(jnp.bfloat16)
        block = jnp.where((code & 8) != 0, changed, block)
        block = jnp.where((code & 16) != 0, lower2, block)
        out_ref[0, j] = block


def both_updates(front, codes, lower1, lower2, upper1, upper2):
    rows, cols, bs, _ = front.shape
    row_block = pl.BlockSpec((1, cols, bs, bs), lambda i, c: (i, 0, 0, 0))
    lower_block = pl.BlockSpec((1, bs, bs), lambda i, c: (i, 0, 0))
    upper_block = pl.BlockSpec((cols, bs, bs), lambda i, c: (0, 0, 0))
    return pl.pallas_call(
        update_kernel,
        grid_spec=pltpu.PrefetchScalarGridSpec(
            num_scalar_prefetch=1,
            grid=(rows,),
            in_specs=[row_block, lower_block, lower_block, upper_block, upper_block],
            out_specs=row_block,
        ),
        out_shape=jax.ShapeDtypeStruct(front.shape, front.dtype),
        compiler_params=pltpu.CompilerParams(dimension_semantics=("arbitrary",)),
    )(codes, front, lower1, lower2, upper1, upper2)


def masked(blocks, keep):
    shape = keep.shape + (1,) * (blocks.ndim - keep.ndim)
    return jnp.where(keep.reshape(shape) > 0, blocks, jnp.zeros_like(blocks))


def body(front, pattern, pivots, pivot_inv):
    rows_dev = front.shape[0]
    cols_dev = front.shape[1]
    nrow = lax.axis_size("row")
    ncol = lax.axis_size("col")
    row_index = lax.axis_index("row")
    col_index = lax.axis_index("col")
    grid = pattern.reshape(rows_dev, nrow, cols_dev, ncol)
    local = lax.dynamic_index_in_dim(grid, row_index, 1, keepdims=False)
    local = lax.dynamic_index_in_dim(local, col_index, 2, keepdims=False)
    front_rows = jnp.arange(rows_dev, dtype=jnp.int32) * nrow + row_index
    front_cols = jnp.arange(cols_dev, dtype=jnp.int32) * ncol + col_index
    first = pivots[0]
    second = pivots[1]
    rows_first = front_rows != first
    cols_first = front_cols != first
    rows_second = rows_first & (front_rows != second)
    cols_second = cols_first & (front_cols != second)

    a1, b1 = first // nrow, first // ncol
    a2, b2 = second // nrow, second // ncol
    r1, c1 = first % nrow, first % ncol
    r2, c2 = second % nrow, second % ncol

    def local_row(a):
        return masked(
            lax.dynamic_index_in_dim(front, a, 0, keepdims=False),
            lax.dynamic_index_in_dim(local, a, 0, keepdims=False),
        )

    def local_col(b):
        return masked(
            lax.dynamic_index_in_dim(front, b, 1, keepdims=False),
            lax.dynamic_index_in_dim(local, b, 1, keepdims=False),
        )

    lower_first = lower_local(local_col(b1), pivot_inv[0], rows_first)
    cols_sent = xor_bcast(jnp.stack([lower_first, local_col(b2)]), jnp.stack([c1, c2]), False)
    rows_sent = xor_bcast(jnp.stack([local_row(a1), local_row(a2)]), jnp.stack([r1, r2]), True)
    lower_first, second_col = cols_sent[0], cols_sent[1]
    upper_first, second_row = rows_sent[0], rows_sent[1]

    cross = all_bcast(
        jnp.stack([masked(front[a1, b2], local[a1, b2]), masked(front[a2, b1], local[a2, b1])]),
        jnp.stack([r1 * ncol + c2, r2 * ncol + c1]),
    )
    first_at_second, second_at_first = cross[0], cross[1]

    second_ok = (second != first)[None]
    lower_first_at_second = lower_local(second_at_first[None], pivot_inv[0], second_ok)
    row_after = eliminate(
        second_row[None],
        lower_first_at_second,
        upper_first,
        first,
        second_ok,
        cols_first,
        pattern[second][front_cols][None],
        front_cols,
    )
    upper_second = row_after[0]
    col_after = eliminate(
        second_col[:, None],
        lower_first,
        first_at_second[None],
        first,
        rows_first,
        second_ok,
        pattern[front_rows, second][:, None],
        second[None],
    )
    lower_second = lower_local(col_after[:, 0], pivot_inv[1], rows_second)

    keep = local > 0
    update_first = rows_first[:, None] & cols_first[None, :] & keep
    place_first = rows_first[:, None] & (front_cols == first)[None, :]
    update_second = rows_second[:, None] & cols_second[None, :] & keep
    place_second = rows_second[:, None] & (front_cols == second)[None, :]
    codes = (
        keep.astype(jnp.int32)
        + 2 * update_first.astype(jnp.int32)
        + 4 * place_first.astype(jnp.int32)
        + 8 * update_second.astype(jnp.int32)
        + 16 * place_second.astype(jnp.int32)
    )
    return both_updates(front, codes, lower_first, lower_second, upper_first, upper_second)


def solution(mesh):
    placed = (P("row", "col", None, None), P(), P(), P())
    return jax.shard_map(
        body, mesh=mesh, in_specs=placed, out_specs=P("row", "col", None, None), check_vma=False
    )
```

```python
import jax
import jax.numpy as jnp
from jax import lax
from jax.experimental import pallas as pl
from jax.experimental.pallas import tpu as pltpu
from jax.sharding import PartitionSpec as P

RING = 4
CORES = 2


def per_part(cond, a, b):
    return jnp.where(cond.reshape((-1,) + (1,) * (a.ndim - 1)), a, b)


def pick(index, options):
    out = options[-1]
    for k in range(len(options) - 2, -1, -1):
        out = per_part(index == k, options[k], out)
    return out


def ring_bcast(value, axis, plus, minus, me, root):
    half = value.shape[0] // 2
    first, second = value[:half], value[half:]
    got_plus = lax.ppermute(first, axis, plus)
    got_minus = lax.ppermute(second, axis, minus)
    dist = (me - root) % RING
    at_root = dist == 0
    send_plus = jnp.where(at_root, second, got_plus)
    send_minus = jnp.where(at_root, first, got_minus)
    got_plus2 = lax.ppermute(send_plus, axis, plus)
    got_minus2 = lax.ppermute(send_minus, axis, minus)
    out_first = pick(dist, [first, got_plus, got_plus2, got_minus2])
    out_second = pick(dist, [second, got_plus2, got_minus2, got_minus])
    return jnp.concatenate([out_first, out_second], axis=0)


def row_pairs(step_z, step_x):
    return [
        (RING * z + x, RING * ((z + step_z) % RING) + (x + step_x) % RING)
        for z in range(RING)
        for x in range(RING)
    ]


def row_bcast(value, root):
    me = lax.axis_index("row")
    mz, mx = me // RING, me % RING
    rz, rx = root // RING, root % RING
    xp, xm = row_pairs(0, 1), row_pairs(0, RING - 1)
    zp, zm = row_pairs(1, 0), row_pairs(RING - 1, 0)
    half = value.shape[0] // 2
    along_x = value[:half]
    along_z = value[half:]
    along_x = ring_bcast(along_x, "row", xp, xm, mx, rx)
    along_z = ring_bcast(along_z, "row", zp, zm, mz, rz)
    along_x = ring_bcast(along_x, "row", zp, zm, mz, rz)
    along_z = ring_bcast(along_z, "row", xp, xm, mx, rx)
    return jnp.concatenate([along_x, along_z], axis=0)


def col_bcast(value, root):
    me = lax.axis_index("col")
    my, mk = me // CORES, me % CORES
    ry = root // CORES
    swap = [(CORES * y + k, CORES * y + 1 - k) for y in range(RING) for k in range(CORES)]
    hop = [(CORES * y, CORES * ((y + 1) % RING)) for y in range(RING)] + [
        (CORES * y + 1, CORES * ((y - 1) % RING) + 1) for y in range(RING)
    ]
    got_swap = lax.ppermute(value, "col", swap)
    on_root_chip = jnp.where(me == root, value, got_swap)
    got_hop = lax.ppermute(on_root_chip, "col", hop)
    dist = (my - ry) % RING
    near = jnp.where(dist == 0, on_root_chip, got_hop)
    got_swap2 = lax.ppermute(near, "col", swap)
    half = value.shape[0] // 2
    fwd = jnp.where(mk == 0, near[:half], near[half:])
    got_fwd = lax.ppermute(fwd, "col", hop)
    got_swap3 = lax.ppermute(got_fwd, "col", swap)
    far = jnp.where(
        mk == 0,
        jnp.concatenate([got_fwd, got_swap3], axis=0),
        jnp.concatenate([got_swap3, got_fwd], axis=0),
    )
    own_hop = (dist == 1) & (mk == 0) | (dist == 3) & (mk == 1)
    other_hop = (dist == 1) & (mk == 1) | (dist == 3) & (mk == 0)
    out = jnp.where(own_hop, got_hop, far)
    out = jnp.where(other_hop, got_swap2, out)
    return jnp.where(dist == 0, on_root_chip, out)


ROW_ORDERS = ((3, 2, 1, 0), (1, 0, 3, 2))
COL_ORDER = (0, 1, 2)


def xor_pairs(nrow, ncol, on_row, step):
    pairs = []
    for r in range(nrow):
        for c in range(ncol):
            if on_row:
                pairs.append((r * ncol + c, (r ^ (1 << ROW_ORDERS[c % CORES][step])) * ncol + c))
            else:
                pairs.append((r * ncol + c, r * ncol + (c ^ (1 << COL_ORDER[step]))))
    return pairs


def dims_of(on_row, parity, step):
    if on_row:
        z_first = (parity == 0) == (step == 0)
        return (2 if z_first else 0), RING
    return ((0, CORES), (1, RING))[step]


def digit_pairs(nrow, ncol, on_row, step, mask):
    pairs = []
    for r in range(nrow):
        for c in range(ncol):
            shift, _ = dims_of(on_row, c % CORES, step)
            if on_row:
                pairs.append((r * ncol + c, (r ^ (mask << shift)) * ncol + c))
            else:
                pairs.append((r * ncol + c, r * ncol + (c ^ (mask << shift))))
    return pairs


def xor_bcast(value, root, on_row, rider, rider_root):
    nrow = lax.axis_size("row")
    ncol = lax.axis_size("col")
    me = lax.axis_index("row") if on_row else lax.axis_index("col")
    parity = lax.axis_index("col") % CORES
    axes = ("row", "col")

    def digit(step, relative):
        if on_row:
            shift = jnp.where(parity == 0, 2 if step == 0 else 0, 0 if step == 0 else 2)
        else:
            shift = dims_of(False, 0, step)[0]
        return (relative >> shift) & (RING - 1 if on_row or step == 1 else CORES - 1)

    def send(main, extra, step, mask):
        pairs = digit_pairs(nrow, ncol, on_row, step, mask)
        flat = main.reshape(main.shape[0], -1, main.shape[-1])
        both = jnp.concatenate([flat, extra.reshape(extra.shape[0], -1, extra.shape[-1])], axis=1)
        got = lax.ppermute(both, axes, pairs)
        return got[:, : flat.shape[1]].reshape(main.shape), got[:, flat.shape[1] :].reshape(extra.shape)

    def ride(step, gots):
        return pick(digit(step, me ^ rider_root), [rider] + gots)

    relative = me ^ root
    sizes = [dims_of(on_row, 0, step)[1] for step in range(2)]
    shape = value.shape
    buf = value.reshape(shape[0], sizes[0], sizes[1], -1, shape[-1])
    for step in range(2):
        groups = [buf[:, m] for m in range(sizes[step])]
        if on_row:
            got = [
                lax.ppermute(groups[m], axes, digit_pairs(nrow, ncol, on_row, step, m))
                for m in range(1, sizes[step])
            ]
        else:
            pairs = [send(groups[m], rider, step, m) for m in range(1, sizes[step])]
            got = [g for g, _ in pairs]
            rider = ride(step, [r for _, r in pairs])
        buf = pick(digit(step, relative), [groups[0]] + got)
    for step in reversed(range(2)):
        if on_row:
            pairs = [send(buf, rider, step, m) for m in range(1, sizes[step])]
            got = [buf] + [g for g, _ in pairs]
            rider = ride(step, [r for _, r in pairs])
        else:
            got = [buf] + [
                lax.ppermute(buf, axes, digit_pairs(nrow, ncol, on_row, step, m))
                for m in range(1, sizes[step])
            ]
        d = digit(step, relative)
        buf = jnp.stack(
            [pick(d, [got[dd ^ t] for dd in range(sizes[step])]) for t in range(sizes[step])], axis=1
        )
    return buf.reshape(shape), rider


def all_bcast(value, root):
    nrow = lax.axis_size("row")
    ncol = lax.axis_size("col")
    n = nrow * ncol
    relative = (lax.axis_index("row") * ncol + lax.axis_index("col")) ^ root
    shift = 0
    for size in (CORES, RING, RING, RING):
        mask = size - 1
        got = [value] + [
            lax.ppermute(value, ("row", "col"), [(d, d ^ (m << shift)) for d in range(n)])
            for m in range(1, size)
        ]
        value = pick((relative >> shift) & mask, got)
        shift += mask.bit_length()
    return value


def lower_local(column, inverse, rows_ok):
    lower = jnp.einsum("iab,bc->iac", column, inverse, preferred_element_type=jnp.float32)
    return jnp.where(rows_ok[:, None, None], lower, 0.0).astype(jnp.bfloat16)


def eliminate(matrix, lower, upper, pivot, rows_ok, cols_ok, local, front_cols):
    product = jnp.einsum("iab,jbc->ijac", lower, upper, preferred_element_type=jnp.float32)
    update = rows_ok[:, None] & cols_ok[None, :] & (local > 0)
    changed = (matrix.astype(jnp.float32) - product).astype(jnp.bfloat16)
    result = jnp.where(update[:, :, None, None], changed, matrix)
    place = rows_ok[:, None] & (front_cols == pivot)[None, :]
    return jnp.where(place[:, :, None, None], lower[:, None], result)


def update_kernel(codes, front_ref, l1_ref, l2_ref, u1_ref, u2_ref, out_ref):
    i = pl.program_id(0)
    lower1 = l1_ref[0]
    lower2 = l2_ref[0]
    for j in range(front_ref.shape[1]):
        code = codes[i, j]
        block = front_ref[0, j]
        block = jnp.where((code & 1) != 0, block, jnp.zeros_like(block))
        product = jnp.dot(lower1, u1_ref[j], preferred_element_type=jnp.float32)
        changed = (block.astype(jnp.float32) - product).astype(jnp.bfloat16)
        block = jnp.where((code & 2) != 0, changed, block)
        block = jnp.where((code & 4) != 0, lower1, block)
        product = jnp.dot(lower2, u2_ref[j], preferred_element_type=jnp.float32)
        changed = (block.astype(jnp.float32) - product).astype(jnp.bfloat16)
        block = jnp.where((code & 8) != 0, changed, block)
        block = jnp.where((code & 16) != 0, lower2, block)
        out_ref[0, j] = block


def both_updates(front, codes, lower1, lower2, upper1, upper2):
    rows, cols, bs, _ = front.shape
    row_block = pl.BlockSpec((1, cols, bs, bs), lambda i, c: (i, 0, 0, 0))
    lower_block = pl.BlockSpec((1, bs, bs), lambda i, c: (i, 0, 0))
    upper_block = pl.BlockSpec((cols, bs, bs), lambda i, c: (0, 0, 0))
    return pl.pallas_call(
        update_kernel,
        grid_spec=pltpu.PrefetchScalarGridSpec(
            num_scalar_prefetch=1,
            grid=(rows,),
            in_specs=[row_block, lower_block, lower_block, upper_block, upper_block],
            out_specs=row_block,
        ),
        out_shape=jax.ShapeDtypeStruct(front.shape, front.dtype),
        compiler_params=pltpu.CompilerParams(dimension_semantics=("arbitrary",)),
    )(codes, front, lower1, lower2, upper1, upper2)


def masked(blocks, keep):
    shape = keep.shape + (1,) * (blocks.ndim - keep.ndim)
    return jnp.where(keep.reshape(shape) > 0, blocks, jnp.zeros_like(blocks))


def body(front, pattern, pivots, pivot_inv):
    rows_dev = front.shape[0]
    cols_dev = front.shape[1]
    nrow = lax.axis_size("row")
    ncol = lax.axis_size("col")
    row_index = lax.axis_index("row")
    col_index = lax.axis_index("col")
    grid = pattern.reshape(rows_dev, nrow, cols_dev, ncol)
    local = lax.dynamic_index_in_dim(grid, row_index, 1, keepdims=False)
    local = lax.dynamic_index_in_dim(local, col_index, 2, keepdims=False)
    front_rows = jnp.arange(rows_dev, dtype=jnp.int32) * nrow + row_index
    front_cols = jnp.arange(cols_dev, dtype=jnp.int32) * ncol + col_index
    first = pivots[0]
    second = pivots[1]
    rows_first = front_rows != first
    cols_first = front_cols != first
    rows_second = rows_first & (front_rows != second)
    cols_second = cols_first & (front_cols != second)

    a1, b1 = first // nrow, first // ncol
    a2, b2 = second // nrow, second // ncol
    r1, c1 = first % nrow, first % ncol
    r2, c2 = second % nrow, second % ncol

    def local_row(a):
        return masked(
            lax.dynamic_index_in_dim(front, a, 0, keepdims=False),
            lax.dynamic_index_in_dim(local, a, 0, keepdims=False),
        )

    def local_col(b):
        return masked(
            lax.dynamic_index_in_dim(front, b, 1, keepdims=False),
            lax.dynamic_index_in_dim(local, b, 1, keepdims=False),
        )

    lower_first = lower_local(local_col(b1), pivot_inv[0], rows_first)
    cross = jnp.stack([masked(front[a1, b2], local[a1, b2]), masked(front[a2, b1], local[a2, b1])])
    cols_sent, cross = xor_bcast(
        jnp.stack([lower_first, local_col(b2)]), jnp.stack([c1, c2]), False, cross, jnp.stack([c2, c1])
    )
    rows_sent, cross = xor_bcast(
        jnp.stack([local_row(a1), local_row(a2)]), jnp.stack([r1, r2]), True, cross, jnp.stack([r1, r2])
    )
    lower_first, second_col = cols_sent[0], cols_sent[1]
    upper_first, second_row = rows_sent[0], rows_sent[1]
    first_at_second, second_at_first = cross[0], cross[1]

    second_ok = (second != first)[None]
    lower_first_at_second = lower_local(second_at_first[None], pivot_inv[0], second_ok)
    row_after = eliminate(
        second_row[None],
        lower_first_at_second,
        upper_first,
        first,
        second_ok,
        cols_first,
        pattern[second][front_cols][None],
        front_cols,
    )
    upper_second = row_after[0]
    col_after = eliminate(
        second_col[:, None],
        lower_first,
        first_at_second[None],
        first,
        rows_first,
        second_ok,
        pattern[front_rows, second][:, None],
        second[None],
    )
    lower_second = lower_local(col_after[:, 0], pivot_inv[1], rows_second)

    keep = local > 0
    update_first = rows_first[:, None] & cols_first[None, :] & keep
    place_first = rows_first[:, None] & (front_cols == first)[None, :]
    update_second = rows_second[:, None] & cols_second[None, :] & keep
    place_second = rows_second[:, None] & (front_cols == second)[None, :]
    codes = (
        keep.astype(jnp.int32)
        + 2 * update_first.astype(jnp.int32)
        + 4 * place_first.astype(jnp.int32)
        + 8 * update_second.astype(jnp.int32)
        + 16 * place_second.astype(jnp.int32)
    )
    return both_updates(front, codes, lower_first, lower_second, upper_first, upper_second)


def solution(mesh):
    placed = (P("row", "col", None, None), P(), P(), P())
    return jax.shard_map(
        body, mesh=mesh, in_specs=placed, out_specs=P("row", "col", None, None), check_vma=False
    )
```

```python
import jax
import jax.numpy as jnp
from jax import lax
from jax.experimental import pallas as pl
from jax.experimental.pallas import tpu as pltpu
from jax.sharding import PartitionSpec as P

RING = 4
CORES = 2


def per_part(cond, a, b):
    return jnp.where(cond.reshape((-1,) + (1,) * (a.ndim - 1)), a, b)


def pick(index, options):
    out = options[-1]
    for k in range(len(options) - 2, -1, -1):
        out = per_part(index == k, options[k], out)
    return out


def ring_bcast(value, axis, plus, minus, me, root):
    half = value.shape[0] // 2
    first, second = value[:half], value[half:]
    got_plus = lax.ppermute(first, axis, plus)
    got_minus = lax.ppermute(second, axis, minus)
    dist = (me - root) % RING
    at_root = dist == 0
    send_plus = jnp.where(at_root, second, got_plus)
    send_minus = jnp.where(at_root, first, got_minus)
    got_plus2 = lax.ppermute(send_plus, axis, plus)
    got_minus2 = lax.ppermute(send_minus, axis, minus)
    out_first = pick(dist, [first, got_plus, got_plus2, got_minus2])
    out_second = pick(dist, [second, got_plus2, got_minus2, got_minus])
    return jnp.concatenate([out_first, out_second], axis=0)


def row_pairs(step_z, step_x):
    return [
        (RING * z + x, RING * ((z + step_z) % RING) + (x + step_x) % RING)
        for z in range(RING)
        for x in range(RING)
    ]


def row_bcast(value, root):
    me = lax.axis_index("row")
    mz, mx = me // RING, me % RING
    rz, rx = root // RING, root % RING
    xp, xm = row_pairs(0, 1), row_pairs(0, RING - 1)
    zp, zm = row_pairs(1, 0), row_pairs(RING - 1, 0)
    half = value.shape[0] // 2
    along_x = value[:half]
    along_z = value[half:]
    along_x = ring_bcast(along_x, "row", xp, xm, mx, rx)
    along_z = ring_bcast(along_z, "row", zp, zm, mz, rz)
    along_x = ring_bcast(along_x, "row", zp, zm, mz, rz)
    along_z = ring_bcast(along_z, "row", xp, xm, mx, rx)
    return jnp.concatenate([along_x, along_z], axis=0)


def col_bcast(value, root):
    me = lax.axis_index("col")
    my, mk = me // CORES, me % CORES
    ry = root // CORES
    swap = [(CORES * y + k, CORES * y + 1 - k) for y in range(RING) for k in range(CORES)]
    hop = [(CORES * y, CORES * ((y + 1) % RING)) for y in range(RING)] + [
        (CORES * y + 1, CORES * ((y - 1) % RING) + 1) for y in range(RING)
    ]
    got_swap = lax.ppermute(value, "col", swap)
    on_root_chip = jnp.where(me == root, value, got_swap)
    got_hop = lax.ppermute(on_root_chip, "col", hop)
    dist = (my - ry) % RING
    near = jnp.where(dist == 0, on_root_chip, got_hop)
    got_swap2 = lax.ppermute(near, "col", swap)
    half = value.shape[0] // 2
    fwd = jnp.where(mk == 0, near[:half], near[half:])
    got_fwd = lax.ppermute(fwd, "col", hop)
    got_swap3 = lax.ppermute(got_fwd, "col", swap)
    far = jnp.where(
        mk == 0,
        jnp.concatenate([got_fwd, got_swap3], axis=0),
        jnp.concatenate([got_swap3, got_fwd], axis=0),
    )
    own_hop = (dist == 1) & (mk == 0) | (dist == 3) & (mk == 1)
    other_hop = (dist == 1) & (mk == 1) | (dist == 3) & (mk == 0)
    out = jnp.where(own_hop, got_hop, far)
    out = jnp.where(other_hop, got_swap2, out)
    return jnp.where(dist == 0, on_root_chip, out)


ROW_ORDERS = ((3, 2, 1, 0), (1, 0, 3, 2))
COL_ORDER = (0, 1, 2)


def xor_pairs(nrow, ncol, on_row, step):
    pairs = []
    for r in range(nrow):
        for c in range(ncol):
            if on_row:
                pairs.append((r * ncol + c, (r ^ (1 << ROW_ORDERS[c % CORES][step])) * ncol + c))
            else:
                pairs.append((r * ncol + c, r * ncol + (c ^ (1 << COL_ORDER[step]))))
    return pairs


def dims_of(on_row, parity, step):
    if on_row:
        z_first = (parity == 0) == (step == 0)
        return (2 if z_first else 0), RING
    return ((0, CORES), (1, RING))[step]


def digit_pairs(nrow, ncol, on_row, step, mask):
    pairs = []
    for r in range(nrow):
        for c in range(ncol):
            shift, _ = dims_of(on_row, c % CORES, step)
            if on_row:
                pairs.append((r * ncol + c, (r ^ (mask << shift)) * ncol + c))
            else:
                pairs.append((r * ncol + c, r * ncol + (c ^ (mask << shift))))
    return pairs


def xor_bcast(value, root, on_row, hold=None):
    nrow = lax.axis_size("row")
    ncol = lax.axis_size("col")
    me = lax.axis_index("row") if on_row else lax.axis_index("col")
    parity = lax.axis_index("col") % CORES
    relative = me ^ root
    axes = ("row", "col")

    def digit(step):
        if on_row:
            shift = jnp.where(parity == 0, 2 if step == 0 else 0, 0 if step == 0 else 2)
        else:
            shift = dims_of(False, 0, step)[0]
        return (relative >> shift) & (RING - 1 if on_row or step == 1 else CORES - 1)

    sizes = [dims_of(on_row, 0, step)[1] for step in range(2)]
    shape = value.shape
    buf = value.reshape(shape[0], sizes[0], sizes[1], -1, shape[-1])
    for step in range(2):
        d = digit(step)
        groups = [buf[:, m] for m in range(sizes[step])]
        got = [None] + [
            lax.ppermute(groups[m], axes, digit_pairs(nrow, ncol, on_row, step, m))
            for m in range(1, sizes[step])
        ]
        buf = pick(d, [groups[0]] + got[1:])
    if hold is not None:
        buf, hold = lax.optimization_barrier((buf, hold))
    for step in reversed(range(2)):
        d = digit(step)
        got = [buf] + [
            lax.ppermute(buf, axes, digit_pairs(nrow, ncol, on_row, step, m))
            for m in range(1, sizes[step])
        ]
        buf = jnp.stack(
            [pick(d, [got[dd ^ t] for dd in range(sizes[step])]) for t in range(sizes[step])], axis=1
        )
    return buf.reshape(shape), hold


def all_bcast(value, root):
    nrow = lax.axis_size("row")
    ncol = lax.axis_size("col")
    n = nrow * ncol
    relative = (lax.axis_index("row") * ncol + lax.axis_index("col")) ^ root
    for b in range(n.bit_length() - 1):
        got = lax.ppermute(value, ("row", "col"), [(d, d ^ (1 << b)) for d in range(n)])
        value = per_part((relative >> b) == 1, got, value)
    return value


def lower_local(column, inverse, rows_ok):
    lower = jnp.einsum("iab,bc->iac", column, inverse, preferred_element_type=jnp.float32)
    return jnp.where(rows_ok[:, None, None], lower, 0.0).astype(jnp.bfloat16)


def eliminate(matrix, lower, upper, pivot, rows_ok, cols_ok, local, front_cols):
    product = jnp.einsum("iab,jbc->ijac", lower, upper, preferred_element_type=jnp.float32)
    update = rows_ok[:, None] & cols_ok[None, :] & (local > 0)
    changed = (matrix.astype(jnp.float32) - product).astype(jnp.bfloat16)
    result = jnp.where(update[:, :, None, None], changed, matrix)
    place = rows_ok[:, None] & (front_cols == pivot)[None, :]
    return jnp.where(place[:, :, None, None], lower[:, None], result)


def update_kernel(codes, front_ref, l1_ref, l2_ref, u1_ref, u2_ref, out_ref):
    i = pl.program_id(0)
    lower1 = l1_ref[0]
    lower2 = l2_ref[0]
    for j in range(front_ref.shape[1]):
        code = codes[i, j]
        block = front_ref[0, j]
        block = jnp.where((code & 1) != 0, block, jnp.zeros_like(block))
        product = jnp.dot(lower1, u1_ref[j], preferred_element_type=jnp.float32)
        changed = (block.astype(jnp.float32) - product).astype(jnp.bfloat16)
        block = jnp.where((code & 2) != 0, changed, block)
        block = jnp.where((code & 4) != 0, lower1, block)
        product = jnp.dot(lower2, u2_ref[j], preferred_element_type=jnp.float32)
        changed = (block.astype(jnp.float32) - product).astype(jnp.bfloat16)
        block = jnp.where((code & 8) != 0, changed, block)
        block = jnp.where((code & 16) != 0, lower2, block)
        out_ref[0, j] = block


def both_updates(front, codes, lower1, lower2, upper1, upper2):
    rows, cols, bs, _ = front.shape
    row_block = pl.BlockSpec((1, cols, bs, bs), lambda i, c: (i, 0, 0, 0))
    lower_block = pl.BlockSpec((1, bs, bs), lambda i, c: (i, 0, 0))
    upper_block = pl.BlockSpec((cols, bs, bs), lambda i, c: (0, 0, 0))
    return pl.pallas_call(
        update_kernel,
        grid_spec=pltpu.PrefetchScalarGridSpec(
            num_scalar_prefetch=1,
            grid=(rows,),
            in_specs=[row_block, lower_block, lower_block, upper_block, upper_block],
            out_specs=row_block,
        ),
        out_shape=jax.ShapeDtypeStruct(front.shape, front.dtype),
        compiler_params=pltpu.CompilerParams(dimension_semantics=("arbitrary",)),
    )(codes, front, lower1, lower2, upper1, upper2)


def masked(blocks, keep):
    shape = keep.shape + (1,) * (blocks.ndim - keep.ndim)
    return jnp.where(keep.reshape(shape) > 0, blocks, jnp.zeros_like(blocks))


def body(front, pattern, pivots, pivot_inv):
    rows_dev = front.shape[0]
    cols_dev = front.shape[1]
    nrow = lax.axis_size("row")
    ncol = lax.axis_size("col")
    row_index = lax.axis_index("row")
    col_index = lax.axis_index("col")
    grid = pattern.reshape(rows_dev, nrow, cols_dev, ncol)
    local = lax.dynamic_index_in_dim(grid, row_index, 1, keepdims=False)
    local = lax.dynamic_index_in_dim(local, col_index, 2, keepdims=False)
    front_rows = jnp.arange(rows_dev, dtype=jnp.int32) * nrow + row_index
    front_cols = jnp.arange(cols_dev, dtype=jnp.int32) * ncol + col_index
    first = pivots[0]
    second = pivots[1]
    rows_first = front_rows != first
    cols_first = front_cols != first
    rows_second = rows_first & (front_rows != second)
    cols_second = cols_first & (front_cols != second)

    a1, b1 = first // nrow, first // ncol
    a2, b2 = second // nrow, second // ncol
    r1, c1 = first % nrow, first % ncol
    r2, c2 = second % nrow, second % ncol

    def local_row(a):
        return masked(
            lax.dynamic_index_in_dim(front, a, 0, keepdims=False),
            lax.dynamic_index_in_dim(local, a, 0, keepdims=False),
        )

    def local_col(b):
        return masked(
            lax.dynamic_index_in_dim(front, b, 1, keepdims=False),
            lax.dynamic_index_in_dim(local, b, 1, keepdims=False),
        )

    lower_first = lower_local(local_col(b1), pivot_inv[0], rows_first)
    cross = all_bcast(
        jnp.stack([masked(front[a1, b2], local[a1, b2]), masked(front[a2, b1], local[a2, b1])]),
        jnp.stack([r1 * ncol + c2, r2 * ncol + c1]),
    )
    cols_sent, _ = xor_bcast(jnp.stack([lower_first, local_col(b2)]), jnp.stack([c1, c2]), False)
    rows_sent, cross = xor_bcast(
        jnp.stack([local_row(a1), local_row(a2)]), jnp.stack([r1, r2]), True, cross
    )
    lower_first, second_col = cols_sent[0], cols_sent[1]
    upper_first, second_row = rows_sent[0], rows_sent[1]
    first_at_second, second_at_first = cross[0], cross[1]

    second_ok = (second != first)[None]
    lower_first_at_second = lower_local(second_at_first[None], pivot_inv[0], second_ok)
    row_after = eliminate(
        second_row[None],
        lower_first_at_second,
        upper_first,
        first,
        second_ok,
        cols_first,
        pattern[second][front_cols][None],
        front_cols,
    )
    upper_second = row_after[0]
    col_after = eliminate(
        second_col[:, None],
        lower_first,
        first_at_second[None],
        first,
        rows_first,
        second_ok,
        pattern[front_rows, second][:, None],
        second[None],
    )
    lower_second = lower_local(col_after[:, 0], pivot_inv[1], rows_second)

    keep = local > 0
    update_first = rows_first[:, None] & cols_first[None, :] & keep
    place_first = rows_first[:, None] & (front_cols == first)[None, :]
    update_second = rows_second[:, None] & cols_second[None, :] & keep
    place_second = rows_second[:, None] & (front_cols == second)[None, :]
    codes = (
        keep.astype(jnp.int32)
        + 2 * update_first.astype(jnp.int32)
        + 4 * place_first.astype(jnp.int32)
        + 8 * update_second.astype(jnp.int32)
        + 16 * place_second.astype(jnp.int32)
    )
    return both_updates(front, codes, lower_first, lower_second, upper_first, upper_second)


def solution(mesh):
    placed = (P("row", "col", None, None), P(), P(), P())
    return jax.shard_map(
        body, mesh=mesh, in_specs=placed, out_specs=P("row", "col", None, None), check_vma=False
    )
```

```python
import jax
import jax.numpy as jnp
from jax import lax
from jax.experimental import pallas as pl
from jax.experimental.pallas import tpu as pltpu
from jax.sharding import PartitionSpec as P

RING = 4
CORES = 2


def per_part(cond, a, b):
    return jnp.where(cond.reshape((-1,) + (1,) * (a.ndim - 1)), a, b)


def pick(index, options):
    out = options[-1]
    for k in range(len(options) - 2, -1, -1):
        out = per_part(index == k, options[k], out)
    return out


def ring_bcast(value, axis, plus, minus, me, root):
    half = value.shape[0] // 2
    first, second = value[:half], value[half:]
    got_plus = lax.ppermute(first, axis, plus)
    got_minus = lax.ppermute(second, axis, minus)
    dist = (me - root) % RING
    at_root = dist == 0
    send_plus = jnp.where(at_root, second, got_plus)
    send_minus = jnp.where(at_root, first, got_minus)
    got_plus2 = lax.ppermute(send_plus, axis, plus)
    got_minus2 = lax.ppermute(send_minus, axis, minus)
    out_first = pick(dist, [first, got_plus, got_plus2, got_minus2])
    out_second = pick(dist, [second, got_plus2, got_minus2, got_minus])
    return jnp.concatenate([out_first, out_second], axis=0)


def row_pairs(step_z, step_x):
    return [
        (RING * z + x, RING * ((z + step_z) % RING) + (x + step_x) % RING)
        for z in range(RING)
        for x in range(RING)
    ]


def row_bcast(value, root):
    me = lax.axis_index("row")
    mz, mx = me // RING, me % RING
    rz, rx = root // RING, root % RING
    xp, xm = row_pairs(0, 1), row_pairs(0, RING - 1)
    zp, zm = row_pairs(1, 0), row_pairs(RING - 1, 0)
    half = value.shape[0] // 2
    along_x = value[:half]
    along_z = value[half:]
    along_x = ring_bcast(along_x, "row", xp, xm, mx, rx)
    along_z = ring_bcast(along_z, "row", zp, zm, mz, rz)
    along_x = ring_bcast(along_x, "row", zp, zm, mz, rz)
    along_z = ring_bcast(along_z, "row", xp, xm, mx, rx)
    return jnp.concatenate([along_x, along_z], axis=0)


def col_bcast(value, root):
    me = lax.axis_index("col")
    my, mk = me // CORES, me % CORES
    ry = root // CORES
    swap = [(CORES * y + k, CORES * y + 1 - k) for y in range(RING) for k in range(CORES)]
    hop = [(CORES * y, CORES * ((y + 1) % RING)) for y in range(RING)] + [
        (CORES * y + 1, CORES * ((y - 1) % RING) + 1) for y in range(RING)
    ]
    got_swap = lax.ppermute(value, "col", swap)
    on_root_chip = jnp.where(me == root, value, got_swap)
    got_hop = lax.ppermute(on_root_chip, "col", hop)
    dist = (my - ry) % RING
    near = jnp.where(dist == 0, on_root_chip, got_hop)
    got_swap2 = lax.ppermute(near, "col", swap)
    half = value.shape[0] // 2
    fwd = jnp.where(mk == 0, near[:half], near[half:])
    got_fwd = lax.ppermute(fwd, "col", hop)
    got_swap3 = lax.ppermute(got_fwd, "col", swap)
    far = jnp.where(
        mk == 0,
        jnp.concatenate([got_fwd, got_swap3], axis=0),
        jnp.concatenate([got_swap3, got_fwd], axis=0),
    )
    own_hop = (dist == 1) & (mk == 0) | (dist == 3) & (mk == 1)
    other_hop = (dist == 1) & (mk == 1) | (dist == 3) & (mk == 0)
    out = jnp.where(own_hop, got_hop, far)
    out = jnp.where(other_hop, got_swap2, out)
    return jnp.where(dist == 0, on_root_chip, out)


ROW_ORDERS = ((3, 2, 1, 0), (1, 0, 3, 2))
COL_ORDER = (0, 1, 2)


def xor_pairs(nrow, ncol, on_row, step):
    pairs = []
    for r in range(nrow):
        for c in range(ncol):
            if on_row:
                pairs.append((r * ncol + c, (r ^ (1 << ROW_ORDERS[c % CORES][step])) * ncol + c))
            else:
                pairs.append((r * ncol + c, r * ncol + (c ^ (1 << COL_ORDER[step]))))
    return pairs


def dims_of(on_row, parity, step):
    if on_row:
        z_first = (parity == 0) == (step == 0)
        return (2 if z_first else 0), RING
    return ((0, CORES), (1, RING))[step]


def digit_pairs(nrow, ncol, on_row, step, mask):
    pairs = []
    for r in range(nrow):
        for c in range(ncol):
            shift, _ = dims_of(on_row, c % CORES, step)
            if on_row:
                pairs.append((r * ncol + c, (r ^ (mask << shift)) * ncol + c))
            else:
                pairs.append((r * ncol + c, r * ncol + (c ^ (mask << shift))))
    return pairs


def xor_bcast(value, root, on_row):
    nrow = lax.axis_size("row")
    ncol = lax.axis_size("col")
    me = lax.axis_index("row") if on_row else lax.axis_index("col")
    parity = lax.axis_index("col") % CORES
    relative = me ^ root
    axes = ("row", "col")

    def digit(step):
        if on_row:
            shift = jnp.where(parity == 0, 2 if step == 0 else 0, 0 if step == 0 else 2)
        else:
            shift = dims_of(False, 0, step)[0]
        return (relative >> shift) & (RING - 1 if on_row or step == 1 else CORES - 1)

    sizes = [dims_of(on_row, 0, step)[1] for step in range(2)]
    shape = value.shape
    buf = value.reshape(shape[0], sizes[0], sizes[1], -1, shape[-1])
    for step in range(2):
        d = digit(step)
        groups = [buf[:, m] for m in range(sizes[step])]
        got = [None] + [
            lax.ppermute(groups[m], axes, digit_pairs(nrow, ncol, on_row, step, m))
            for m in range(1, sizes[step])
        ]
        buf = pick(d, [groups[0]] + got[1:])
    for step in reversed(range(2)):
        d = digit(step)
        got = [buf] + [
            lax.ppermute(buf, axes, digit_pairs(nrow, ncol, on_row, step, m))
            for m in range(1, sizes[step])
        ]
        buf = jnp.stack(
            [pick(d, [got[dd ^ t] for dd in range(sizes[step])]) for t in range(sizes[step])], axis=1
        )
    return buf.reshape(shape)


def all_bcast(value, root):
    nrow = lax.axis_size("row")
    ncol = lax.axis_size("col")
    n = nrow * ncol
    relative = (lax.axis_index("row") * ncol + lax.axis_index("col")) ^ root
    for b in range(n.bit_length() - 1):
        got = lax.ppermute(value, ("row", "col"), [(d, d ^ (1 << b)) for d in range(n)])
        value = per_part((relative >> b) == 1, got, value)
    return value


def lower_local(column, inverse, rows_ok):
    lower = jnp.einsum("iab,bc->iac", column, inverse, preferred_element_type=jnp.float32)
    return jnp.where(rows_ok[:, None, None], lower, 0.0).astype(jnp.bfloat16)


def eliminate(matrix, lower, upper, pivot, rows_ok, cols_ok, local, front_cols):
    product = jnp.einsum("iab,jbc->ijac", lower, upper, preferred_element_type=jnp.float32)
    update = rows_ok[:, None] & cols_ok[None, :] & (local > 0)
    changed = (matrix.astype(jnp.float32) - product).astype(jnp.bfloat16)
    result = jnp.where(update[:, :, None, None], changed, matrix)
    place = rows_ok[:, None] & (front_cols == pivot)[None, :]
    return jnp.where(place[:, :, None, None], lower[:, None], result)


def update_kernel(codes, front_ref, l1_ref, l2_ref, u1_ref, u2_ref, out_ref):
    i = pl.program_id(0)
    lower1 = l1_ref[0]
    lower2 = l2_ref[0]
    for j in range(front_ref.shape[1]):
        code = codes[i, j]
        block = front_ref[0, j]
        block = jnp.where((code & 1) != 0, block, jnp.zeros_like(block))
        product = jnp.dot(lower1, u1_ref[j], preferred_element_type=jnp.float32)
        changed = (block.astype(jnp.float32) - product).astype(jnp.bfloat16)
        block = jnp.where((code & 2) != 0, changed, block)
        block = jnp.where((code & 4) != 0, lower1, block)
        product = jnp.dot(lower2, u2_ref[j], preferred_element_type=jnp.float32)
        changed = (block.astype(jnp.float32) - product).astype(jnp.bfloat16)
        block = jnp.where((code & 8) != 0, changed, block)
        block = jnp.where((code & 16) != 0, lower2, block)
        out_ref[0, j] = block


def both_updates(front, codes, lower1, lower2, upper1, upper2):
    rows, cols, bs, _ = front.shape
    row_block = pl.BlockSpec((1, cols, bs, bs), lambda i, c: (i, 0, 0, 0))
    lower_block = pl.BlockSpec((1, bs, bs), lambda i, c: (i, 0, 0))
    upper_block = pl.BlockSpec((cols, bs, bs), lambda i, c: (0, 0, 0))
    return pl.pallas_call(
        update_kernel,
        grid_spec=pltpu.PrefetchScalarGridSpec(
            num_scalar_prefetch=1,
            grid=(rows,),
            in_specs=[row_block, lower_block, lower_block, upper_block, upper_block],
            out_specs=row_block,
        ),
        out_shape=jax.ShapeDtypeStruct(front.shape, front.dtype),
        compiler_params=pltpu.CompilerParams(dimension_semantics=("arbitrary",)),
    )(codes, front, lower1, lower2, upper1, upper2)


def masked(blocks, keep):
    shape = keep.shape + (1,) * (blocks.ndim - keep.ndim)
    return jnp.where(keep.reshape(shape) > 0, blocks, jnp.zeros_like(blocks))


def body(front, pattern, pivots, pivot_inv):
    rows_dev = front.shape[0]
    cols_dev = front.shape[1]
    nrow = lax.axis_size("row")
    ncol = lax.axis_size("col")
    row_index = lax.axis_index("row")
    col_index = lax.axis_index("col")
    grid = pattern.reshape(rows_dev, nrow, cols_dev, ncol)
    local = lax.dynamic_index_in_dim(grid, row_index, 1, keepdims=False)
    local = lax.dynamic_index_in_dim(local, col_index, 2, keepdims=False)
    front_rows = jnp.arange(rows_dev, dtype=jnp.int32) * nrow + row_index
    front_cols = jnp.arange(cols_dev, dtype=jnp.int32) * ncol + col_index
    first = pivots[0]
    second = pivots[1]
    rows_first = front_rows != first
    cols_first = front_cols != first
    rows_second = rows_first & (front_rows != second)
    cols_second = cols_first & (front_cols != second)

    a1, b1 = first // nrow, first // ncol
    a2, b2 = second // nrow, second // ncol
    r1, c1 = first % nrow, first % ncol
    r2, c2 = second % nrow, second % ncol

    def local_row(a):
        return masked(
            lax.dynamic_index_in_dim(front, a, 0, keepdims=False),
            lax.dynamic_index_in_dim(local, a, 0, keepdims=False),
        )

    def local_col(b):
        return masked(
            lax.dynamic_index_in_dim(front, b, 1, keepdims=False),
            lax.dynamic_index_in_dim(local, b, 1, keepdims=False),
        )

    cols_sent = xor_bcast(jnp.stack([local_col(b1), local_col(b2)]), jnp.stack([c1, c2]), False)
    rows_sent = xor_bcast(jnp.stack([local_row(a1), local_row(a2)]), jnp.stack([r1, r2]), True)
    lower_first = lower_local(cols_sent[0], pivot_inv[0], rows_first)
    second_col = cols_sent[1]
    upper_first, second_row = rows_sent[0], rows_sent[1]

    cross = all_bcast(
        jnp.stack([masked(front[a1, b2], local[a1, b2]), masked(front[a2, b1], local[a2, b1])]),
        jnp.stack([r1 * ncol + c2, r2 * ncol + c1]),
    )
    first_at_second, second_at_first = cross[0], cross[1]

    second_ok = (second != first)[None]
    lower_first_at_second = lower_local(second_at_first[None], pivot_inv[0], second_ok)
    row_after = eliminate(
        second_row[None],
        lower_first_at_second,
        upper_first,
        first,
        second_ok,
        cols_first,
        pattern[second][front_cols][None],
        front_cols,
    )
    upper_second = row_after[0]
    col_after = eliminate(
        second_col[:, None],
        lower_first,
        first_at_second[None],
        first,
        rows_first,
        second_ok,
        pattern[front_rows, second][:, None],
        second[None],
    )
    lower_second = lower_local(col_after[:, 0], pivot_inv[1], rows_second)

    keep = local > 0
    update_first = rows_first[:, None] & cols_first[None, :] & keep
    place_first = rows_first[:, None] & (front_cols == first)[None, :]
    update_second = rows_second[:, None] & cols_second[None, :] & keep
    place_second = rows_second[:, None] & (front_cols == second)[None, :]
    codes = (
        keep.astype(jnp.int32)
        + 2 * update_first.astype(jnp.int32)
        + 4 * place_first.astype(jnp.int32)
        + 8 * update_second.astype(jnp.int32)
        + 16 * place_second.astype(jnp.int32)
    )
    return both_updates(front, codes, lower_first, lower_second, upper_first, upper_second)


def solution(mesh):
    placed = (P("row", "col", None, None), P(), P(), P())
    return jax.shard_map(
        body, mesh=mesh, in_specs=placed, out_specs=P("row", "col", None, None), check_vma=False
    )
```

```python
import jax
import jax.numpy as jnp
from jax import lax
from jax.experimental import pallas as pl
from jax.experimental.pallas import tpu as pltpu
from jax.sharding import PartitionSpec as P

RING = 4
CORES = 2


def per_part(cond, a, b):
    return jnp.where(cond.reshape((-1,) + (1,) * (a.ndim - 1)), a, b)


def pick(index, options):
    out = options[-1]
    for k in range(len(options) - 2, -1, -1):
        out = per_part(index == k, options[k], out)
    return out


def ring_bcast(value, axis, plus, minus, me, root):
    half = value.shape[0] // 2
    first, second = value[:half], value[half:]
    got_plus = lax.ppermute(first, axis, plus)
    got_minus = lax.ppermute(second, axis, minus)
    dist = (me - root) % RING
    at_root = dist == 0
    send_plus = jnp.where(at_root, second, got_plus)
    send_minus = jnp.where(at_root, first, got_minus)
    got_plus2 = lax.ppermute(send_plus, axis, plus)
    got_minus2 = lax.ppermute(send_minus, axis, minus)
    out_first = pick(dist, [first, got_plus, got_plus2, got_minus2])
    out_second = pick(dist, [second, got_plus2, got_minus2, got_minus])
    return jnp.concatenate([out_first, out_second], axis=0)


def row_pairs(step_z, step_x):
    return [
        (RING * z + x, RING * ((z + step_z) % RING) + (x + step_x) % RING)
        for z in range(RING)
        for x in range(RING)
    ]


def row_bcast(value, root):
    me = lax.axis_index("row")
    mz, mx = me // RING, me % RING
    rz, rx = root // RING, root % RING
    xp, xm = row_pairs(0, 1), row_pairs(0, RING - 1)
    zp, zm = row_pairs(1, 0), row_pairs(RING - 1, 0)
    half = value.shape[0] // 2
    along_x = value[:half]
    along_z = value[half:]
    along_x = ring_bcast(along_x, "row", xp, xm, mx, rx)
    along_z = ring_bcast(along_z, "row", zp, zm, mz, rz)
    along_x = ring_bcast(along_x, "row", zp, zm, mz, rz)
    along_z = ring_bcast(along_z, "row", xp, xm, mx, rx)
    return jnp.concatenate([along_x, along_z], axis=0)


def col_bcast(value, root):
    me = lax.axis_index("col")
    my, mk = me // CORES, me % CORES
    ry = root // CORES
    swap = [(CORES * y + k, CORES * y + 1 - k) for y in range(RING) for k in range(CORES)]
    hop = [(CORES * y, CORES * ((y + 1) % RING)) for y in range(RING)] + [
        (CORES * y + 1, CORES * ((y - 1) % RING) + 1) for y in range(RING)
    ]
    got_swap = lax.ppermute(value, "col", swap)
    on_root_chip = jnp.where(me == root, value, got_swap)
    got_hop = lax.ppermute(on_root_chip, "col", hop)
    dist = (my - ry) % RING
    near = jnp.where(dist == 0, on_root_chip, got_hop)
    got_swap2 = lax.ppermute(near, "col", swap)
    half = value.shape[0] // 2
    fwd = jnp.where(mk == 0, near[:half], near[half:])
    got_fwd = lax.ppermute(fwd, "col", hop)
    got_swap3 = lax.ppermute(got_fwd, "col", swap)
    far = jnp.where(
        mk == 0,
        jnp.concatenate([got_fwd, got_swap3], axis=0),
        jnp.concatenate([got_swap3, got_fwd], axis=0),
    )
    own_hop = (dist == 1) & (mk == 0) | (dist == 3) & (mk == 1)
    other_hop = (dist == 1) & (mk == 1) | (dist == 3) & (mk == 0)
    out = jnp.where(own_hop, got_hop, far)
    out = jnp.where(other_hop, got_swap2, out)
    return jnp.where(dist == 0, on_root_chip, out)


ROW_ORDERS = ((3, 2, 1, 0), (1, 0, 3, 2))
COL_ORDER = (0, 1, 2)


def xor_pairs(nrow, ncol, on_row, step):
    pairs = []
    for r in range(nrow):
        for c in range(ncol):
            if on_row:
                pairs.append((r * ncol + c, (r ^ (1 << ROW_ORDERS[c % CORES][step])) * ncol + c))
            else:
                pairs.append((r * ncol + c, r * ncol + (c ^ (1 << COL_ORDER[step]))))
    return pairs


def dims_of(on_row, parity, step):
    if on_row:
        z_first = (parity == 0) == (step == 0)
        return (2 if z_first else 0), RING
    return ((0, CORES), (1, RING))[step]


def digit_pairs(nrow, ncol, on_row, step, mask):
    pairs = []
    for r in range(nrow):
        for c in range(ncol):
            shift, _ = dims_of(on_row, c % CORES, step)
            if on_row:
                pairs.append((r * ncol + c, (r ^ (mask << shift)) * ncol + c))
            else:
                pairs.append((r * ncol + c, r * ncol + (c ^ (mask << shift))))
    return pairs


def xor_bcast(value, root, on_row):
    nrow = lax.axis_size("row")
    ncol = lax.axis_size("col")
    me = lax.axis_index("row") if on_row else lax.axis_index("col")
    parity = lax.axis_index("col") % CORES
    relative = me ^ root
    axes = ("row", "col")

    def digit(step):
        if on_row:
            shift = jnp.where(parity == 0, 2 if step == 0 else 0, 0 if step == 0 else 2)
        else:
            shift = dims_of(False, 0, step)[0]
        return (relative >> shift) & (RING - 1 if on_row or step == 1 else CORES - 1)

    sizes = [dims_of(on_row, 0, step)[1] for step in range(2)]
    shape = value.shape
    buf = value.reshape(shape[0], sizes[0], sizes[1], -1, shape[-1])
    for step in range(2):
        d = digit(step)
        groups = [buf[:, m] for m in range(sizes[step])]
        got = [None] + [
            lax.ppermute(groups[m], axes, digit_pairs(nrow, ncol, on_row, step, m))
            for m in range(1, sizes[step])
        ]
        buf = pick(d, [groups[0]] + got[1:])
    for step in reversed(range(2)):
        d = digit(step)
        got = [buf] + [
            lax.ppermute(buf, axes, digit_pairs(nrow, ncol, on_row, step, m))
            for m in range(1, sizes[step])
        ]
        buf = jnp.stack(
            [pick(d, [got[dd ^ t] for dd in range(sizes[step])]) for t in range(sizes[step])], axis=1
        )
    return buf.reshape(shape)


def all_bcast(value, root):
    nrow = lax.axis_size("row")
    ncol = lax.axis_size("col")
    n = nrow * ncol
    relative = (lax.axis_index("row") * ncol + lax.axis_index("col")) ^ root
    col_bits = (ncol.bit_length() - 1)
    bits = list(range(col_bits, n.bit_length() - 1)) + list(range(col_bits - 1, -1, -1))
    for b in bits:
        got = lax.ppermute(value, ("row", "col"), [(d, d ^ (1 << b)) for d in range(n)])
        value = per_part(((relative >> b) & 1) == 1, got, value)
    return value


def lower_local(column, inverse, rows_ok):
    lower = jnp.einsum("iab,bc->iac", column, inverse, preferred_element_type=jnp.float32)
    return jnp.where(rows_ok[:, None, None], lower, 0.0).astype(jnp.bfloat16)


def eliminate(matrix, lower, upper, pivot, rows_ok, cols_ok, local, front_cols):
    product = jnp.einsum("iab,jbc->ijac", lower, upper, preferred_element_type=jnp.float32)
    update = rows_ok[:, None] & cols_ok[None, :] & (local > 0)
    changed = (matrix.astype(jnp.float32) - product).astype(jnp.bfloat16)
    result = jnp.where(update[:, :, None, None], changed, matrix)
    place = rows_ok[:, None] & (front_cols == pivot)[None, :]
    return jnp.where(place[:, :, None, None], lower[:, None], result)


def update_kernel(codes, front_ref, l1_ref, l2_ref, u1_ref, u2_ref, out_ref):
    i = pl.program_id(0)
    lower1 = l1_ref[0]
    lower2 = l2_ref[0]
    for j in range(front_ref.shape[1]):
        code = codes[i, j]
        block = front_ref[0, j]
        block = jnp.where((code & 1) != 0, block, jnp.zeros_like(block))
        product = jnp.dot(lower1, u1_ref[j], preferred_element_type=jnp.float32)
        changed = (block.astype(jnp.float32) - product).astype(jnp.bfloat16)
        block = jnp.where((code & 2) != 0, changed, block)
        block = jnp.where((code & 4) != 0, lower1, block)
        product = jnp.dot(lower2, u2_ref[j], preferred_element_type=jnp.float32)
        changed = (block.astype(jnp.float32) - product).astype(jnp.bfloat16)
        block = jnp.where((code & 8) != 0, changed, block)
        block = jnp.where((code & 16) != 0, lower2, block)
        out_ref[0, j] = block


def both_updates(front, codes, lower1, lower2, upper1, upper2):
    rows, cols, bs, _ = front.shape
    row_block = pl.BlockSpec((1, cols, bs, bs), lambda i, c: (i, 0, 0, 0))
    lower_block = pl.BlockSpec((1, bs, bs), lambda i, c: (i, 0, 0))
    upper_block = pl.BlockSpec((cols, bs, bs), lambda i, c: (0, 0, 0))
    return pl.pallas_call(
        update_kernel,
        grid_spec=pltpu.PrefetchScalarGridSpec(
            num_scalar_prefetch=1,
            grid=(rows,),
            in_specs=[row_block, lower_block, lower_block, upper_block, upper_block],
            out_specs=row_block,
        ),
        out_shape=jax.ShapeDtypeStruct(front.shape, front.dtype),
        compiler_params=pltpu.CompilerParams(dimension_semantics=("arbitrary",)),
    )(codes, front, lower1, lower2, upper1, upper2)


def masked(blocks, keep):
    shape = keep.shape + (1,) * (blocks.ndim - keep.ndim)
    return jnp.where(keep.reshape(shape) > 0, blocks, jnp.zeros_like(blocks))


def body(front, pattern, pivots, pivot_inv):
    rows_dev = front.shape[0]
    cols_dev = front.shape[1]
    nrow = lax.axis_size("row")
    ncol = lax.axis_size("col")
    row_index = lax.axis_index("row")
    col_index = lax.axis_index("col")
    grid = pattern.reshape(rows_dev, nrow, cols_dev, ncol)
    local = lax.dynamic_index_in_dim(grid, row_index, 1, keepdims=False)
    local = lax.dynamic_index_in_dim(local, col_index, 2, keepdims=False)
    front_rows = jnp.arange(rows_dev, dtype=jnp.int32) * nrow + row_index
    front_cols = jnp.arange(cols_dev, dtype=jnp.int32) * ncol + col_index
    first = pivots[0]
    second = pivots[1]
    rows_first = front_rows != first
    cols_first = front_cols != first
    rows_second = rows_first & (front_rows != second)
    cols_second = cols_first & (front_cols != second)

    a1, b1 = first // nrow, first // ncol
    a2, b2 = second // nrow, second // ncol
    r1, c1 = first % nrow, first % ncol
    r2, c2 = second % nrow, second % ncol

    def local_row(a):
        return masked(
            lax.dynamic_index_in_dim(front, a, 0, keepdims=False),
            lax.dynamic_index_in_dim(local, a, 0, keepdims=False),
        )

    def local_col(b):
        return masked(
            lax.dynamic_index_in_dim(front, b, 1, keepdims=False),
            lax.dynamic_index_in_dim(local, b, 1, keepdims=False),
        )

    cols_sent = xor_bcast(jnp.stack([local_col(b1), local_col(b2)]), jnp.stack([c1, c2]), False)
    rows_sent = xor_bcast(jnp.stack([local_row(a1), local_row(a2)]), jnp.stack([r1, r2]), True)
    lower_first = lower_local(cols_sent[0], pivot_inv[0], rows_first)
    second_col = cols_sent[1]
    upper_first, second_row = rows_sent[0], rows_sent[1]

    cross = all_bcast(
        jnp.stack([masked(front[a1, b2], local[a1, b2]), masked(front[a2, b1], local[a2, b1])]),
        jnp.stack([r1 * ncol + c2, r2 * ncol + c1]),
    )
    first_at_second, second_at_first = cross[0], cross[1]

    second_ok = (second != first)[None]
    lower_first_at_second = lower_local(second_at_first[None], pivot_inv[0], second_ok)
    row_after = eliminate(
        second_row[None],
        lower_first_at_second,
        upper_first,
        first,
        second_ok,
        cols_first,
        pattern[second][front_cols][None],
        front_cols,
    )
    upper_second = row_after[0]
    col_after = eliminate(
        second_col[:, None],
        lower_first,
        first_at_second[None],
        first,
        rows_first,
        second_ok,
        pattern[front_rows, second][:, None],
        second[None],
    )
    lower_second = lower_local(col_after[:, 0], pivot_inv[1], rows_second)

    keep = local > 0
    update_first = rows_first[:, None] & cols_first[None, :] & keep
    place_first = rows_first[:, None] & (front_cols == first)[None, :]
    update_second = rows_second[:, None] & cols_second[None, :] & keep
    place_second = rows_second[:, None] & (front_cols == second)[None, :]
    codes = (
        keep.astype(jnp.int32)
        + 2 * update_first.astype(jnp.int32)
        + 4 * place_first.astype(jnp.int32)
        + 8 * update_second.astype(jnp.int32)
        + 16 * place_second.astype(jnp.int32)
    )
    return both_updates(front, codes, lower_first, lower_second, upper_first, upper_second)


def solution(mesh):
    placed = (P("row", "col", None, None), P(), P(), P())
    return jax.shard_map(
        body, mesh=mesh, in_specs=placed, out_specs=P("row", "col", None, None), check_vma=False
    )
```

```python
import jax
import jax.numpy as jnp
from jax import lax
from jax.experimental import pallas as pl
from jax.experimental.pallas import tpu as pltpu
from jax.sharding import PartitionSpec as P

RING = 4
CORES = 2


def per_part(cond, a, b):
    return jnp.where(cond.reshape((-1,) + (1,) * (a.ndim - 1)), a, b)


def pick(index, options):
    out = options[-1]
    for k in range(len(options) - 2, -1, -1):
        out = per_part(index == k, options[k], out)
    return out


def ring_bcast(value, axis, plus, minus, me, root):
    half = value.shape[0] // 2
    first, second = value[:half], value[half:]
    got_plus = lax.ppermute(first, axis, plus)
    got_minus = lax.ppermute(second, axis, minus)
    dist = (me - root) % RING
    at_root = dist == 0
    send_plus = jnp.where(at_root, second, got_plus)
    send_minus = jnp.where(at_root, first, got_minus)
    got_plus2 = lax.ppermute(send_plus, axis, plus)
    got_minus2 = lax.ppermute(send_minus, axis, minus)
    out_first = pick(dist, [first, got_plus, got_plus2, got_minus2])
    out_second = pick(dist, [second, got_plus2, got_minus2, got_minus])
    return jnp.concatenate([out_first, out_second], axis=0)


def row_pairs(step_z, step_x):
    return [
        (RING * z + x, RING * ((z + step_z) % RING) + (x + step_x) % RING)
        for z in range(RING)
        for x in range(RING)
    ]


def row_bcast(value, root):
    me = lax.axis_index("row")
    mz, mx = me // RING, me % RING
    rz, rx = root // RING, root % RING
    xp, xm = row_pairs(0, 1), row_pairs(0, RING - 1)
    zp, zm = row_pairs(1, 0), row_pairs(RING - 1, 0)
    half = value.shape[0] // 2
    along_x = value[:half]
    along_z = value[half:]
    along_x = ring_bcast(along_x, "row", xp, xm, mx, rx)
    along_z = ring_bcast(along_z, "row", zp, zm, mz, rz)
    along_x = ring_bcast(along_x, "row", zp, zm, mz, rz)
    along_z = ring_bcast(along_z, "row", xp, xm, mx, rx)
    return jnp.concatenate([along_x, along_z], axis=0)


def col_bcast(value, root):
    me = lax.axis_index("col")
    my, mk = me // CORES, me % CORES
    ry = root // CORES
    swap = [(CORES * y + k, CORES * y + 1 - k) for y in range(RING) for k in range(CORES)]
    hop = [(CORES * y, CORES * ((y + 1) % RING)) for y in range(RING)] + [
        (CORES * y + 1, CORES * ((y - 1) % RING) + 1) for y in range(RING)
    ]
    got_swap = lax.ppermute(value, "col", swap)
    on_root_chip = jnp.where(me == root, value, got_swap)
    got_hop = lax.ppermute(on_root_chip, "col", hop)
    dist = (my - ry) % RING
    near = jnp.where(dist == 0, on_root_chip, got_hop)
    got_swap2 = lax.ppermute(near, "col", swap)
    half = value.shape[0] // 2
    fwd = jnp.where(mk == 0, near[:half], near[half:])
    got_fwd = lax.ppermute(fwd, "col", hop)
    got_swap3 = lax.ppermute(got_fwd, "col", swap)
    far = jnp.where(
        mk == 0,
        jnp.concatenate([got_fwd, got_swap3], axis=0),
        jnp.concatenate([got_swap3, got_fwd], axis=0),
    )
    own_hop = (dist == 1) & (mk == 0) | (dist == 3) & (mk == 1)
    other_hop = (dist == 1) & (mk == 1) | (dist == 3) & (mk == 0)
    out = jnp.where(own_hop, got_hop, far)
    out = jnp.where(other_hop, got_swap2, out)
    return jnp.where(dist == 0, on_root_chip, out)


ROW_ORDERS = ((3, 2, 1, 0), (1, 0, 3, 2))
COL_ORDER = (0, 1, 2)


def xor_pairs(nrow, ncol, on_row, step):
    pairs = []
    for r in range(nrow):
        for c in range(ncol):
            if on_row:
                pairs.append((r * ncol + c, (r ^ (1 << ROW_ORDERS[c % CORES][step])) * ncol + c))
            else:
                pairs.append((r * ncol + c, r * ncol + (c ^ (1 << COL_ORDER[step]))))
    return pairs


def dims_of(on_row, parity, step):
    if on_row:
        z_first = (parity == 0) == (step == 0)
        return (2 if z_first else 0), RING
    return ((0, CORES), (1, RING))[step]


def digit_pairs(nrow, ncol, on_row, step, mask):
    pairs = []
    for r in range(nrow):
        for c in range(ncol):
            shift, _ = dims_of(on_row, c % CORES, step)
            if on_row:
                pairs.append((r * ncol + c, (r ^ (mask << shift)) * ncol + c))
            else:
                pairs.append((r * ncol + c, r * ncol + (c ^ (mask << shift))))
    return pairs


def xor_bcast(value, root, on_row):
    nrow = lax.axis_size("row")
    ncol = lax.axis_size("col")
    me = lax.axis_index("row") if on_row else lax.axis_index("col")
    parity = lax.axis_index("col") % CORES
    relative = me ^ root
    axes = ("row", "col")

    def digit(step):
        if on_row:
            shift = jnp.where(parity == 0, 2 if step == 0 else 0, 0 if step == 0 else 2)
        else:
            shift = dims_of(False, 0, step)[0]
        return (relative >> shift) & (RING - 1 if on_row or step == 1 else CORES - 1)

    sizes = [dims_of(on_row, 0, step)[1] for step in range(2)]
    shape = value.shape
    buf = value.reshape(shape[0], sizes[0], sizes[1], -1, shape[-1])
    for step in range(2):
        d = digit(step)
        groups = [buf[:, m] for m in range(sizes[step])]
        got = [None] + [
            lax.ppermute(groups[m], axes, digit_pairs(nrow, ncol, on_row, step, m))
            for m in range(1, sizes[step])
        ]
        buf = pick(d, [groups[0]] + got[1:])
    for step in reversed(range(2)):
        d = digit(step)
        got = [buf] + [
            lax.ppermute(buf, axes, digit_pairs(nrow, ncol, on_row, step, m))
            for m in range(1, sizes[step])
        ]
        buf = jnp.stack(
            [pick(d, [got[dd ^ t] for dd in range(sizes[step])]) for t in range(sizes[step])], axis=1
        )
    return buf.reshape(shape)


def all_bcast(value, root):
    nrow = lax.axis_size("row")
    ncol = lax.axis_size("col")
    n = nrow * ncol
    relative = (lax.axis_index("row") * ncol + lax.axis_index("col")) ^ root
    for b in range(n.bit_length() - 1):
        got = lax.ppermute(value, ("row", "col"), [(d, d ^ (1 << b)) for d in range(n)])
        value = per_part((relative >> b) == 1, got, value)
    return value


def lower_local(column, inverse, rows_ok):
    lower = jnp.einsum("iab,bc->iac", column, inverse, preferred_element_type=jnp.float32)
    return jnp.where(rows_ok[:, None, None], lower, 0.0).astype(jnp.bfloat16)


def eliminate(matrix, lower, upper, pivot, rows_ok, cols_ok, local, front_cols):
    product = jnp.einsum("iab,jbc->ijac", lower, upper, preferred_element_type=jnp.float32)
    update = rows_ok[:, None] & cols_ok[None, :] & (local > 0)
    changed = (matrix.astype(jnp.float32) - product).astype(jnp.bfloat16)
    result = jnp.where(update[:, :, None, None], changed, matrix)
    place = rows_ok[:, None] & (front_cols == pivot)[None, :]
    return jnp.where(place[:, :, None, None], lower[:, None], result)


def update_kernel(
    codes, row_codes, front_ref, c1_ref, c2_ref, x_ref, p1_ref, p2_ref, u1_ref, u2_ref, out_ref
):
    i = pl.program_id(0)
    row_code = row_codes[i]
    lower1 = jnp.dot(c1_ref[0], p1_ref[...], preferred_element_type=jnp.float32).astype(jnp.bfloat16)
    lower1 = jnp.where((row_code & 1) != 0, lower1, jnp.zeros_like(lower1))
    column = c2_ref[0]
    product = jnp.dot(lower1, x_ref[...], preferred_element_type=jnp.float32)
    changed = (column.astype(jnp.float32) - product).astype(jnp.bfloat16)
    column = jnp.where((row_code & 4) != 0, changed, column)
    lower2 = jnp.dot(column, p2_ref[...], preferred_element_type=jnp.float32).astype(jnp.bfloat16)
    lower2 = jnp.where((row_code & 2) != 0, lower2, jnp.zeros_like(lower2))
    for j in range(front_ref.shape[1]):
        code = codes[i, j]
        block = front_ref[0, j]
        block = jnp.where((code & 1) != 0, block, jnp.zeros_like(block))
        product = jnp.dot(lower1, u1_ref[j], preferred_element_type=jnp.float32)
        changed = (block.astype(jnp.float32) - product).astype(jnp.bfloat16)
        block = jnp.where((code & 2) != 0, changed, block)
        block = jnp.where((code & 4) != 0, lower1, block)
        product = jnp.dot(lower2, u2_ref[j], preferred_element_type=jnp.float32)
        changed = (block.astype(jnp.float32) - product).astype(jnp.bfloat16)
        block = jnp.where((code & 8) != 0, changed, block)
        block = jnp.where((code & 16) != 0, lower2, block)
        out_ref[0, j] = block


def both_updates(front, codes, row_codes, column1, column2, cross, inverse, upper1, upper2):
    rows, cols, bs, _ = front.shape
    row_block = pl.BlockSpec((1, cols, bs, bs), lambda i, c, r: (i, 0, 0, 0))
    lower_block = pl.BlockSpec((1, bs, bs), lambda i, c, r: (i, 0, 0))
    one_block = pl.BlockSpec((bs, bs), lambda i, c, r: (0, 0))
    upper_block = pl.BlockSpec((cols, bs, bs), lambda i, c, r: (0, 0, 0))
    return pl.pallas_call(
        update_kernel,
        grid_spec=pltpu.PrefetchScalarGridSpec(
            num_scalar_prefetch=2,
            grid=(rows,),
            in_specs=[
                row_block, lower_block, lower_block, one_block, one_block, one_block,
                upper_block, upper_block,
            ],
            out_specs=row_block,
        ),
        out_shape=jax.ShapeDtypeStruct(front.shape, front.dtype),
        compiler_params=pltpu.CompilerParams(dimension_semantics=("arbitrary",)),
    )(codes, row_codes, front, column1, column2, cross, inverse[0], inverse[1], upper1, upper2)


def masked(blocks, keep):
    shape = keep.shape + (1,) * (blocks.ndim - keep.ndim)
    return jnp.where(keep.reshape(shape) > 0, blocks, jnp.zeros_like(blocks))


def body(front, pattern, pivots, pivot_inv):
    rows_dev = front.shape[0]
    cols_dev = front.shape[1]
    nrow = lax.axis_size("row")
    ncol = lax.axis_size("col")
    row_index = lax.axis_index("row")
    col_index = lax.axis_index("col")
    grid = pattern.reshape(rows_dev, nrow, cols_dev, ncol)
    local = lax.dynamic_index_in_dim(grid, row_index, 1, keepdims=False)
    local = lax.dynamic_index_in_dim(local, col_index, 2, keepdims=False)
    front_rows = jnp.arange(rows_dev, dtype=jnp.int32) * nrow + row_index
    front_cols = jnp.arange(cols_dev, dtype=jnp.int32) * ncol + col_index
    first = pivots[0]
    second = pivots[1]
    rows_first = front_rows != first
    cols_first = front_cols != first
    rows_second = rows_first & (front_rows != second)
    cols_second = cols_first & (front_cols != second)

    a1, b1 = first // nrow, first // ncol
    a2, b2 = second // nrow, second // ncol
    r1, c1 = first % nrow, first % ncol
    r2, c2 = second % nrow, second % ncol

    def local_row(a):
        return masked(
            lax.dynamic_index_in_dim(front, a, 0, keepdims=False),
            lax.dynamic_index_in_dim(local, a, 0, keepdims=False),
        )

    def local_col(b):
        return masked(
            lax.dynamic_index_in_dim(front, b, 1, keepdims=False),
            lax.dynamic_index_in_dim(local, b, 1, keepdims=False),
        )

    cols_sent = xor_bcast(jnp.stack([local_col(b1), local_col(b2)]), jnp.stack([c1, c2]), False)
    rows_sent = xor_bcast(jnp.stack([local_row(a1), local_row(a2)]), jnp.stack([r1, r2]), True)
    second_col = cols_sent[1]
    upper_first, second_row = rows_sent[0], rows_sent[1]

    cross = all_bcast(
        jnp.stack([masked(front[a1, b2], local[a1, b2]), masked(front[a2, b1], local[a2, b1])]),
        jnp.stack([r1 * ncol + c2, r2 * ncol + c1]),
    )
    first_at_second, second_at_first = cross[0], cross[1]

    second_ok = (second != first)[None]
    lower_first_at_second = lower_local(second_at_first[None], pivot_inv[0], second_ok)
    row_after = eliminate(
        second_row[None],
        lower_first_at_second,
        upper_first,
        first,
        second_ok,
        cols_first,
        pattern[second][front_cols][None],
        front_cols,
    )
    upper_second = row_after[0]
    row_codes = (
        rows_first.astype(jnp.int32)
        + 2 * rows_second.astype(jnp.int32)
        + 4 * (rows_first & second_ok[0] & (pattern[front_rows, second] > 0)).astype(jnp.int32)
    )

    keep = local > 0
    update_first = rows_first[:, None] & cols_first[None, :] & keep
    place_first = rows_first[:, None] & (front_cols == first)[None, :]
    update_second = rows_second[:, None] & cols_second[None, :] & keep
    place_second = rows_second[:, None] & (front_cols == second)[None, :]
    codes = (
        keep.astype(jnp.int32)
        + 2 * update_first.astype(jnp.int32)
        + 4 * place_first.astype(jnp.int32)
        + 8 * update_second.astype(jnp.int32)
        + 16 * place_second.astype(jnp.int32)
    )
    return both_updates(
        front, codes, row_codes, cols_sent[0], second_col, first_at_second, pivot_inv,
        upper_first, upper_second,
    )


def solution(mesh):
    placed = (P("row", "col", None, None), P(), P(), P())
    return jax.shard_map(
        body, mesh=mesh, in_specs=placed, out_specs=P("row", "col", None, None), check_vma=False
    )
```

```python
import jax
import jax.numpy as jnp
from jax import lax
from jax.experimental import pallas as pl
from jax.experimental.pallas import tpu as pltpu
from jax.sharding import PartitionSpec as P

RING = 4
CORES = 2


def per_part(cond, a, b):
    return jnp.where(cond.reshape((-1,) + (1,) * (a.ndim - 1)), a, b)


def pick(index, options):
    out = options[-1]
    for k in range(len(options) - 2, -1, -1):
        out = per_part(index == k, options[k], out)
    return out


def ring_bcast(value, axis, plus, minus, me, root):
    half = value.shape[0] // 2
    first, second = value[:half], value[half:]
    got_plus = lax.ppermute(first, axis, plus)
    got_minus = lax.ppermute(second, axis, minus)
    dist = (me - root) % RING
    at_root = dist == 0
    send_plus = jnp.where(at_root, second, got_plus)
    send_minus = jnp.where(at_root, first, got_minus)
    got_plus2 = lax.ppermute(send_plus, axis, plus)
    got_minus2 = lax.ppermute(send_minus, axis, minus)
    out_first = pick(dist, [first, got_plus, got_plus2, got_minus2])
    out_second = pick(dist, [second, got_plus2, got_minus2, got_minus])
    return jnp.concatenate([out_first, out_second], axis=0)


def row_pairs(step_z, step_x):
    return [
        (RING * z + x, RING * ((z + step_z) % RING) + (x + step_x) % RING)
        for z in range(RING)
        for x in range(RING)
    ]


def row_bcast(value, root):
    me = lax.axis_index("row")
    mz, mx = me // RING, me % RING
    rz, rx = root // RING, root % RING
    xp, xm = row_pairs(0, 1), row_pairs(0, RING - 1)
    zp, zm = row_pairs(1, 0), row_pairs(RING - 1, 0)
    half = value.shape[0] // 2
    along_x = value[:half]
    along_z = value[half:]
    along_x = ring_bcast(along_x, "row", xp, xm, mx, rx)
    along_z = ring_bcast(along_z, "row", zp, zm, mz, rz)
    along_x = ring_bcast(along_x, "row", zp, zm, mz, rz)
    along_z = ring_bcast(along_z, "row", xp, xm, mx, rx)
    return jnp.concatenate([along_x, along_z], axis=0)


def col_bcast(value, root):
    me = lax.axis_index("col")
    my, mk = me // CORES, me % CORES
    ry = root // CORES
    swap = [(CORES * y + k, CORES * y + 1 - k) for y in range(RING) for k in range(CORES)]
    hop = [(CORES * y, CORES * ((y + 1) % RING)) for y in range(RING)] + [
        (CORES * y + 1, CORES * ((y - 1) % RING) + 1) for y in range(RING)
    ]
    got_swap = lax.ppermute(value, "col", swap)
    on_root_chip = jnp.where(me == root, value, got_swap)
    got_hop = lax.ppermute(on_root_chip, "col", hop)
    dist = (my - ry) % RING
    near = jnp.where(dist == 0, on_root_chip, got_hop)
    got_swap2 = lax.ppermute(near, "col", swap)
    half = value.shape[0] // 2
    fwd = jnp.where(mk == 0, near[:half], near[half:])
    got_fwd = lax.ppermute(fwd, "col", hop)
    got_swap3 = lax.ppermute(got_fwd, "col", swap)
    far = jnp.where(
        mk == 0,
        jnp.concatenate([got_fwd, got_swap3], axis=0),
        jnp.concatenate([got_swap3, got_fwd], axis=0),
    )
    own_hop = (dist == 1) & (mk == 0) | (dist == 3) & (mk == 1)
    other_hop = (dist == 1) & (mk == 1) | (dist == 3) & (mk == 0)
    out = jnp.where(own_hop, got_hop, far)
    out = jnp.where(other_hop, got_swap2, out)
    return jnp.where(dist == 0, on_root_chip, out)


ROW_ORDERS = ((3, 2, 1, 0), (1, 0, 3, 2))
COL_ORDER = (0, 1, 2)


def xor_pairs(nrow, ncol, on_row, step):
    pairs = []
    for r in range(nrow):
        for c in range(ncol):
            if on_row:
                pairs.append((r * ncol + c, (r ^ (1 << ROW_ORDERS[c % CORES][step])) * ncol + c))
            else:
                pairs.append((r * ncol + c, r * ncol + (c ^ (1 << COL_ORDER[step]))))
    return pairs


def dims_of(on_row, parity, step):
    if on_row:
        z_first = (parity == 0) == (step == 0)
        return (2 if z_first else 0), RING
    return ((0, CORES), (1, RING))[step]


def digit_pairs(nrow, ncol, on_row, step, mask):
    pairs = []
    for r in range(nrow):
        for c in range(ncol):
            shift, _ = dims_of(on_row, c % CORES, step)
            if on_row:
                pairs.append((r * ncol + c, (r ^ (mask << shift)) * ncol + c))
            else:
                pairs.append((r * ncol + c, r * ncol + (c ^ (mask << shift))))
    return pairs


def xor_bcast(value, root, on_row):
    nrow = lax.axis_size("row")
    ncol = lax.axis_size("col")
    me = lax.axis_index("row") if on_row else lax.axis_index("col")
    parity = lax.axis_index("col") % CORES
    relative = me ^ root
    axes = ("row", "col")

    def digit(step):
        if on_row:
            shift = jnp.where(parity == 0, 2 if step == 0 else 0, 0 if step == 0 else 2)
        else:
            shift = dims_of(False, 0, step)[0]
        return (relative >> shift) & (RING - 1 if on_row or step == 1 else CORES - 1)

    sizes = [dims_of(on_row, 0, step)[1] for step in range(2)]
    shape = value.shape
    buf = value.reshape(shape[0], sizes[0], sizes[1], -1, shape[-1])
    for step in range(2):
        d = digit(step)
        groups = [buf[:, m] for m in range(sizes[step])]
        got = [None] + [
            lax.ppermute(groups[m], axes, digit_pairs(nrow, ncol, on_row, step, m))
            for m in range(1, sizes[step])
        ]
        buf = pick(d, [groups[0]] + got[1:])
    for step in reversed(range(2)):
        d = digit(step)
        got = [buf] + [
            lax.ppermute(buf, axes, digit_pairs(nrow, ncol, on_row, step, m))
            for m in range(1, sizes[step])
        ]
        buf = jnp.stack(
            [pick(d, [got[dd ^ t] for dd in range(sizes[step])]) for t in range(sizes[step])], axis=1
        )
    return buf.reshape(shape)


def all_bcast(value, root):
    nrow = lax.axis_size("row")
    ncol = lax.axis_size("col")
    n = nrow * ncol
    relative = (lax.axis_index("row") * ncol + lax.axis_index("col")) ^ root
    for b in range(n.bit_length() - 1):
        got = lax.ppermute(value, ("row", "col"), [(d, d ^ (1 << b)) for d in range(n)])
        value = per_part((relative >> b) == 1, got, value)
    return value


def lower_local(column, inverse, rows_ok):
    lower = jnp.einsum("iab,bc->iac", column, inverse, preferred_element_type=jnp.float32)
    return jnp.where(rows_ok[:, None, None], lower, 0.0).astype(jnp.bfloat16)


def eliminate(matrix, lower, upper, pivot, rows_ok, cols_ok, local, front_cols):
    product = jnp.einsum("iab,jbc->ijac", lower, upper, preferred_element_type=jnp.float32)
    update = rows_ok[:, None] & cols_ok[None, :] & (local > 0)
    changed = (matrix.astype(jnp.float32) - product).astype(jnp.bfloat16)
    result = jnp.where(update[:, :, None, None], changed, matrix)
    place = rows_ok[:, None] & (front_cols == pivot)[None, :]
    return jnp.where(place[:, :, None, None], lower[:, None], result)


def update_kernel(
    codes, row_codes, col_codes, front_ref, c1_ref, c2_ref, x_ref, y_ref, p1_ref, p2_ref, u1_ref,
    r2_ref, out_ref, u2_ref,
):
    i = pl.program_id(0)

    @pl.when(i == 0)
    def _():
        lower = jnp.dot(y_ref[...], p1_ref[...], preferred_element_type=jnp.float32).astype(jnp.bfloat16)
        for j in range(r2_ref.shape[0]):
            code = col_codes[j]
            block = r2_ref[j]
            product = jnp.dot(lower, u1_ref[j], preferred_element_type=jnp.float32)
            changed = (block.astype(jnp.float32) - product).astype(jnp.bfloat16)
            block = jnp.where((code & 1) != 0, changed, block)
            u2_ref[j] = jnp.where((code & 2) != 0, lower, block)

    row_code = row_codes[i]
    lower1 = jnp.dot(c1_ref[0], p1_ref[...], preferred_element_type=jnp.float32).astype(jnp.bfloat16)
    lower1 = jnp.where((row_code & 1) != 0, lower1, jnp.zeros_like(lower1))
    column = c2_ref[0]
    product = jnp.dot(lower1, x_ref[...], preferred_element_type=jnp.float32)
    changed = (column.astype(jnp.float32) - product).astype(jnp.bfloat16)
    column = jnp.where((row_code & 4) != 0, changed, column)
    lower2 = jnp.dot(column, p2_ref[...], preferred_element_type=jnp.float32).astype(jnp.bfloat16)
    lower2 = jnp.where((row_code & 2) != 0, lower2, jnp.zeros_like(lower2))
    for j in range(front_ref.shape[1]):
        code = codes[i, j]
        block = front_ref[0, j]
        block = jnp.where((code & 1) != 0, block, jnp.zeros_like(block))
        product = jnp.dot(lower1, u1_ref[j], preferred_element_type=jnp.float32)
        changed = (block.astype(jnp.float32) - product).astype(jnp.bfloat16)
        block = jnp.where((code & 2) != 0, changed, block)
        block = jnp.where((code & 4) != 0, lower1, block)
        product = jnp.dot(lower2, u2_ref[j], preferred_element_type=jnp.float32)
        changed = (block.astype(jnp.float32) - product).astype(jnp.bfloat16)
        block = jnp.where((code & 8) != 0, changed, block)
        block = jnp.where((code & 16) != 0, lower2, block)
        out_ref[0, j] = block


def both_updates(front, codes, row_codes, col_codes, column1, column2, cross, inverse, upper1, row2):
    rows, cols, bs, _ = front.shape
    row_block = pl.BlockSpec((1, cols, bs, bs), lambda i, c, r, k: (i, 0, 0, 0))
    lower_block = pl.BlockSpec((1, bs, bs), lambda i, c, r, k: (i, 0, 0))
    one_block = pl.BlockSpec((bs, bs), lambda i, c, r, k: (0, 0))
    upper_block = pl.BlockSpec((cols, bs, bs), lambda i, c, r, k: (0, 0, 0))
    return pl.pallas_call(
        update_kernel,
        grid_spec=pltpu.PrefetchScalarGridSpec(
            num_scalar_prefetch=3,
            grid=(rows,),
            in_specs=[
                row_block, lower_block, lower_block, one_block, one_block, one_block, one_block,
                upper_block, upper_block,
            ],
            out_specs=row_block,
            scratch_shapes=[pltpu.VMEM((cols, bs, bs), front.dtype)],
        ),
        out_shape=jax.ShapeDtypeStruct(front.shape, front.dtype),
        compiler_params=pltpu.CompilerParams(dimension_semantics=("arbitrary",)),
    )(
        codes, row_codes, col_codes, front, column1, column2, cross[0], cross[1], inverse[0],
        inverse[1], upper1, row2,
    )


def masked(blocks, keep):
    shape = keep.shape + (1,) * (blocks.ndim - keep.ndim)
    return jnp.where(keep.reshape(shape) > 0, blocks, jnp.zeros_like(blocks))


def body(front, pattern, pivots, pivot_inv):
    rows_dev = front.shape[0]
    cols_dev = front.shape[1]
    nrow = lax.axis_size("row")
    ncol = lax.axis_size("col")
    row_index = lax.axis_index("row")
    col_index = lax.axis_index("col")
    grid = pattern.reshape(rows_dev, nrow, cols_dev, ncol)
    local = lax.dynamic_index_in_dim(grid, row_index, 1, keepdims=False)
    local = lax.dynamic_index_in_dim(local, col_index, 2, keepdims=False)
    front_rows = jnp.arange(rows_dev, dtype=jnp.int32) * nrow + row_index
    front_cols = jnp.arange(cols_dev, dtype=jnp.int32) * ncol + col_index
    first = pivots[0]
    second = pivots[1]
    rows_first = front_rows != first
    cols_first = front_cols != first
    rows_second = rows_first & (front_rows != second)
    cols_second = cols_first & (front_cols != second)

    a1, b1 = first // nrow, first // ncol
    a2, b2 = second // nrow, second // ncol
    r1, c1 = first % nrow, first % ncol
    r2, c2 = second % nrow, second % ncol

    def local_row(a):
        return masked(
            lax.dynamic_index_in_dim(front, a, 0, keepdims=False),
            lax.dynamic_index_in_dim(local, a, 0, keepdims=False),
        )

    def local_col(b):
        return masked(
            lax.dynamic_index_in_dim(front, b, 1, keepdims=False),
            lax.dynamic_index_in_dim(local, b, 1, keepdims=False),
        )

    cols_sent = xor_bcast(jnp.stack([local_col(b1), local_col(b2)]), jnp.stack([c1, c2]), False)
    rows_sent = xor_bcast(jnp.stack([local_row(a1), local_row(a2)]), jnp.stack([r1, r2]), True)
    second_col = cols_sent[1]
    upper_first, second_row = rows_sent[0], rows_sent[1]

    cross = all_bcast(
        jnp.stack([masked(front[a1, b2], local[a1, b2]), masked(front[a2, b1], local[a2, b1])]),
        jnp.stack([r1 * ncol + c2, r2 * ncol + c1]),
    )
    first_at_second, second_at_first = cross[0], cross[1]

    second_ok = (second != first)[None]
    col_codes = (
        (second_ok[0] & cols_first & (pattern[second][front_cols] > 0)).astype(jnp.int32)
        + 2 * (second_ok[0] & (front_cols == first)).astype(jnp.int32)
    )
    row_codes = (
        rows_first.astype(jnp.int32)
        + 2 * rows_second.astype(jnp.int32)
        + 4 * (rows_first & second_ok[0] & (pattern[front_rows, second] > 0)).astype(jnp.int32)
    )

    keep = local > 0
    update_first = rows_first[:, None] & cols_first[None, :] & keep
    place_first = rows_first[:, None] & (front_cols == first)[None, :]
    update_second = rows_second[:, None] & cols_second[None, :] & keep
    place_second = rows_second[:, None] & (front_cols == second)[None, :]
    codes = (
        keep.astype(jnp.int32)
        + 2 * update_first.astype(jnp.int32)
        + 4 * place_first.astype(jnp.int32)
        + 8 * update_second.astype(jnp.int32)
        + 16 * place_second.astype(jnp.int32)
    )
    return both_updates(
        front, codes, row_codes, col_codes, cols_sent[0], second_col, cross, pivot_inv,
        upper_first, second_row,
    )


def solution(mesh):
    placed = (P("row", "col", None, None), P(), P(), P())
    return jax.shard_map(
        body, mesh=mesh, in_specs=placed, out_specs=P("row", "col", None, None), check_vma=False
    )
```

```python
import jax
import jax.numpy as jnp
from jax import lax
from jax.experimental import pallas as pl
from jax.experimental.pallas import tpu as pltpu
from jax.sharding import PartitionSpec as P

RING = 4
CORES = 2


def per_part(cond, a, b):
    return jnp.where(cond.reshape((-1,) + (1,) * (a.ndim - 1)), a, b)


def pick(index, options):
    out = options[-1]
    for k in range(len(options) - 2, -1, -1):
        out = per_part(index == k, options[k], out)
    return out


def ring_bcast(value, axis, plus, minus, me, root):
    half = value.shape[0] // 2
    first, second = value[:half], value[half:]
    got_plus = lax.ppermute(first, axis, plus)
    got_minus = lax.ppermute(second, axis, minus)
    dist = (me - root) % RING
    at_root = dist == 0
    send_plus = jnp.where(at_root, second, got_plus)
    send_minus = jnp.where(at_root, first, got_minus)
    got_plus2 = lax.ppermute(send_plus, axis, plus)
    got_minus2 = lax.ppermute(send_minus, axis, minus)
    out_first = pick(dist, [first, got_plus, got_plus2, got_minus2])
    out_second = pick(dist, [second, got_plus2, got_minus2, got_minus])
    return jnp.concatenate([out_first, out_second], axis=0)


def row_pairs(step_z, step_x):
    return [
        (RING * z + x, RING * ((z + step_z) % RING) + (x + step_x) % RING)
        for z in range(RING)
        for x in range(RING)
    ]


def row_bcast(value, root):
    me = lax.axis_index("row")
    mz, mx = me // RING, me % RING
    rz, rx = root // RING, root % RING
    xp, xm = row_pairs(0, 1), row_pairs(0, RING - 1)
    zp, zm = row_pairs(1, 0), row_pairs(RING - 1, 0)
    half = value.shape[0] // 2
    along_x = value[:half]
    along_z = value[half:]
    along_x = ring_bcast(along_x, "row", xp, xm, mx, rx)
    along_z = ring_bcast(along_z, "row", zp, zm, mz, rz)
    along_x = ring_bcast(along_x, "row", zp, zm, mz, rz)
    along_z = ring_bcast(along_z, "row", xp, xm, mx, rx)
    return jnp.concatenate([along_x, along_z], axis=0)


def col_bcast(value, root):
    me = lax.axis_index("col")
    my, mk = me // CORES, me % CORES
    ry = root // CORES
    swap = [(CORES * y + k, CORES * y + 1 - k) for y in range(RING) for k in range(CORES)]
    hop = [(CORES * y, CORES * ((y + 1) % RING)) for y in range(RING)] + [
        (CORES * y + 1, CORES * ((y - 1) % RING) + 1) for y in range(RING)
    ]
    got_swap = lax.ppermute(value, "col", swap)
    on_root_chip = jnp.where(me == root, value, got_swap)
    got_hop = lax.ppermute(on_root_chip, "col", hop)
    dist = (my - ry) % RING
    near = jnp.where(dist == 0, on_root_chip, got_hop)
    got_swap2 = lax.ppermute(near, "col", swap)
    half = value.shape[0] // 2
    fwd = jnp.where(mk == 0, near[:half], near[half:])
    got_fwd = lax.ppermute(fwd, "col", hop)
    got_swap3 = lax.ppermute(got_fwd, "col", swap)
    far = jnp.where(
        mk == 0,
        jnp.concatenate([got_fwd, got_swap3], axis=0),
        jnp.concatenate([got_swap3, got_fwd], axis=0),
    )
    own_hop = (dist == 1) & (mk == 0) | (dist == 3) & (mk == 1)
    other_hop = (dist == 1) & (mk == 1) | (dist == 3) & (mk == 0)
    out = jnp.where(own_hop, got_hop, far)
    out = jnp.where(other_hop, got_swap2, out)
    return jnp.where(dist == 0, on_root_chip, out)


ROW_ORDERS = ((3, 2, 1, 0), (1, 0, 3, 2))
COL_ORDER = (0, 1, 2)


def xor_pairs(nrow, ncol, on_row, step):
    pairs = []
    for r in range(nrow):
        for c in range(ncol):
            if on_row:
                pairs.append((r * ncol + c, (r ^ (1 << ROW_ORDERS[c % CORES][step])) * ncol + c))
            else:
                pairs.append((r * ncol + c, r * ncol + (c ^ (1 << COL_ORDER[step]))))
    return pairs


def dims_of(on_row, parity, step):
    if on_row:
        z_first = (parity == 0) == (step == 0)
        return (2 if z_first else 0), RING
    return ((0, CORES), (1, RING))[step]


def digit_pairs(nrow, ncol, on_row, step, mask):
    pairs = []
    for r in range(nrow):
        for c in range(ncol):
            shift, _ = dims_of(on_row, c % CORES, step)
            if on_row:
                pairs.append((r * ncol + c, (r ^ (mask << shift)) * ncol + c))
            else:
                pairs.append((r * ncol + c, r * ncol + (c ^ (mask << shift))))
    return pairs


def xor_bcast(value, root, on_row):
    nrow = lax.axis_size("row")
    ncol = lax.axis_size("col")
    me = lax.axis_index("row") if on_row else lax.axis_index("col")
    parity = lax.axis_index("col") % CORES
    relative = me ^ root
    axes = ("row", "col")

    def digit(step):
        if on_row:
            shift = jnp.where(parity == 0, 2 if step == 0 else 0, 0 if step == 0 else 2)
        else:
            shift = dims_of(False, 0, step)[0]
        return (relative >> shift) & (RING - 1 if on_row or step == 1 else CORES - 1)

    sizes = [dims_of(on_row, 0, step)[1] for step in range(2)]
    shape = value.shape
    buf = value.reshape(shape[0], sizes[0], sizes[1], -1, shape[-1])
    for step in range(2):
        d = digit(step)
        groups = [buf[:, m] for m in range(sizes[step])]
        got = [None] + [
            lax.ppermute(groups[m], axes, digit_pairs(nrow, ncol, on_row, step, m))
            for m in range(1, sizes[step])
        ]
        buf = pick(d, [groups[0]] + got[1:])
    for step in reversed(range(2)):
        d = digit(step)
        got = [buf] + [
            lax.ppermute(buf, axes, digit_pairs(nrow, ncol, on_row, step, m))
            for m in range(1, sizes[step])
        ]
        buf = jnp.stack(
            [pick(d, [got[dd ^ t] for dd in range(sizes[step])]) for t in range(sizes[step])], axis=1
        )
    return buf.reshape(shape)


def all_bcast(value, root):
    nrow = lax.axis_size("row")
    ncol = lax.axis_size("col")
    n = nrow * ncol
    relative = (lax.axis_index("row") * ncol + lax.axis_index("col")) ^ root
    for b in range(n.bit_length() - 1):
        got = lax.ppermute(value, ("row", "col"), [(d, d ^ (1 << b)) for d in range(n)])
        value = per_part((relative >> b) == 1, got, value)
    return value


def lower_local(column, inverse, rows_ok):
    lower = jnp.einsum("iab,bc->iac", column, inverse, preferred_element_type=jnp.float32)
    return jnp.where(rows_ok[:, None, None], lower, 0.0).astype(jnp.bfloat16)


def eliminate(matrix, lower, upper, pivot, rows_ok, cols_ok, local, front_cols):
    product = jnp.einsum("iab,jbc->ijac", lower, upper, preferred_element_type=jnp.float32)
    update = rows_ok[:, None] & cols_ok[None, :] & (local > 0)
    changed = (matrix.astype(jnp.float32) - product).astype(jnp.bfloat16)
    result = jnp.where(update[:, :, None, None], changed, matrix)
    place = rows_ok[:, None] & (front_cols == pivot)[None, :]
    return jnp.where(place[:, :, None, None], lower[:, None], result)


def update_kernel(
    codes, row_codes, front_ref, c1_ref, c2_ref, x_ref, p1_ref, p2_ref, u1_ref, u2_ref, out_ref
):
    for r in range(front_ref.shape[0]):
        i = pl.program_id(0) * front_ref.shape[0] + r
        row_code = row_codes[i]
        lower1 = jnp.dot(c1_ref[r], p1_ref[...], preferred_element_type=jnp.float32).astype(jnp.bfloat16)
        lower1 = jnp.where((row_code & 1) != 0, lower1, jnp.zeros_like(lower1))
        column = c2_ref[r]
        product = jnp.dot(lower1, x_ref[...], preferred_element_type=jnp.float32)
        changed = (column.astype(jnp.float32) - product).astype(jnp.bfloat16)
        column = jnp.where((row_code & 4) != 0, changed, column)
        lower2 = jnp.dot(column, p2_ref[...], preferred_element_type=jnp.float32).astype(jnp.bfloat16)
        lower2 = jnp.where((row_code & 2) != 0, lower2, jnp.zeros_like(lower2))
        for j in range(front_ref.shape[1]):
            code = codes[i, j]
            block = front_ref[r, j]
            block = jnp.where((code & 1) != 0, block, jnp.zeros_like(block))
            product = jnp.dot(lower1, u1_ref[j], preferred_element_type=jnp.float32)
            changed = (block.astype(jnp.float32) - product).astype(jnp.bfloat16)
            block = jnp.where((code & 2) != 0, changed, block)
            block = jnp.where((code & 4) != 0, lower1, block)
            product = jnp.dot(lower2, u2_ref[j], preferred_element_type=jnp.float32)
            changed = (block.astype(jnp.float32) - product).astype(jnp.bfloat16)
            block = jnp.where((code & 8) != 0, changed, block)
            block = jnp.where((code & 16) != 0, lower2, block)
            out_ref[r, j] = block


ROWS_PER_STEP = 2


def both_updates(front, codes, row_codes, column1, column2, cross, inverse, upper1, upper2):
    rows, cols, bs, _ = front.shape
    step = ROWS_PER_STEP
    row_block = pl.BlockSpec((step, cols, bs, bs), lambda i, c, r: (i, 0, 0, 0))
    lower_block = pl.BlockSpec((step, bs, bs), lambda i, c, r: (i, 0, 0))
    one_block = pl.BlockSpec((bs, bs), lambda i, c, r: (0, 0))
    upper_block = pl.BlockSpec((cols, bs, bs), lambda i, c, r: (0, 0, 0))
    return pl.pallas_call(
        update_kernel,
        grid_spec=pltpu.PrefetchScalarGridSpec(
            num_scalar_prefetch=2,
            grid=(rows // step,),
            in_specs=[
                row_block, lower_block, lower_block, one_block, one_block, one_block,
                upper_block, upper_block,
            ],
            out_specs=row_block,
        ),
        out_shape=jax.ShapeDtypeStruct(front.shape, front.dtype),
        compiler_params=pltpu.CompilerParams(dimension_semantics=("arbitrary",)),
    )(codes, row_codes, front, column1, column2, cross, inverse[0], inverse[1], upper1, upper2)


def masked(blocks, keep):
    shape = keep.shape + (1,) * (blocks.ndim - keep.ndim)
    return jnp.where(keep.reshape(shape) > 0, blocks, jnp.zeros_like(blocks))


def body(front, pattern, pivots, pivot_inv):
    rows_dev = front.shape[0]
    cols_dev = front.shape[1]
    nrow = lax.axis_size("row")
    ncol = lax.axis_size("col")
    row_index = lax.axis_index("row")
    col_index = lax.axis_index("col")
    grid = pattern.reshape(rows_dev, nrow, cols_dev, ncol)
    local = lax.dynamic_index_in_dim(grid, row_index, 1, keepdims=False)
    local = lax.dynamic_index_in_dim(local, col_index, 2, keepdims=False)
    front_rows = jnp.arange(rows_dev, dtype=jnp.int32) * nrow + row_index
    front_cols = jnp.arange(cols_dev, dtype=jnp.int32) * ncol + col_index
    first = pivots[0]
    second = pivots[1]
    rows_first = front_rows != first
    cols_first = front_cols != first
    rows_second = rows_first & (front_rows != second)
    cols_second = cols_first & (front_cols != second)

    a1, b1 = first // nrow, first // ncol
    a2, b2 = second // nrow, second // ncol
    r1, c1 = first % nrow, first % ncol
    r2, c2 = second % nrow, second % ncol

    def local_row(a):
        return masked(
            lax.dynamic_index_in_dim(front, a, 0, keepdims=False),
            lax.dynamic_index_in_dim(local, a, 0, keepdims=False),
        )

    def local_col(b):
        return masked(
            lax.dynamic_index_in_dim(front, b, 1, keepdims=False),
            lax.dynamic_index_in_dim(local, b, 1, keepdims=False),
        )

    cols_sent = xor_bcast(jnp.stack([local_col(b1), local_col(b2)]), jnp.stack([c1, c2]), False)
    rows_sent = xor_bcast(jnp.stack([local_row(a1), local_row(a2)]), jnp.stack([r1, r2]), True)
    second_col = cols_sent[1]
    upper_first, second_row = rows_sent[0], rows_sent[1]

    cross = all_bcast(
        jnp.stack([masked(front[a1, b2], local[a1, b2]), masked(front[a2, b1], local[a2, b1])]),
        jnp.stack([r1 * ncol + c2, r2 * ncol + c1]),
    )
    first_at_second, second_at_first = cross[0], cross[1]

    second_ok = (second != first)[None]
    lower_first_at_second = lower_local(second_at_first[None], pivot_inv[0], second_ok)
    row_after = eliminate(
        second_row[None],
        lower_first_at_second,
        upper_first,
        first,
        second_ok,
        cols_first,
        pattern[second][front_cols][None],
        front_cols,
    )
    upper_second = row_after[0]
    row_codes = (
        rows_first.astype(jnp.int32)
        + 2 * rows_second.astype(jnp.int32)
        + 4 * (rows_first & second_ok[0] & (pattern[front_rows, second] > 0)).astype(jnp.int32)
    )

    keep = local > 0
    update_first = rows_first[:, None] & cols_first[None, :] & keep
    place_first = rows_first[:, None] & (front_cols == first)[None, :]
    update_second = rows_second[:, None] & cols_second[None, :] & keep
    place_second = rows_second[:, None] & (front_cols == second)[None, :]
    codes = (
        keep.astype(jnp.int32)
        + 2 * update_first.astype(jnp.int32)
        + 4 * place_first.astype(jnp.int32)
        + 8 * update_second.astype(jnp.int32)
        + 16 * place_second.astype(jnp.int32)
    )
    return both_updates(
        front, codes, row_codes, cols_sent[0], second_col, first_at_second, pivot_inv,
        upper_first, upper_second,
    )


def solution(mesh):
    placed = (P("row", "col", None, None), P(), P(), P())
    return jax.shard_map(
        body, mesh=mesh, in_specs=placed, out_specs=P("row", "col", None, None), check_vma=False
    )
```

```python
import jax
import jax.numpy as jnp
from jax import lax
from jax.experimental import pallas as pl
from jax.experimental.pallas import tpu as pltpu
from jax.sharding import PartitionSpec as P

RING = 4
CORES = 2


def per_part(cond, a, b):
    return jnp.where(cond.reshape((-1,) + (1,) * (a.ndim - 1)), a, b)


def pick(index, options):
    out = options[-1]
    for k in range(len(options) - 2, -1, -1):
        out = per_part(index == k, options[k], out)
    return out


def ring_bcast(value, axis, plus, minus, me, root):
    half = value.shape[0] // 2
    first, second = value[:half], value[half:]
    got_plus = lax.ppermute(first, axis, plus)
    got_minus = lax.ppermute(second, axis, minus)
    dist = (me - root) % RING
    at_root = dist == 0
    send_plus = jnp.where(at_root, second, got_plus)
    send_minus = jnp.where(at_root, first, got_minus)
    got_plus2 = lax.ppermute(send_plus, axis, plus)
    got_minus2 = lax.ppermute(send_minus, axis, minus)
    out_first = pick(dist, [first, got_plus, got_plus2, got_minus2])
    out_second = pick(dist, [second, got_plus2, got_minus2, got_minus])
    return jnp.concatenate([out_first, out_second], axis=0)


def row_pairs(step_z, step_x):
    return [
        (RING * z + x, RING * ((z + step_z) % RING) + (x + step_x) % RING)
        for z in range(RING)
        for x in range(RING)
    ]


def row_bcast(value, root):
    me = lax.axis_index("row")
    mz, mx = me // RING, me % RING
    rz, rx = root // RING, root % RING
    xp, xm = row_pairs(0, 1), row_pairs(0, RING - 1)
    zp, zm = row_pairs(1, 0), row_pairs(RING - 1, 0)
    half = value.shape[0] // 2
    along_x = value[:half]
    along_z = value[half:]
    along_x = ring_bcast(along_x, "row", xp, xm, mx, rx)
    along_z = ring_bcast(along_z, "row", zp, zm, mz, rz)
    along_x = ring_bcast(along_x, "row", zp, zm, mz, rz)
    along_z = ring_bcast(along_z, "row", xp, xm, mx, rx)
    return jnp.concatenate([along_x, along_z], axis=0)


def col_bcast(value, root):
    me = lax.axis_index("col")
    my, mk = me // CORES, me % CORES
    ry = root // CORES
    swap = [(CORES * y + k, CORES * y + 1 - k) for y in range(RING) for k in range(CORES)]
    hop = [(CORES * y, CORES * ((y + 1) % RING)) for y in range(RING)] + [
        (CORES * y + 1, CORES * ((y - 1) % RING) + 1) for y in range(RING)
    ]
    got_swap = lax.ppermute(value, "col", swap)
    on_root_chip = jnp.where(me == root, value, got_swap)
    got_hop = lax.ppermute(on_root_chip, "col", hop)
    dist = (my - ry) % RING
    near = jnp.where(dist == 0, on_root_chip, got_hop)
    got_swap2 = lax.ppermute(near, "col", swap)
    half = value.shape[0] // 2
    fwd = jnp.where(mk == 0, near[:half], near[half:])
    got_fwd = lax.ppermute(fwd, "col", hop)
    got_swap3 = lax.ppermute(got_fwd, "col", swap)
    far = jnp.where(
        mk == 0,
        jnp.concatenate([got_fwd, got_swap3], axis=0),
        jnp.concatenate([got_swap3, got_fwd], axis=0),
    )
    own_hop = (dist == 1) & (mk == 0) | (dist == 3) & (mk == 1)
    other_hop = (dist == 1) & (mk == 1) | (dist == 3) & (mk == 0)
    out = jnp.where(own_hop, got_hop, far)
    out = jnp.where(other_hop, got_swap2, out)
    return jnp.where(dist == 0, on_root_chip, out)


ROW_ORDERS = ((3, 2, 1, 0), (1, 0, 3, 2))
COL_ORDER = (0, 1, 2)


def xor_pairs(nrow, ncol, on_row, step):
    pairs = []
    for r in range(nrow):
        for c in range(ncol):
            if on_row:
                pairs.append((r * ncol + c, (r ^ (1 << ROW_ORDERS[c % CORES][step])) * ncol + c))
            else:
                pairs.append((r * ncol + c, r * ncol + (c ^ (1 << COL_ORDER[step]))))
    return pairs


def dims_of(on_row, parity, step):
    if on_row:
        z_first = (parity == 0) == (step == 0)
        return (2 if z_first else 0), RING
    return ((0, CORES), (1, RING))[step]


def digit_pairs(nrow, ncol, on_row, step, mask):
    pairs = []
    for r in range(nrow):
        for c in range(ncol):
            shift, _ = dims_of(on_row, c % CORES, step)
            if on_row:
                pairs.append((r * ncol + c, (r ^ (mask << shift)) * ncol + c))
            else:
                pairs.append((r * ncol + c, r * ncol + (c ^ (mask << shift))))
    return pairs


def xor_bcast(value, root, on_row):
    nrow = lax.axis_size("row")
    ncol = lax.axis_size("col")
    me = lax.axis_index("row") if on_row else lax.axis_index("col")
    parity = lax.axis_index("col") % CORES
    relative = me ^ root
    axes = ("row", "col")

    def digit(step):
        if on_row:
            shift = jnp.where(parity == 0, 2 if step == 0 else 0, 0 if step == 0 else 2)
        else:
            shift = dims_of(False, 0, step)[0]
        return (relative >> shift) & (RING - 1 if on_row or step == 1 else CORES - 1)

    sizes = [dims_of(on_row, 0, step)[1] for step in range(2)]
    shape = value.shape
    buf = value.reshape(shape[0], sizes[0], sizes[1], -1, shape[-1])
    for step in range(2):
        d = digit(step)
        groups = [buf[:, m] for m in range(sizes[step])]
        got = [None] + [
            lax.ppermute(groups[m], axes, digit_pairs(nrow, ncol, on_row, step, m))
            for m in range(1, sizes[step])
        ]
        buf = pick(d, [groups[0]] + got[1:])
    for step in reversed(range(2)):
        d = digit(step)
        got = [buf] + [
            lax.ppermute(buf, axes, digit_pairs(nrow, ncol, on_row, step, m))
            for m in range(1, sizes[step])
        ]
        buf = jnp.stack(
            [pick(d, [got[dd ^ t] for dd in range(sizes[step])]) for t in range(sizes[step])], axis=1
        )
    return buf.reshape(shape)


def all_bcast(value, root):
    nrow = lax.axis_size("row")
    ncol = lax.axis_size("col")
    n = nrow * ncol
    relative = (lax.axis_index("row") * ncol + lax.axis_index("col")) ^ root
    for b in range(n.bit_length() - 1):
        got = lax.ppermute(value, ("row", "col"), [(d, d ^ (1 << b)) for d in range(n)])
        value = per_part((relative >> b) == 1, got, value)
    return value


def lower_local(column, inverse, rows_ok):
    lower = jnp.einsum("iab,bc->iac", column, inverse, preferred_element_type=jnp.float32)
    return jnp.where(rows_ok[:, None, None], lower, 0.0).astype(jnp.bfloat16)


def eliminate(matrix, lower, upper, pivot, rows_ok, cols_ok, local, front_cols):
    product = jnp.einsum("iab,jbc->ijac", lower, upper, preferred_element_type=jnp.float32)
    update = rows_ok[:, None] & cols_ok[None, :] & (local > 0)
    changed = (matrix.astype(jnp.float32) - product).astype(jnp.bfloat16)
    result = jnp.where(update[:, :, None, None], changed, matrix)
    place = rows_ok[:, None] & (front_cols == pivot)[None, :]
    return jnp.where(place[:, :, None, None], lower[:, None], result)


def update_kernel(
    codes, row_codes, front_ref, c1_ref, c2_ref, x_ref, p1_ref, p2_ref, u1_ref, u2_ref, out_ref
):
    for r in range(front_ref.shape[0]):
        i = pl.program_id(0) * front_ref.shape[0] + r
        row_code = row_codes[i]
        lower1 = jnp.dot(c1_ref[r], p1_ref[...], preferred_element_type=jnp.float32).astype(jnp.bfloat16)
        lower1 = jnp.where((row_code & 1) != 0, lower1, jnp.zeros_like(lower1))
        column = c2_ref[r]
        product = jnp.dot(lower1, x_ref[...], preferred_element_type=jnp.float32)
        changed = (column.astype(jnp.float32) - product).astype(jnp.bfloat16)
        column = jnp.where((row_code & 4) != 0, changed, column)
        lower2 = jnp.dot(column, p2_ref[...], preferred_element_type=jnp.float32).astype(jnp.bfloat16)
        lower2 = jnp.where((row_code & 2) != 0, lower2, jnp.zeros_like(lower2))
        for j in range(front_ref.shape[1]):
            code = codes[i, j]
            block = front_ref[r, j]
            block = jnp.where((code & 1) != 0, block, jnp.zeros_like(block))
            product = jnp.dot(lower1, u1_ref[j], preferred_element_type=jnp.float32)
            changed = (block.astype(jnp.float32) - product).astype(jnp.bfloat16)
            block = jnp.where((code & 2) != 0, changed, block)
            block = jnp.where((code & 4) != 0, lower1, block)
            product = jnp.dot(lower2, u2_ref[j], preferred_element_type=jnp.float32)
            changed = (block.astype(jnp.float32) - product).astype(jnp.bfloat16)
            block = jnp.where((code & 8) != 0, changed, block)
            block = jnp.where((code & 16) != 0, lower2, block)
            out_ref[r, j] = block


ROWS_PER_STEP = 4


def both_updates(front, codes, row_codes, column1, column2, cross, inverse, upper1, upper2):
    rows, cols, bs, _ = front.shape
    step = ROWS_PER_STEP
    row_block = pl.BlockSpec((step, cols, bs, bs), lambda i, c, r: (i, 0, 0, 0))
    lower_block = pl.BlockSpec((step, bs, bs), lambda i, c, r: (i, 0, 0))
    one_block = pl.BlockSpec((bs, bs), lambda i, c, r: (0, 0))
    upper_block = pl.BlockSpec((cols, bs, bs), lambda i, c, r: (0, 0, 0))
    return pl.pallas_call(
        update_kernel,
        grid_spec=pltpu.PrefetchScalarGridSpec(
            num_scalar_prefetch=2,
            grid=(rows // step,),
            in_specs=[
                row_block, lower_block, lower_block, one_block, one_block, one_block,
                upper_block, upper_block,
            ],
            out_specs=row_block,
        ),
        out_shape=jax.ShapeDtypeStruct(front.shape, front.dtype),
        compiler_params=pltpu.CompilerParams(dimension_semantics=("arbitrary",)),
    )(codes, row_codes, front, column1, column2, cross, inverse[0], inverse[1], upper1, upper2)


def masked(blocks, keep):
    shape = keep.shape + (1,) * (blocks.ndim - keep.ndim)
    return jnp.where(keep.reshape(shape) > 0, blocks, jnp.zeros_like(blocks))


def body(front, pattern, pivots, pivot_inv):
    rows_dev = front.shape[0]
    cols_dev = front.shape[1]
    nrow = lax.axis_size("row")
    ncol = lax.axis_size("col")
    row_index = lax.axis_index("row")
    col_index = lax.axis_index("col")
    grid = pattern.reshape(rows_dev, nrow, cols_dev, ncol)
    local = lax.dynamic_index_in_dim(grid, row_index, 1, keepdims=False)
    local = lax.dynamic_index_in_dim(local, col_index, 2, keepdims=False)
    front_rows = jnp.arange(rows_dev, dtype=jnp.int32) * nrow + row_index
    front_cols = jnp.arange(cols_dev, dtype=jnp.int32) * ncol + col_index
    first = pivots[0]
    second = pivots[1]
    rows_first = front_rows != first
    cols_first = front_cols != first
    rows_second = rows_first & (front_rows != second)
    cols_second = cols_first & (front_cols != second)

    a1, b1 = first // nrow, first // ncol
    a2, b2 = second // nrow, second // ncol
    r1, c1 = first % nrow, first % ncol
    r2, c2 = second % nrow, second % ncol

    def local_row(a):
        return masked(
            lax.dynamic_index_in_dim(front, a, 0, keepdims=False),
            lax.dynamic_index_in_dim(local, a, 0, keepdims=False),
        )

    def local_col(b):
        return masked(
            lax.dynamic_index_in_dim(front, b, 1, keepdims=False),
            lax.dynamic_index_in_dim(local, b, 1, keepdims=False),
        )

    cols_sent = xor_bcast(jnp.stack([local_col(b1), local_col(b2)]), jnp.stack([c1, c2]), False)
    rows_sent = xor_bcast(jnp.stack([local_row(a1), local_row(a2)]), jnp.stack([r1, r2]), True)
    second_col = cols_sent[1]
    upper_first, second_row = rows_sent[0], rows_sent[1]

    cross = all_bcast(
        jnp.stack([masked(front[a1, b2], local[a1, b2]), masked(front[a2, b1], local[a2, b1])]),
        jnp.stack([r1 * ncol + c2, r2 * ncol + c1]),
    )
    first_at_second, second_at_first = cross[0], cross[1]

    second_ok = (second != first)[None]
    lower_first_at_second = lower_local(second_at_first[None], pivot_inv[0], second_ok)
    row_after = eliminate(
        second_row[None],
        lower_first_at_second,
        upper_first,
        first,
        second_ok,
        cols_first,
        pattern[second][front_cols][None],
        front_cols,
    )
    upper_second = row_after[0]
    row_codes = (
        rows_first.astype(jnp.int32)
        + 2 * rows_second.astype(jnp.int32)
        + 4 * (rows_first & second_ok[0] & (pattern[front_rows, second] > 0)).astype(jnp.int32)
    )

    keep = local > 0
    update_first = rows_first[:, None] & cols_first[None, :] & keep
    place_first = rows_first[:, None] & (front_cols == first)[None, :]
    update_second = rows_second[:, None] & cols_second[None, :] & keep
    place_second = rows_second[:, None] & (front_cols == second)[None, :]
    codes = (
        keep.astype(jnp.int32)
        + 2 * update_first.astype(jnp.int32)
        + 4 * place_first.astype(jnp.int32)
        + 8 * update_second.astype(jnp.int32)
        + 16 * place_second.astype(jnp.int32)
    )
    return both_updates(
        front, codes, row_codes, cols_sent[0], second_col, first_at_second, pivot_inv,
        upper_first, upper_second,
    )


def solution(mesh):
    placed = (P("row", "col", None, None), P(), P(), P())
    return jax.shard_map(
        body, mesh=mesh, in_specs=placed, out_specs=P("row", "col", None, None), check_vma=False
    )
```
